32 devices in a mesh: groups: 2 (over y), wide: 4 (over z), narrow: 2 (over x), slab: 2 (over core).
Axes of the slice: x: 2, y: 2, z: 4, core: 2. Of those that a mesh axis runs over, the one named last changes fastest.
Arguments:
- obs_latitude: float32 [256, 128], P(('groups', 'wide')), parts along dimension 0, may hold values from -0.1 to 0.1
- obs_offset: float32 [256, 128], P(('groups', 'wide')), parts along dimension 0, may hold values from -16 to 17
- innovation: float32 [256, 128], P(('groups', 'wide')), parts along dimension 0, may hold values from -6 to 6
- obs_error: float32 [256, 128], P(('groups', 'wide')), parts along dimension 0, may hold values from 0.5 to 1.5
- region_sizes: int32 [256], P(('groups', 'wide')), parts along dimension 0, may hold values from 1 to 128, as said below
- tile_columns: int32 [256, 4], P(('groups', 'wide')), parts along dimension 0, may hold values from 0 to 127, as said below
- slab_list: int32 [256, 4], P(('groups', 'wide')), parts along dimension 0, may hold values from 0 to 31, as said below
- slab_order: int32 [64], P('groups'), parts along dimension 0, may hold values from 0 to 31, each once
- grid_latitude: float32 [32, 512], replicated, may hold values from -0.1 to 0.1
- grid_offset: float32 [32, 512], replicated, may hold values from -4 to 5
- ridge_weight: float32 [16], P('narrow'), may hold values from 0.1 to 2
- huber_cut: float32 [16], P('narrow'), may hold values from 0.5 to 2.5
- step_size: float32 [16], P('narrow'), may hold values from 0.3 to 0.6
Outputs:
- obs_weights: float32 [256, 16, 128], P(('groups', 'wide'), 'narrow'), parts along dimension 0
- grid_increment: float32 [64, 16, 512], P(('groups', 'wide', 'slab'), 'narrow'), parts along dimension 0
The draws below stay inside these ranges and needn't reach their ends.
There are 2 independent parts, one for each index of `groups`. The reference program is written for one: setup_inputs(seed, part) draws one part's arguments, and reference() takes and returns one part's arrays. A program takes and returns all parts, laid end to end along the dimension named above; an argument that names none is the same for every part. Nothing has to cross between parts.
Inputs may be any that keep to these rules, and one draw needn't show every extreme that they name: `tile_columns`: the 4 entries of a row a are distinct regions (a + o) mod 128 with offsets o from -16 to 16. `slab_list`: the 4 entries of a row a are distinct slabs (a * 32 // 128 + o) mod 32 with offsets o from -4 to 4. `slab_order`: a permutation of the slabs. `region_sizes`: in each analysis case the largest is exactly 128.
All inputs are finite; a program needn't handle non-finite values.
Results may differ from the reference program's by a relative error of at most 0.0001.
Values sent between devices are 32-bit elements; how exact they have to be, the bound alone decides.
No kernel may reach another device: no remote copies, remote signals or barrier semaphores. Data moves between devices by JAX's collectives and lax.ppermute only.
A program may use at most 64 MiB of HBM per device.

```python
import math
import jax
import jax.numpy as jnp
from jax import lax

K = 16
CAP = 128
TPR = 4
GPR = 4
SR = 4
GPTS = 512
ITERS = 2
REGIONS = 128
HALF = 16
SLABS = 32


TURN_ANGLE = 6.283185307179586


def draw_innovation(key, part):
    keys = jax.random.split(key, 5)
    angle = TURN_ANGLE * jnp.arange(REGIONS, dtype=jnp.float32) / REGIONS
    waves = jax.random.randint(keys[0], (2,), 1, 4).astype(jnp.float32)
    phases = jax.random.uniform(keys[1], (2,), minval=0.0, maxval=TURN_ANGLE)
    spread = jax.random.uniform(keys[2], (2,), minval=0.0, maxval=1.0)
    first_amp = 1.0 + 0.5 * spread[0]
    second_amp = 0.4 + 0.4 * spread[1]
    region_part = jnp.clip(0.5 * jax.random.normal(keys[3], (REGIONS,)), -1.5, 1.5)
    rough = jnp.clip(0.7 * jax.random.normal(keys[4], (REGIONS, CAP)), -2.2, 2.2)
    smooth = first_amp * jnp.sin(waves[0] * angle + phases[0]) + second_amp * jnp.sin(waves[1] * angle + phases[1])
    return (smooth[:, None] + region_part[:, None] + rough).astype(jnp.float32)


def draw_region_sizes(key, part):
    keys = jax.random.split(key, 3)
    first_pick = jax.random.randint(keys[0], (REGIONS,), 1, CAP + 1)
    second_pick = jax.random.randint(keys[1], (REGIONS,), 1, CAP + 1)
    sizes = jnp.maximum(first_pick, second_pick)
    fullest = jax.random.randint(keys[2], (), 0, REGIONS)
    sizes = jnp.where(jnp.arange(REGIONS, dtype=jnp.int32) == fullest, CAP, sizes)
    return sizes.astype(jnp.int32)


def draw_tile_columns(key, part):
    split_keys = jax.random.split(key, REGIONS)

    def pick_offsets(row_key):
        return jax.random.permutation(row_key, 2 * HALF + 1)[:TPR]
    offsets = jax.vmap(pick_offsets)(split_keys) - HALF
    row_ids = jnp.arange(REGIONS, dtype=jnp.int32)[:, None]
    return ((row_ids + offsets) % REGIONS).astype(jnp.int32)


def draw_slab_list(key, part):
    split_keys = jax.random.split(key, REGIONS)

    def pick_offsets(row_key):
        return jax.random.permutation(row_key, 2 * SR + 1)[:GPR]
    offsets = jax.vmap(pick_offsets)(split_keys) - SR
    home_slab = jnp.arange(REGIONS, dtype=jnp.int32)[:, None] * SLABS // REGIONS
    return ((home_slab + offsets) % SLABS).astype(jnp.int32)


def block_scale(rng, extent, cuts, low, largest):
    factor_of, own = 1.0, jax.random.fold_in(rng, 6)
    for axis_at, blocks in cuts:
        draws = jnp.exp(jax.random.uniform(jax.random.fold_in(own, axis_at), (blocks,), jnp.float32, low / len(cuts), largest / len(cuts)))
        factor_of = factor_of * jnp.repeat(draws, extent[axis_at] // blocks).reshape([-1 if axis == axis_at else 1 for axis in range(len(extent))])
    return factor_of


def setup_inputs(seed: int = 0, part: int = 0) -> dict:
    streams_of = jax.random.split(jax.random.key(seed), 14)
    own_keys = jax.random.split(jax.random.fold_in(streams_of[13], part), 14)
    obs_latitude = jnp.clip(jax.random.uniform(own_keys[0], (REGIONS, CAP), jnp.float32, -0.1, 0.1) * block_scale(own_keys[0], (REGIONS, CAP), ((0, 4),), -0.4, 0.0), -0.1, 0.1)
    obs_offset = jnp.clip(-16.0 + 33.0 * jax.random.uniform(own_keys[1], (REGIONS, CAP), jnp.float32) ** block_scale(own_keys[1], (REGIONS, CAP), ((0, 4),), -0.2, 0.2), -16.0, 17.0)
    innovation = draw_innovation(jax.random.fold_in(jax.random.fold_in(streams_of[13], part), 71), part)
    obs_error = jnp.clip(jnp.exp(math.log(1.5) - 1.0986123 * jax.random.uniform(own_keys[3], (REGIONS, CAP), jnp.float32) ** block_scale(own_keys[3], (REGIONS, CAP), ((0, 4),), -0.2, 0.2)), 0.5, 1.5)
    region_sizes = draw_region_sizes(jax.random.fold_in(jax.random.fold_in(streams_of[13], part), 71), part)
    tile_columns = draw_tile_columns(jax.random.fold_in(jax.random.fold_in(streams_of[13], part), 71), part)
    slab_list = draw_slab_list(jax.random.fold_in(jax.random.fold_in(streams_of[13], part), 71), part)
    slab_order = jax.random.permutation(own_keys[7], SLABS).astype(jnp.int32)
    grid_latitude = jnp.clip(jax.random.uniform(streams_of[8], (SLABS, GPTS), jnp.float32, -0.1, 0.1), -0.1, 0.1)
    grid_offset = jnp.clip(jax.random.uniform(streams_of[9], (SLABS, GPTS), jnp.float32, -4.0, 5.0), -4.0, 5.0)
    ridge_weight = jnp.clip(jnp.exp(math.log(2.0) - 2.9957323 * jax.random.uniform(streams_of[10], (K,), jnp.float32) ** block_scale(streams_of[10], (K,), ((0, 2),), -0.2, 0.2)), 0.1, 2.0)
    huber_cut = jnp.clip(jnp.exp(math.log(2.5) - 1.609438 * jax.random.uniform(streams_of[11], (K,), jnp.float32) ** block_scale(streams_of[11], (K,), ((0, 2),), -0.2, 0.2)), 0.5, 2.5)
    step_size = jnp.clip(0.3 + 0.3 * jax.random.uniform(streams_of[12], (K,), jnp.float32) ** block_scale(streams_of[12], (K,), ((0, 2),), -0.2, 0.2), 0.3, 0.6)
    return dict(obs_latitude=obs_latitude, obs_offset=obs_offset, innovation=innovation, obs_error=obs_error, region_sizes=region_sizes, tile_columns=tile_columns, slab_list=slab_list, slab_order=slab_order, grid_latitude=grid_latitude, grid_offset=grid_offset, ridge_weight=ridge_weight, huber_cut=huber_cut, step_size=step_size)


DECAY_RATE = 1.0 / 0.15
FULL_TURN = 6.283185307179586
HIGHEST = lax.Precision.HIGHEST

def unit_vectors(latitude, longitude):
    return jnp.stack([jnp.cos(latitude) * jnp.cos(longitude), jnp.cos(latitude) * jnp.sin(longitude), jnp.sin(latitude)], axis=-2)

def correlate(first, second):
    spread = first[..., :, :, None] - second[..., :, None, :]
    return jnp.exp(-jnp.sqrt(lax.optimization_barrier(jnp.sum(spread * spread, axis=-3))) * DECAY_RATE)

def reference(obs_latitude, obs_offset, innovation, obs_error, region_sizes, tile_columns, slab_list, slab_order, grid_latitude, grid_offset, ridge_weight, huber_cut, step_size):
    row_ids = jnp.arange(REGIONS, dtype=jnp.int32)
    obs_lon = FULL_TURN * (row_ids[:, None].astype(jnp.float32) + obs_offset) / REGIONS
    obs_sites = unit_vectors(obs_latitude, obs_lon)
    live_mask = (jnp.arange(CAP, dtype=jnp.int32)[None, :] < region_sizes[:, None]).astype(jnp.float32)
    diagonal = (obs_error * obs_error)[:, None, :] + ridge_weight[None, :, None]
    observed = (innovation * live_mask)[:, None, :]
    threshold = huber_cut[None, :, None] * obs_error[:, None, :]
    obs_weights = observed / diagonal
    tile_scale = 2.0 / (CAP * TPR)
    for sweep_index in range(ITERS):
        current = obs_weights

        def region_product(packed):
            own_sites, columns = packed
            return jnp.einsum('tpq,tkq->kp', correlate(own_sites, obs_sites[columns]), current[columns], precision=HIGHEST)
        covariance = lax.map(region_product, (obs_sites, tile_columns))
        applied = covariance * tile_scale + diagonal * obs_weights
        residual = (observed - applied) * live_mask[:, None, :]
        factor = threshold / jnp.maximum(jnp.abs(residual), threshold)
        obs_weights = obs_weights + step_size[None, :, None] * factor * residual / diagonal
    grid_lon = FULL_TURN * (jnp.arange(SLABS, dtype=jnp.float32)[:, None] + grid_offset) / SLABS
    grid_sites = unit_vectors(grid_latitude, grid_lon)

    def add_region(total, packed):
        own_sites, region_weights, listed_slabs = packed
        cross = correlate(grid_sites[listed_slabs], own_sites)
        contrib = jnp.einsum('ngq,kq->nkg', cross, region_weights, precision=HIGHEST) / CAP
        return (total.at[listed_slabs].add(contrib), None)
    start_total = jnp.zeros((SLABS, K, GPTS), jnp.float32)
    by_slab, unused = lax.scan(add_region, start_total, (obs_sites, obs_weights, slab_list))
    return (obs_weights, by_slab[slab_order])
```

```python
import jax
import jax.numpy as jnp
from jax import lax
from jax.experimental import pallas as pl
from jax.experimental.pallas import tpu as pltpu
from jax.sharding import PartitionSpec as P

ITERS = 2
SLAB_REACH = 4

DECAY_RATE = 1.0 / 0.15
FULL_TURN = 6.283185307179586
HIGHEST = lax.Precision.HIGHEST
ROWS = 8


def with_halo(cells, axis, width):
    count = lax.axis_size(axis)
    head = lax.slice_in_dim(cells, 0, width, axis=0)
    tail = lax.slice_in_dim(cells, cells.shape[0] - width, cells.shape[0], axis=0)
    return jnp.concatenate(
        [
            lax.ppermute(tail, axis, [(i, (i + 1) % count) for i in range(count)]),
            cells,
            lax.ppermute(head, axis, [((i + 1) % count, i) for i in range(count)]),
        ],
        axis=0,
    )


def gather_slots(x, axis):
    count = lax.axis_size(axis)
    parts = [x]
    for s in range(1, count):
        parts.append(lax.ppermute(x, axis, [(i, (i + s) % count) for i in range(count)]))
    return jnp.concatenate(parts, axis=0)


def unit_rows(latitude, longitude):
    c = jnp.cos(latitude)
    zero = jnp.zeros_like(latitude)
    return jnp.stack(
        [c * jnp.cos(longitude), c * jnp.sin(longitude), jnp.sin(latitude)] + [zero] * (ROWS - 3),
        axis=-2,
    )


def corr_block(col_t, row):
    dx = col_t[:, 0:1] - row[0:1, :]
    dy = col_t[:, 1:2] - row[1:2, :]
    dz = col_t[:, 2:3] - row[2:3, :]
    d2 = dx * dx + dy * dy + dz * dz
    return jnp.exp(jnp.sqrt(d2) * (-DECAY_RATE))


def contract_lanes(w, c):
    return lax.dot_general(
        w, c, (((1,), (1,)), ((), ())), precision=HIGHEST, preferred_element_type=jnp.float32
    )


def cov_kernel(cols_ref, own_ref, halo_ref, w_ref, out_ref):
    reg_dev = own_ref.shape[0]
    tiles = cols_ref.shape[0] // reg_dev

    def region(a, carry):
        own_t = own_ref[a].T
        acc = jnp.zeros(out_ref.shape[1:], jnp.float32)
        for t in range(tiles):
            b = cols_ref[a * tiles + t]
            c = corr_block(own_t, halo_ref[b])
            acc = acc + contract_lanes(w_ref[b], c)
        out_ref[a] = acc
        return carry

    lax.fori_loop(0, reg_dev, region, 0)


def covariance(cols, own_sites, halo_sites, halo_w):
    reg_dev, solves, cap = own_sites.shape[0], halo_w.shape[1], own_sites.shape[2]
    vmem = pl.BlockSpec(memory_space=pltpu.VMEM)
    return pl.pallas_call(
        cov_kernel,
        out_shape=jax.ShapeDtypeStruct((reg_dev, solves, cap), jnp.float32),
        in_specs=[pl.BlockSpec(memory_space=pltpu.SMEM), vmem, vmem, vmem],
        out_specs=vmem,
    )(cols, own_sites, halo_sites, halo_w)


def make_grid_kernel(slab_count, per_slab, reg_dev, n_wide, cap):
    def grid_kernel(me_ref, own_slabs_ref, list_ref, sites_ref, w_ref, gsites_ref, out_ref):
        n_own = out_ref.shape[0]
        regions = sites_ref.shape[0]
        gpr = list_ref.shape[0] // regions
        me = me_ref[0]
        window = (2 * SLAB_REACH + 1) * per_slab
        for j in range(n_own):
            slab = own_slabs_ref[j]
            g_t = gsites_ref[j].T
            start = (slab - SLAB_REACH) * per_slab + regions

            def candidate(r, acc):
                a = lax.rem(start + r, regions)
                owner = a // reg_dev
                slot = lax.rem(me - owner + n_wide, n_wide) * reg_dev + lax.rem(a, reg_dev)
                listed = list_ref[slot * gpr] == slab
                for e in range(1, gpr):
                    listed = jnp.logical_or(listed, list_ref[slot * gpr + e] == slab)

                def add(acc):
                    c = corr_block(g_t, sites_ref[slot])
                    return acc + contract_lanes(w_ref[slot], c)

                return lax.cond(listed, add, lambda acc: acc, acc)

            acc = lax.fori_loop(0, window, candidate, jnp.zeros(out_ref.shape[1:], jnp.float32))
            out_ref[j] = acc / cap

    return grid_kernel


def grid_stage(me, own_slabs, list_slots, site_slots, w_slots, gsites, slab_count, reg_dev, n_wide):
    regions, solves, cap = w_slots.shape
    n_own, _, gpts = gsites.shape
    kernel = make_grid_kernel(slab_count, regions // slab_count, reg_dev, n_wide, cap)
    vmem = pl.BlockSpec(memory_space=pltpu.VMEM)
    smem = pl.BlockSpec(memory_space=pltpu.SMEM)
    return pl.pallas_call(
        kernel,
        out_shape=jax.ShapeDtypeStruct((n_own, solves, gpts), jnp.float32),
        in_specs=[smem, smem, smem, vmem, vmem, vmem],
        out_specs=vmem,
    )(me, own_slabs, list_slots, site_slots, w_slots, gsites)


def body(
    obs_latitude,
    obs_offset,
    innovation,
    obs_error,
    region_sizes,
    tile_columns,
    slab_list,
    slab_order,
    grid_latitude,
    grid_offset,
    ridge_weight,
    huber_cut,
    step_size,
):
    reg_dev, capacity = innovation.shape
    n_wide = lax.axis_size("wide")
    regions = reg_dev * n_wide
    margin = reg_dev // 2
    me = lax.axis_index("wide")
    first_row = me * reg_dev
    row_ids = first_row + jnp.arange(reg_dev, dtype=jnp.int32)
    obs_lon = FULL_TURN * (row_ids[:, None].astype(jnp.float32) + obs_offset) / regions
    obs_sites = unit_rows(obs_latitude, obs_lon)
    site_slots = gather_slots(obs_sites, "wide")
    list_slots = gather_slots(slab_list, "wide").reshape(-1)
    live_mask = (jnp.arange(capacity, dtype=jnp.int32)[None, :] < region_sizes[:, None]).astype(
        jnp.float32
    )
    diagonal = (obs_error * obs_error)[:, None, :] + ridge_weight[None, :, None]
    observed = (innovation * live_mask)[:, None, :]
    threshold = huber_cut[None, :, None] * obs_error[:, None, :]
    obs_weights = observed / diagonal
    sites_wide = with_halo(obs_sites, "wide", margin)
    local_cols = ((tile_columns - first_row + margin) % regions).reshape(-1)
    tile_scale = 2.0 / (capacity * tile_columns.shape[1])
    for sweep_index in range(ITERS):
        weights_wide = with_halo(obs_weights, "wide", margin)
        partial_value = covariance(local_cols, obs_sites, sites_wide, weights_wide)
        applied = partial_value * tile_scale + diagonal * obs_weights
        residual = (observed - applied) * live_mask[:, None, :]
        factor = threshold / jnp.maximum(jnp.abs(residual), threshold)
        obs_weights = obs_weights + step_size[None, :, None] * factor * residual / diagonal
    w_slots = gather_slots(obs_weights, "wide")

    slab_count = slab_order.shape[0]
    n_slab = lax.axis_size("slab")
    n_own = slab_count // (n_wide * n_slab)
    pos0 = (me * n_slab + lax.axis_index("slab")) * n_own
    own_slabs = lax.dynamic_slice_in_dim(slab_order, pos0, n_own, 0)
    g_lat = grid_latitude[own_slabs]
    g_lon = FULL_TURN * (own_slabs[:, None].astype(jnp.float32) + grid_offset[own_slabs]) / slab_count
    gsites = unit_rows(g_lat, g_lon)
    grid_increment = grid_stage(
        me.astype(jnp.int32).reshape(1),
        own_slabs,
        list_slots,
        site_slots,
        w_slots,
        gsites,
        slab_count,
        reg_dev,
        n_wide,
    )
    return (obs_weights, grid_increment)


def solution(mesh):
    in_specs = (
        P(("groups", "wide"), None),
        P(("groups", "wide"), None),
        P(("groups", "wide"), None),
        P(("groups", "wide"), None),
        P(("groups", "wide")),
        P(("groups", "wide"), None),
        P(("groups", "wide"), None),
        P("groups"),
        P(),
        P(),
        P("narrow"),
        P("narrow"),
        P("narrow"),
    )
    out_specs = (
        P(("groups", "wide"), "narrow", None),
        P(("groups", "wide", "slab"), "narrow", None),
    )
    return jax.shard_map(body, mesh=mesh, in_specs=in_specs, out_specs=out_specs, check_vma=False)
```

```python
import jax
import jax.numpy as jnp
from jax import lax
from jax.experimental import pallas as pl
from jax.experimental.pallas import tpu as pltpu
from jax.sharding import PartitionSpec as P

ITERS = 2
SLAB_REACH = 4

DECAY_RATE = 1.0 / 0.15
FULL_TURN = 6.283185307179586
HIGHEST = lax.Precision.HIGHEST
ROWS = 8
GROUP = 4


def with_halo(cells, axis, width):
    count = lax.axis_size(axis)
    head = lax.slice_in_dim(cells, 0, width, axis=0)
    tail = lax.slice_in_dim(cells, cells.shape[0] - width, cells.shape[0], axis=0)
    return jnp.concatenate(
        [
            lax.ppermute(tail, axis, [(i, (i + 1) % count) for i in range(count)]),
            cells,
            lax.ppermute(head, axis, [((i + 1) % count, i) for i in range(count)]),
        ],
        axis=0,
    )


def gather_slots(x, axis):
    count = lax.axis_size(axis)
    parts = [x]
    for s in range(1, count):
        parts.append(lax.ppermute(x, axis, [(i, (i + s) % count) for i in range(count)]))
    return jnp.concatenate(parts, axis=0)


def unit_rows(latitude, longitude):
    c = jnp.cos(latitude)
    zero = jnp.zeros_like(latitude)
    return jnp.stack(
        [c * jnp.cos(longitude), c * jnp.sin(longitude), jnp.sin(latitude)] + [zero] * (ROWS - 3),
        axis=-2,
    )


def corr_block(col_t, row):
    dx = col_t[:, 0:1] - row[0:1, :]
    dy = col_t[:, 1:2] - row[1:2, :]
    dz = col_t[:, 2:3] - row[2:3, :]
    d2 = dx * dx + dy * dy + dz * dz
    return jnp.exp(jnp.sqrt(d2) * (-DECAY_RATE))


def contract_lanes(w, c):
    return lax.dot_general(
        w, c, (((1,), (1,)), ((), ())), precision=HIGHEST, preferred_element_type=jnp.float32
    )


def make_update_kernel(margin, tile_scale):
    def update_kernel(cols_ref, own_ref, halo_ref, w_ref, obs_ref, diag_ref, thr_ref, live_ref, step_ref, out_ref):
        reg_dev = own_ref.shape[0]
        tiles = cols_ref.shape[0] // reg_dev

        def region(a, carry):
            own_t = own_ref[a].T
            blocks, weights = [], []
            for t in range(tiles):
                b = cols_ref[a * tiles + t]
                blocks.append(corr_block(own_t, halo_ref[b]))
                weights.append(w_ref[b])
            cov = contract_lanes(
                jnp.concatenate(weights, axis=1), jnp.concatenate(blocks, axis=1)
            )
            current = w_ref[a + margin]
            diag = diag_ref[a]
            thr = thr_ref[a]
            applied = cov * tile_scale + diag * current
            residual = (obs_ref[a] - applied) * live_ref[a]
            factor = thr / jnp.maximum(jnp.abs(residual), thr)
            out_ref[a] = current + step_ref[...] * factor * residual / diag
            return carry

        lax.fori_loop(0, reg_dev, region, 0)

    return update_kernel


def update(cols, own_sites, halo_sites, halo_w, observed, diagonal, threshold, live, step, margin, tile_scale):
    vmem = pl.BlockSpec(memory_space=pltpu.VMEM)
    return pl.pallas_call(
        make_update_kernel(margin, tile_scale),
        out_shape=jax.ShapeDtypeStruct(diagonal.shape, jnp.float32),
        in_specs=[pl.BlockSpec(memory_space=pltpu.SMEM)] + [vmem] * 8,
        out_specs=vmem,
    )(cols, own_sites, halo_sites, halo_w, observed, diagonal, threshold, live, step)


def make_grid_kernel(per_slab, reg_dev, n_wide, cap, regions):
    window = (2 * SLAB_REACH + 1) * per_slab

    def grid_kernel(me_ref, own_slabs_ref, list_ref, sites_ref, w_ref, gsites_ref, out_ref, sel_ref):
        n_own = out_ref.shape[0]
        gpr = list_ref.shape[0] // regions
        me = me_ref[0]
        for j in range(n_own):
            slab = own_slabs_ref[j]
            g_t = gsites_ref[j].T
            start = (slab - SLAB_REACH) * per_slab + regions

            def scan(r, count):
                a = lax.rem(start + r, regions)
                owner = a // reg_dev
                slot = lax.rem(me - owner + n_wide, n_wide) * reg_dev + lax.rem(a, reg_dev)
                listed = list_ref[slot * gpr] == slab
                for e in range(1, gpr):
                    listed = jnp.logical_or(listed, list_ref[slot * gpr + e] == slab)
                sel_ref[count] = slot
                return count + listed.astype(jnp.int32)

            count = lax.fori_loop(0, window, scan, jnp.int32(0))
            for e in range(GROUP):
                sel_ref[count + e] = regions

            def group(gi, acc):
                blocks, weights = [], []
                for e in range(GROUP):
                    slot = sel_ref[gi * GROUP + e]
                    blocks.append(corr_block(g_t, sites_ref[slot]))
                    weights.append(w_ref[slot])
                return acc + contract_lanes(
                    jnp.concatenate(weights, axis=1), jnp.concatenate(blocks, axis=1)
                )

            n_groups = (count + GROUP - 1) // GROUP
            acc = lax.fori_loop(0, n_groups, group, jnp.zeros(out_ref.shape[1:], jnp.float32))
            out_ref[j] = acc / cap

    return grid_kernel, window


def grid_stage(me, own_slabs, list_slots, site_slots, w_slots, gsites, reg_dev, n_wide, regions, slab_count):
    solves, cap = w_slots.shape[1:]
    n_own, _, gpts = gsites.shape
    kernel, window = make_grid_kernel(regions // slab_count, reg_dev, n_wide, cap, regions)
    vmem = pl.BlockSpec(memory_space=pltpu.VMEM)
    smem = pl.BlockSpec(memory_space=pltpu.SMEM)
    return pl.pallas_call(
        kernel,
        out_shape=jax.ShapeDtypeStruct((n_own, solves, gpts), jnp.float32),
        in_specs=[smem, smem, smem, vmem, vmem, vmem],
        out_specs=vmem,
        scratch_shapes=[pltpu.SMEM((window + GROUP,), jnp.int32)],
    )(me, own_slabs, list_slots, site_slots, w_slots, gsites)


def body(
    obs_latitude,
    obs_offset,
    innovation,
    obs_error,
    region_sizes,
    tile_columns,
    slab_list,
    slab_order,
    grid_latitude,
    grid_offset,
    ridge_weight,
    huber_cut,
    step_size,
):
    reg_dev, capacity = innovation.shape
    n_wide = lax.axis_size("wide")
    regions = reg_dev * n_wide
    margin = reg_dev // 2
    me = lax.axis_index("wide")
    first_row = me * reg_dev
    row_ids = first_row + jnp.arange(reg_dev, dtype=jnp.int32)
    obs_lon = FULL_TURN * (row_ids[:, None].astype(jnp.float32) + obs_offset) / regions
    obs_sites = unit_rows(obs_latitude, obs_lon)
    gpr = slab_list.shape[1]
    packed = jnp.concatenate(
        [
            obs_sites[:, :4, :],
            jnp.pad(slab_list.astype(jnp.float32), ((0, 0), (0, capacity - gpr)))[:, None, :],
        ],
        axis=1,
    )
    slots = gather_slots(packed, "wide")
    spare = jnp.zeros((ROWS, ROWS, capacity), jnp.float32)
    site_slots = jnp.concatenate(
        [jnp.pad(slots[:, :3, :], ((0, 0), (0, ROWS - 3), (0, 0))), spare], axis=0
    )
    list_slots = slots[:, 4, :gpr].astype(jnp.int32).reshape(-1)
    left = site_slots[2 * reg_dev - margin : 2 * reg_dev]
    right = site_slots[(n_wide - 1) * reg_dev : (n_wide - 1) * reg_dev + margin]
    sites_wide = jnp.concatenate([left, obs_sites, right], axis=0)
    live_mask = (jnp.arange(capacity, dtype=jnp.int32)[None, :] < region_sizes[:, None]).astype(
        jnp.float32
    )
    solves = ridge_weight.shape[0]
    diagonal = (obs_error * obs_error)[:, None, :] + ridge_weight[None, :, None]
    observed = (innovation * live_mask)[:, None, :]
    threshold = huber_cut[None, :, None] * obs_error[:, None, :]
    obs_weights = observed / diagonal
    live = live_mask[:, None, :]
    step = jnp.broadcast_to(step_size[:, None], (solves, capacity))
    local_cols = ((tile_columns - first_row + margin) % regions).reshape(-1)
    tile_scale = 2.0 / (capacity * tile_columns.shape[1])
    for sweep_index in range(ITERS):
        weights_wide = with_halo(obs_weights, "wide", margin)
        obs_weights = update(
            local_cols, obs_sites, sites_wide, weights_wide, observed, diagonal, threshold,
            live, step, margin, tile_scale,
        )
    w_slots = jnp.concatenate(
        [gather_slots(obs_weights, "wide"), jnp.zeros((ROWS, solves, capacity), jnp.float32)], axis=0
    )

    slab_count = slab_order.shape[0]
    n_slab = lax.axis_size("slab")
    n_own = slab_count // (n_wide * n_slab)
    pos0 = (me * n_slab + lax.axis_index("slab")) * n_own
    own_slabs = lax.dynamic_slice_in_dim(slab_order, pos0, n_own, 0)
    g_lat = grid_latitude[own_slabs]
    g_lon = FULL_TURN * (own_slabs[:, None].astype(jnp.float32) + grid_offset[own_slabs]) / slab_count
    gsites = unit_rows(g_lat, g_lon)
    grid_increment = grid_stage(
        me.astype(jnp.int32).reshape(1),
        own_slabs,
        list_slots,
        site_slots,
        w_slots,
        gsites,
        reg_dev,
        n_wide,
        regions,
        slab_count,
    )
    return (obs_weights, grid_increment)


def solution(mesh):
    in_specs = (
        P(("groups", "wide"), None),
        P(("groups", "wide"), None),
        P(("groups", "wide"), None),
        P(("groups", "wide"), None),
        P(("groups", "wide")),
        P(("groups", "wide"), None),
        P(("groups", "wide"), None),
        P("groups"),
        P(),
        P(),
        P("narrow"),
        P("narrow"),
        P("narrow"),
    )
    out_specs = (
        P(("groups", "wide"), "narrow", None),
        P(("groups", "wide", "slab"), "narrow", None),
    )
    return jax.shard_map(body, mesh=mesh, in_specs=in_specs, out_specs=out_specs, check_vma=False)
```

```python
import jax
import jax.numpy as jnp
from jax import lax
from jax.experimental import pallas as pl
from jax.experimental.pallas import tpu as pltpu
from jax.sharding import PartitionSpec as P

ITERS = 2
SLAB_REACH = 4

DECAY_RATE = 1.0 / 0.15
FULL_TURN = 6.283185307179586
HIGHEST = lax.Precision.HIGHEST
ROWS = 8
GROUP = 4


def with_halo(cells, axis, width):
    count = lax.axis_size(axis)
    head = lax.slice_in_dim(cells, 0, width, axis=0)
    tail = lax.slice_in_dim(cells, cells.shape[0] - width, cells.shape[0], axis=0)
    return jnp.concatenate(
        [
            lax.ppermute(tail, axis, [(i, (i + 1) % count) for i in range(count)]),
            cells,
            lax.ppermute(head, axis, [((i + 1) % count, i) for i in range(count)]),
        ],
        axis=0,
    )


def gather_slots(x, axis):
    count = lax.axis_size(axis)
    parts = [x]
    for s in range(1, count):
        parts.append(lax.ppermute(x, axis, [(i, (i + s) % count) for i in range(count)]))
    return jnp.concatenate(parts, axis=0)


def unit_rows(latitude, longitude):
    c = jnp.cos(latitude)
    zero = jnp.zeros_like(latitude)
    return jnp.stack(
        [c * jnp.cos(longitude), c * jnp.sin(longitude), jnp.sin(latitude)] + [zero] * (ROWS - 3),
        axis=-2,
    )


def corr_block(col_t, row):
    dx = col_t[:, 0:1] - row[0:1, :]
    dy = col_t[:, 1:2] - row[1:2, :]
    dz = col_t[:, 2:3] - row[2:3, :]
    d2 = dx * dx + dy * dy + dz * dz
    return jnp.exp(jnp.sqrt(d2) * (-DECAY_RATE))


def contract_lanes(w, c):
    return lax.dot_general(
        w, c, (((1,), (1,)), ((), ())), precision=HIGHEST, preferred_element_type=jnp.float32
    )


def make_update_kernel(margin, tile_scale):
    def update_kernel(
        cols_ref, own_ref, halo_ref, w_ref, obs_ref, diag_ref, thr_ref, live_ref, step_ref,
        out_ref, buf0, buf1,
    ):
        reg_dev, _, cap = own_ref.shape
        tiles = cols_ref.shape[0] // reg_dev

        def fill(a, buf):
            own_t = own_ref[a].T
            for t in range(tiles):
                b = cols_ref[a * tiles + t]
                buf[:, t * cap : (t + 1) * cap] = corr_block(own_t, halo_ref[b])

        def use(a, buf):
            weights = jnp.concatenate(
                [w_ref[cols_ref[a * tiles + t]] for t in range(tiles)], axis=1
            )
            cov = contract_lanes(weights, buf[...])
            current = w_ref[a + margin]
            diag = diag_ref[a]
            thr = thr_ref[a]
            applied = cov * tile_scale + diag * current
            residual = (obs_ref[a] - applied) * live_ref[a]
            factor = thr / jnp.maximum(jnp.abs(residual), thr)
            out_ref[a] = current + step_ref[...] * factor * residual / diag

        fill(0, buf0)

        def pair(i, carry):
            a = 2 * i
            use(a, buf0)
            fill(a + 1, buf1)
            use(a + 1, buf1)
            fill(jnp.minimum(a + 2, reg_dev - 1), buf0)
            return carry

        lax.fori_loop(0, reg_dev // 2, pair, 0)

    return update_kernel


def update(cols, own_sites, halo_sites, halo_w, observed, diagonal, threshold, live, step, margin, tile_scale):
    reg_dev, _, cap = own_sites.shape
    assert reg_dev % 2 == 0
    tiles = cols.shape[0] // reg_dev
    vmem = pl.BlockSpec(memory_space=pltpu.VMEM)
    return pl.pallas_call(
        make_update_kernel(margin, tile_scale),
        out_shape=jax.ShapeDtypeStruct(diagonal.shape, jnp.float32),
        in_specs=[pl.BlockSpec(memory_space=pltpu.SMEM)] + [vmem] * 8,
        out_specs=vmem,
        scratch_shapes=[pltpu.VMEM((cap, tiles * cap), jnp.float32)] * 2,
    )(cols, own_sites, halo_sites, halo_w, observed, diagonal, threshold, live, step)


def make_grid_kernel(per_slab, reg_dev, n_wide, cap, regions):
    window = (2 * SLAB_REACH + 1) * per_slab

    def grid_kernel(
        me_ref, own_slabs_ref, list_ref, sites_ref, w_ref, gsites_ref, out_ref,
        sel_ref, slab_ref, buf0, buf1,
    ):
        n_own = out_ref.shape[0]
        gpr = list_ref.shape[0] // regions
        me = me_ref[0]
        total = jnp.int32(0)
        for j in range(n_own):
            slab = own_slabs_ref[j]
            start = (slab - SLAB_REACH) * per_slab + regions

            def scan(r, count):
                a = lax.rem(start + r, regions)
                owner = a // reg_dev
                slot = lax.rem(me - owner + n_wide, n_wide) * reg_dev + lax.rem(a, reg_dev)
                listed = list_ref[slot * gpr] == slab
                for e in range(1, gpr):
                    listed = jnp.logical_or(listed, list_ref[slot * gpr + e] == slab)
                sel_ref[count] = slot
                return count + listed.astype(jnp.int32)

            first_group = total // GROUP
            total = lax.fori_loop(0, window, scan, total)
            for e in range(GROUP):
                sel_ref[total + e] = regions
            total = (total + GROUP - 1) // GROUP * GROUP

            def mark(g, carry):
                slab_ref[g] = j
                return carry

            lax.fori_loop(first_group, total // GROUP, mark, 0)
        n_groups = total // GROUP
        for e in range(GROUP):
            sel_ref[total + e] = regions
        slab_ref[n_groups] = 0
        n_pairs = (n_groups + 1) // 2
        last = 2 * n_pairs - 1
        out_ref[...] = jnp.zeros(out_ref.shape, jnp.float32)

        def fill(g, buf):
            g_t = gsites_ref[slab_ref[g]].T
            for e in range(GROUP):
                slot = sel_ref[g * GROUP + e]
                buf[:, e * cap : (e + 1) * cap] = corr_block(g_t, sites_ref[slot])

        def use(g, buf):
            j = slab_ref[g]
            weights = jnp.concatenate(
                [w_ref[sel_ref[g * GROUP + e]] for e in range(GROUP)], axis=1
            )
            out_ref[j] = out_ref[j] + contract_lanes(weights, buf[...])

        fill(0, buf0)

        def pair(i, carry):
            g = 2 * i
            use(g, buf0)
            fill(g + 1, buf1)
            use(g + 1, buf1)
            fill(jnp.minimum(g + 2, last), buf0)
            return carry

        lax.fori_loop(0, n_pairs, pair, 0)
        out_ref[...] = out_ref[...] / cap

    return grid_kernel, window


def grid_stage(me, own_slabs, list_slots, site_slots, w_slots, gsites, reg_dev, n_wide, regions, slab_count):
    solves, cap = w_slots.shape[1:]
    n_own, _, gpts = gsites.shape
    kernel, window = make_grid_kernel(regions // slab_count, reg_dev, n_wide, cap, regions)
    vmem = pl.BlockSpec(memory_space=pltpu.VMEM)
    smem = pl.BlockSpec(memory_space=pltpu.SMEM)
    sel_len = n_own * (window + GROUP) + 2 * GROUP
    return pl.pallas_call(
        kernel,
        out_shape=jax.ShapeDtypeStruct((n_own, solves, gpts), jnp.float32),
        in_specs=[smem, smem, smem, vmem, vmem, vmem],
        out_specs=vmem,
        scratch_shapes=[
            pltpu.SMEM((sel_len,), jnp.int32),
            pltpu.SMEM((sel_len // GROUP + 2,), jnp.int32),
            pltpu.VMEM((gpts, GROUP * cap), jnp.float32),
            pltpu.VMEM((gpts, GROUP * cap), jnp.float32),
        ],
    )(me, own_slabs, list_slots, site_slots, w_slots, gsites)


def body(
    obs_latitude,
    obs_offset,
    innovation,
    obs_error,
    region_sizes,
    tile_columns,
    slab_list,
    slab_order,
    grid_latitude,
    grid_offset,
    ridge_weight,
    huber_cut,
    step_size,
):
    reg_dev, capacity = innovation.shape
    n_wide = lax.axis_size("wide")
    regions = reg_dev * n_wide
    margin = reg_dev // 2
    me = lax.axis_index("wide")
    first_row = me * reg_dev
    row_ids = first_row + jnp.arange(reg_dev, dtype=jnp.int32)
    obs_lon = FULL_TURN * (row_ids[:, None].astype(jnp.float32) + obs_offset) / regions
    obs_sites = unit_rows(obs_latitude, obs_lon)
    gpr = slab_list.shape[1]
    packed = jnp.concatenate(
        [
            obs_sites[:, :4, :],
            jnp.pad(slab_list.astype(jnp.float32), ((0, 0), (0, capacity - gpr)))[:, None, :],
        ],
        axis=1,
    )
    slots = gather_slots(packed, "wide")
    spare = jnp.zeros((ROWS, ROWS, capacity), jnp.float32)
    site_slots = jnp.concatenate(
        [jnp.pad(slots[:, :3, :], ((0, 0), (0, ROWS - 3), (0, 0))), spare], axis=0
    )
    list_slots = slots[:, 4, :gpr].astype(jnp.int32).reshape(-1)
    left = site_slots[2 * reg_dev - margin : 2 * reg_dev]
    right = site_slots[(n_wide - 1) * reg_dev : (n_wide - 1) * reg_dev + margin]
    sites_wide = jnp.concatenate([left, obs_sites, right], axis=0)
    live_mask = (jnp.arange(capacity, dtype=jnp.int32)[None, :] < region_sizes[:, None]).astype(
        jnp.float32
    )
    solves = ridge_weight.shape[0]
    diagonal = (obs_error * obs_error)[:, None, :] + ridge_weight[None, :, None]
    observed = (innovation * live_mask)[:, None, :]
    threshold = huber_cut[None, :, None] * obs_error[:, None, :]
    obs_weights = observed / diagonal
    live = live_mask[:, None, :]
    step = jnp.broadcast_to(step_size[:, None], (solves, capacity))
    local_cols = ((tile_columns - first_row + margin) % regions).reshape(-1)
    tile_scale = 2.0 / (capacity * tile_columns.shape[1])
    for sweep_index in range(ITERS):
        weights_wide = with_halo(obs_weights, "wide", margin)
        obs_weights = update(
            local_cols, obs_sites, sites_wide, weights_wide, observed, diagonal, threshold,
            live, step, margin, tile_scale,
        )
    w_slots = jnp.concatenate(
        [gather_slots(obs_weights, "wide"), jnp.zeros((ROWS, solves, capacity), jnp.float32)], axis=0
    )

    slab_count = slab_order.shape[0]
    n_slab = lax.axis_size("slab")
    n_own = slab_count // (n_wide * n_slab)
    pos0 = (me * n_slab + lax.axis_index("slab")) * n_own
    own_slabs = lax.dynamic_slice_in_dim(slab_order, pos0, n_own, 0)
    g_lat = grid_latitude[own_slabs]
    g_lon = FULL_TURN * (own_slabs[:, None].astype(jnp.float32) + grid_offset[own_slabs]) / slab_count
    gsites = unit_rows(g_lat, g_lon)
    grid_increment = grid_stage(
        me.astype(jnp.int32).reshape(1),
        own_slabs,
        list_slots,
        site_slots,
        w_slots,
        gsites,
        reg_dev,
        n_wide,
        regions,
        slab_count,
    )
    return (obs_weights, grid_increment)


def solution(mesh):
    in_specs = (
        P(("groups", "wide"), None),
        P(("groups", "wide"), None),
        P(("groups", "wide"), None),
        P(("groups", "wide"), None),
        P(("groups", "wide")),
        P(("groups", "wide"), None),
        P(("groups", "wide"), None),
        P("groups"),
        P(),
        P(),
        P("narrow"),
        P("narrow"),
        P("narrow"),
    )
    out_specs = (
        P(("groups", "wide"), "narrow", None),
        P(("groups", "wide", "slab"), "narrow", None),
    )
    return jax.shard_map(body, mesh=mesh, in_specs=in_specs, out_specs=out_specs, check_vma=False)
```

```python
import jax
import jax.numpy as jnp
from jax import lax
from jax.experimental import pallas as pl
from jax.experimental.pallas import tpu as pltpu
from jax.sharding import PartitionSpec as P

ITERS = 2
SLAB_REACH = 4

DECAY_RATE = 1.0 / 0.15
FULL_TURN = 6.283185307179586
HIGHEST = lax.Precision.HIGHEST
ROWS = 8
GROUP = 4


def with_halo(cells, axis, width):
    count = lax.axis_size(axis)
    head = lax.slice_in_dim(cells, 0, width, axis=0)
    tail = lax.slice_in_dim(cells, cells.shape[0] - width, cells.shape[0], axis=0)
    return jnp.concatenate(
        [
            lax.ppermute(tail, axis, [(i, (i + 1) % count) for i in range(count)]),
            cells,
            lax.ppermute(head, axis, [((i + 1) % count, i) for i in range(count)]),
        ],
        axis=0,
    )


def gather_slots(x, axis):
    count = lax.axis_size(axis)
    parts = [x]
    for s in range(1, count):
        parts.append(lax.ppermute(x, axis, [(i, (i + s) % count) for i in range(count)]))
    return jnp.concatenate(parts, axis=0)


def unit_rows(latitude, longitude):
    c = jnp.cos(latitude)
    zero = jnp.zeros_like(latitude)
    return jnp.stack(
        [c * jnp.cos(longitude), c * jnp.sin(longitude), jnp.sin(latitude)] + [zero] * (ROWS - 3),
        axis=-2,
    )


def corr_block(col_t, row):
    dx = col_t[:, 0:1] - row[0:1, :]
    dy = col_t[:, 1:2] - row[1:2, :]
    dz = col_t[:, 2:3] - row[2:3, :]
    d2 = dx * dx + dy * dy + dz * dz
    return jnp.exp(jnp.sqrt(d2) * (-DECAY_RATE))


def contract_lanes(w, c):
    return lax.dot_general(
        w, c, (((1,), (1,)), ((), ())), precision=HIGHEST, preferred_element_type=jnp.float32
    )


def make_update_kernel(margin, tile_scale):
    def update_kernel(
        base_ref, cols_ref, own_ref, halo_ref, w_ref, obs_ref, diag_ref, thr_ref, live_ref,
        step_ref, out_ref, buf0, buf1,
    ):
        reg_dev, _, cap = own_ref.shape
        count = out_ref.shape[0]
        tiles = cols_ref.shape[0] // reg_dev
        base = base_ref[0]

        def fill(i, buf):
            a = i + base
            own_t = own_ref[a].T
            for t in range(tiles):
                b = cols_ref[a * tiles + t]
                buf[:, t * cap : (t + 1) * cap] = corr_block(own_t, halo_ref[b])

        def use(i, buf):
            a = i + base
            weights = jnp.concatenate(
                [w_ref[cols_ref[a * tiles + t]] for t in range(tiles)], axis=1
            )
            cov = contract_lanes(weights, buf[...])
            current = w_ref[a + margin]
            diag = diag_ref[a]
            thr = thr_ref[a]
            applied = cov * tile_scale + diag * current
            residual = (obs_ref[a] - applied) * live_ref[a]
            factor = thr / jnp.maximum(jnp.abs(residual), thr)
            out_ref[i] = current + step_ref[...] * factor * residual / diag

        fill(0, buf0)

        def pair(i, carry):
            a = 2 * i
            use(a, buf0)
            fill(a + 1, buf1)
            use(a + 1, buf1)
            fill(jnp.minimum(a + 2, count - 1), buf0)
            return carry

        lax.fori_loop(0, count // 2, pair, 0)

    return update_kernel


def update(base, count, cols, own_sites, halo_sites, halo_w, observed, diagonal, threshold, live, step, margin, tile_scale):
    reg_dev, _, cap = own_sites.shape
    assert count % 2 == 0
    tiles = cols.shape[0] // reg_dev
    vmem = pl.BlockSpec(memory_space=pltpu.VMEM)
    smem = pl.BlockSpec(memory_space=pltpu.SMEM)
    return pl.pallas_call(
        make_update_kernel(margin, tile_scale),
        out_shape=jax.ShapeDtypeStruct((count,) + diagonal.shape[1:], jnp.float32),
        in_specs=[smem, smem] + [vmem] * 8,
        out_specs=vmem,
        scratch_shapes=[pltpu.VMEM((cap, tiles * cap), jnp.float32)] * 2,
    )(base, cols, own_sites, halo_sites, halo_w, observed, diagonal, threshold, live, step)


def make_grid_kernel(per_slab, reg_dev, n_wide, cap, regions):
    window = (2 * SLAB_REACH + 1) * per_slab

    def grid_kernel(
        me_ref, own_slabs_ref, list_ref, sites_ref, w_ref, gsites_ref, out_ref,
        sel_ref, slab_ref, buf0, buf1,
    ):
        n_own = out_ref.shape[0]
        gpr = list_ref.shape[0] // regions
        me = me_ref[0]
        total = jnp.int32(0)
        for j in range(n_own):
            slab = own_slabs_ref[j]
            start = (slab - SLAB_REACH) * per_slab + regions

            def scan(r, count):
                a = lax.rem(start + r, regions)
                owner = a // reg_dev
                slot = lax.rem(me - owner + n_wide, n_wide) * reg_dev + lax.rem(a, reg_dev)
                listed = list_ref[slot * gpr] == slab
                for e in range(1, gpr):
                    listed = jnp.logical_or(listed, list_ref[slot * gpr + e] == slab)
                sel_ref[count] = slot
                return count + listed.astype(jnp.int32)

            first_group = total // GROUP
            total = lax.fori_loop(0, window, scan, total)
            for e in range(GROUP):
                sel_ref[total + e] = regions
            total = (total + GROUP - 1) // GROUP * GROUP

            def mark(g, carry):
                slab_ref[g] = j
                return carry

            lax.fori_loop(first_group, total // GROUP, mark, 0)
        n_groups = total // GROUP
        for e in range(GROUP):
            sel_ref[total + e] = regions
        slab_ref[n_groups] = 0
        n_pairs = (n_groups + 1) // 2
        last = 2 * n_pairs - 1
        out_ref[...] = jnp.zeros(out_ref.shape, jnp.float32)

        def fill(g, buf):
            g_t = gsites_ref[slab_ref[g]].T
            for e in range(GROUP):
                slot = sel_ref[g * GROUP + e]
                buf[:, e * cap : (e + 1) * cap] = corr_block(g_t, sites_ref[slot])

        def use(g, buf):
            j = slab_ref[g]
            weights = jnp.concatenate(
                [w_ref[sel_ref[g * GROUP + e]] for e in range(GROUP)], axis=1
            )
            out_ref[j] = out_ref[j] + contract_lanes(weights, buf[...])

        fill(0, buf0)

        def pair(i, carry):
            g = 2 * i
            use(g, buf0)
            fill(g + 1, buf1)
            use(g + 1, buf1)
            fill(jnp.minimum(g + 2, last), buf0)
            return carry

        lax.fori_loop(0, n_pairs, pair, 0)
        out_ref[...] = out_ref[...] / cap

    return grid_kernel, window


def grid_stage(me, own_slabs, list_slots, site_slots, w_slots, gsites, reg_dev, n_wide, regions, slab_count):
    solves, cap = w_slots.shape[1:]
    n_own, _, gpts = gsites.shape
    kernel, window = make_grid_kernel(regions // slab_count, reg_dev, n_wide, cap, regions)
    vmem = pl.BlockSpec(memory_space=pltpu.VMEM)
    smem = pl.BlockSpec(memory_space=pltpu.SMEM)
    sel_len = n_own * (window + GROUP) + 2 * GROUP
    return pl.pallas_call(
        kernel,
        out_shape=jax.ShapeDtypeStruct((n_own, solves, gpts), jnp.float32),
        in_specs=[smem, smem, smem, vmem, vmem, vmem],
        out_specs=vmem,
        scratch_shapes=[
            pltpu.SMEM((sel_len,), jnp.int32),
            pltpu.SMEM((sel_len // GROUP + 2,), jnp.int32),
            pltpu.VMEM((gpts, GROUP * cap), jnp.float32),
            pltpu.VMEM((gpts, GROUP * cap), jnp.float32),
        ],
    )(me, own_slabs, list_slots, site_slots, w_slots, gsites)


def body(
    obs_latitude,
    obs_offset,
    innovation,
    obs_error,
    region_sizes,
    tile_columns,
    slab_list,
    slab_order,
    grid_latitude,
    grid_offset,
    ridge_weight,
    huber_cut,
    step_size,
):
    reg_dev, capacity = innovation.shape
    n_wide = lax.axis_size("wide")
    regions = reg_dev * n_wide
    margin = reg_dev // 2
    me = lax.axis_index("wide")
    first_row = me * reg_dev
    row_ids = first_row + jnp.arange(reg_dev, dtype=jnp.int32)
    obs_lon = FULL_TURN * (row_ids[:, None].astype(jnp.float32) + obs_offset) / regions
    obs_sites = unit_rows(obs_latitude, obs_lon)
    gpr = slab_list.shape[1]
    packed = jnp.concatenate(
        [
            obs_sites[:, :4, :],
            jnp.pad(slab_list.astype(jnp.float32), ((0, 0), (0, capacity - gpr)))[:, None, :],
        ],
        axis=1,
    )
    slots = gather_slots(packed, "wide")
    spare = jnp.zeros((ROWS, ROWS, capacity), jnp.float32)
    site_slots = jnp.concatenate(
        [jnp.pad(slots[:, :3, :], ((0, 0), (0, ROWS - 3), (0, 0))), spare], axis=0
    )
    list_slots = slots[:, 4, :gpr].astype(jnp.int32).reshape(-1)
    left = site_slots[2 * reg_dev - margin : 2 * reg_dev]
    right = site_slots[(n_wide - 1) * reg_dev : (n_wide - 1) * reg_dev + margin]
    sites_wide = jnp.concatenate([left, obs_sites, right], axis=0)
    live_mask = (jnp.arange(capacity, dtype=jnp.int32)[None, :] < region_sizes[:, None]).astype(
        jnp.float32
    )
    solves = ridge_weight.shape[0]
    diagonal = (obs_error * obs_error)[:, None, :] + ridge_weight[None, :, None]
    observed = (innovation * live_mask)[:, None, :]
    threshold = huber_cut[None, :, None] * obs_error[:, None, :]
    obs_weights = observed / diagonal
    live = live_mask[:, None, :]
    step = jnp.broadcast_to(step_size[:, None], (solves, capacity))
    local_cols = ((tile_columns - first_row + margin) % regions).reshape(-1)
    tile_scale = 2.0 / (capacity * tile_columns.shape[1])
    n_slab = lax.axis_size("slab")
    assert n_slab == 2 and margin * n_slab == reg_dev
    sidx = lax.axis_index("slab")
    sub = reg_dev // n_slab
    base = (sidx * sub).astype(jnp.int32).reshape(1)
    blocks = n_wide * n_slab
    pairs = ("wide", "slab")
    other_pairs = [(b, b ^ 1) for b in range(blocks)]
    q1_pairs = [(b, (b - 2) % blocks) if b % 2 == 0 else (b, (b + 2) % blocks) for b in range(blocks)]
    q2_pairs = [(b, (b - 1) % blocks) if b % 2 == 0 else (b, (b + 1) % blocks) for b in range(blocks)]
    first = sidx == 0

    def own_rows(mine):
        other = lax.ppermute(mine, pairs, other_pairs)
        return jnp.where(first, jnp.concatenate([mine, other]), jnp.concatenate([other, mine]))

    weights_wide = with_halo(obs_weights, "wide", margin)
    for sweep_index in range(ITERS):
        mine = update(
            base, sub, local_cols, obs_sites, sites_wide, weights_wide, observed, diagonal,
            threshold, live, step, margin, tile_scale,
        )
        obs_weights = own_rows(mine)
        if sweep_index + 1 < ITERS:
            q1 = lax.ppermute(mine, pairs, q1_pairs)
            q2 = lax.ppermute(mine, pairs, q2_pairs)
            left = jnp.where(first, q2, q1)
            right = jnp.where(first, q1, q2)
            weights_wide = jnp.concatenate([left, obs_weights, right])
    w_slots = jnp.concatenate(
        [gather_slots(obs_weights, "wide"), jnp.zeros((ROWS, solves, capacity), jnp.float32)], axis=0
    )

    slab_count = slab_order.shape[0]
    n_own = slab_count // (n_wide * n_slab)
    pos0 = (me * n_slab + lax.axis_index("slab")) * n_own
    own_slabs = lax.dynamic_slice_in_dim(slab_order, pos0, n_own, 0)
    g_lat = grid_latitude[own_slabs]
    g_lon = FULL_TURN * (own_slabs[:, None].astype(jnp.float32) + grid_offset[own_slabs]) / slab_count
    gsites = unit_rows(g_lat, g_lon)
    grid_increment = grid_stage(
        me.astype(jnp.int32).reshape(1),
        own_slabs,
        list_slots,
        site_slots,
        w_slots,
        gsites,
        reg_dev,
        n_wide,
        regions,
        slab_count,
    )
    return (obs_weights, grid_increment)


def solution(mesh):
    in_specs = (
        P(("groups", "wide"), None),
        P(("groups", "wide"), None),
        P(("groups", "wide"), None),
        P(("groups", "wide"), None),
        P(("groups", "wide")),
        P(("groups", "wide"), None),
        P(("groups", "wide"), None),
        P("groups"),
        P(),
        P(),
        P("narrow"),
        P("narrow"),
        P("narrow"),
    )
    out_specs = (
        P(("groups", "wide"), "narrow", None),
        P(("groups", "wide", "slab"), "narrow", None),
    )
    return jax.shard_map(body, mesh=mesh, in_specs=in_specs, out_specs=out_specs, check_vma=False)
```

```python
import jax
import jax.numpy as jnp
from jax import lax
from jax.experimental import pallas as pl
from jax.experimental.pallas import tpu as pltpu
from jax.sharding import PartitionSpec as P

ITERS = 2
SLAB_REACH = 4

DECAY_RATE = 1.0 / 0.15
FULL_TURN = 6.283185307179586
HIGHEST = lax.Precision.HIGHEST
ROWS = 8
GROUP = 4


def with_halo(cells, axis, width):
    count = lax.axis_size(axis)
    head = lax.slice_in_dim(cells, 0, width, axis=0)
    tail = lax.slice_in_dim(cells, cells.shape[0] - width, cells.shape[0], axis=0)
    return jnp.concatenate(
        [
            lax.ppermute(tail, axis, [(i, (i + 1) % count) for i in range(count)]),
            cells,
            lax.ppermute(head, axis, [((i + 1) % count, i) for i in range(count)]),
        ],
        axis=0,
    )


def gather_slots(x, axis):
    count = lax.axis_size(axis)
    parts = [x]
    for s in range(1, count):
        parts.append(lax.ppermute(x, axis, [(i, (i + s) % count) for i in range(count)]))
    return jnp.concatenate(parts, axis=0)


def unit_rows(latitude, longitude):
    c = jnp.cos(latitude)
    zero = jnp.zeros_like(latitude)
    return jnp.stack(
        [c * jnp.cos(longitude), c * jnp.sin(longitude), jnp.sin(latitude)] + [zero] * (ROWS - 3),
        axis=-2,
    )


def corr_block(col_t, row):
    dx = col_t[:, 0:1] - row[0:1, :]
    dy = col_t[:, 1:2] - row[1:2, :]
    dz = col_t[:, 2:3] - row[2:3, :]
    d2 = dx * dx + dy * dy + dz * dz
    return jnp.exp(jnp.sqrt(d2) * (-DECAY_RATE))


def contract_lanes(w, c):
    return lax.dot_general(
        w, c, (((1,), (1,)), ((), ())), precision=HIGHEST, preferred_element_type=jnp.float32
    )


def make_update_kernel(margin, tile_scale):
    def update_kernel(
        base_ref, cols_ref, own_ref, halo_ref, w_ref, obs_ref, diag_ref, thr_ref, live_ref,
        step_ref, out_ref, buf0, buf1,
    ):
        reg_dev, _, cap = own_ref.shape
        count = out_ref.shape[0]
        tiles = cols_ref.shape[0] // reg_dev
        base = base_ref[0]

        def fill(i, buf):
            a = i + base
            own_t = own_ref[a].T
            for t in range(tiles):
                b = cols_ref[a * tiles + t]
                buf[:, t * cap : (t + 1) * cap] = corr_block(own_t, halo_ref[b])

        def use(i, buf):
            a = i + base
            weights = jnp.concatenate(
                [w_ref[cols_ref[a * tiles + t]] for t in range(tiles)], axis=1
            )
            cov = contract_lanes(weights, buf[...])
            current = w_ref[a + margin]
            diag = diag_ref[a]
            thr = thr_ref[a]
            applied = cov * tile_scale + diag * current
            residual = (obs_ref[a] - applied) * live_ref[a]
            factor = thr / jnp.maximum(jnp.abs(residual), thr)
            out_ref[i] = current + step_ref[...] * factor * residual / diag

        fill(0, buf0)

        def pair(i, carry):
            a = 2 * i
            use(a, buf0)
            fill(a + 1, buf1)
            use(a + 1, buf1)
            fill(jnp.minimum(a + 2, count - 1), buf0)
            return carry

        lax.fori_loop(0, count // 2, pair, 0)

    return update_kernel


def update(base, count, cols, own_sites, halo_sites, halo_w, observed, diagonal, threshold, live, step, margin, tile_scale):
    reg_dev, _, cap = own_sites.shape
    assert count % 2 == 0
    tiles = cols.shape[0] // reg_dev
    vmem = pl.BlockSpec(memory_space=pltpu.VMEM)
    smem = pl.BlockSpec(memory_space=pltpu.SMEM)
    return pl.pallas_call(
        make_update_kernel(margin, tile_scale),
        out_shape=jax.ShapeDtypeStruct((count,) + diagonal.shape[1:], jnp.float32),
        in_specs=[smem, smem] + [vmem] * 8,
        out_specs=vmem,
        scratch_shapes=[pltpu.VMEM((cap, tiles * cap), jnp.float32)] * 2,
    )(base, cols, own_sites, halo_sites, halo_w, observed, diagonal, threshold, live, step)


def make_grid_kernel(per_slab, reg_dev, n_wide, cap, regions, n_split):
    window = (2 * SLAB_REACH + 1) * per_slab

    def grid_kernel(
        me_ref, own_slabs_ref, list_ref, sites_ref, w_ref, gsites_ref, out_ref,
        sel_ref, slab_ref, buf0, buf1,
    ):
        n_own = out_ref.shape[0]
        gpr = list_ref.shape[0] // regions
        me = me_ref[0]
        part = me_ref[1]
        total = jnp.int32(0)
        for j in range(n_own):
            slab = own_slabs_ref[j]
            start = (slab - SLAB_REACH) * per_slab + regions

            def scan(r, count):
                a = lax.rem(start + r, regions)
                owner = a // reg_dev
                slot = lax.rem(me - owner + n_wide, n_wide) * reg_dev + lax.rem(a, reg_dev)
                listed = list_ref[slot * gpr] == slab
                for e in range(1, gpr):
                    listed = jnp.logical_or(listed, list_ref[slot * gpr + e] == slab)
                sel_ref[count] = slot
                return count + listed.astype(jnp.int32)

            first_group = total // GROUP
            total = lax.fori_loop(0, window, scan, total)
            for e in range(GROUP):
                sel_ref[total + e] = regions
            total = (total + GROUP - 1) // GROUP * GROUP

            def mark(g, carry):
                slab_ref[g] = j
                return carry

            lax.fori_loop(first_group, total // GROUP, mark, 0)
        n_groups = total // GROUP
        step = 2 * n_split
        padded = jnp.maximum((n_groups + step - 1) // step * step, step)

        def pad(g, carry):
            for e in range(GROUP):
                sel_ref[g * GROUP + e] = regions
            slab_ref[g] = 0
            return carry

        lax.fori_loop(n_groups, padded, pad, 0)
        n_local = padded // n_split
        out_ref[...] = jnp.zeros(out_ref.shape, jnp.float32)

        def fill(l, buf):
            g = l * n_split + part
            g_t = gsites_ref[slab_ref[g]].T
            for e in range(GROUP):
                slot = sel_ref[g * GROUP + e]
                buf[:, e * cap : (e + 1) * cap] = corr_block(g_t, sites_ref[slot])

        def use(l, buf):
            g = l * n_split + part
            j = slab_ref[g]
            weights = jnp.concatenate(
                [w_ref[sel_ref[g * GROUP + e]] for e in range(GROUP)], axis=1
            )
            out_ref[j] = out_ref[j] + contract_lanes(weights, buf[...])

        fill(0, buf0)

        def pair(i, carry):
            l = 2 * i
            use(l, buf0)
            fill(l + 1, buf1)
            use(l + 1, buf1)
            fill(jnp.minimum(l + 2, n_local - 1), buf0)
            return carry

        lax.fori_loop(0, n_local // 2, pair, 0)
        out_ref[...] = out_ref[...] / cap

    return grid_kernel, window


def grid_stage(me, own_slabs, list_slots, site_slots, w_slots, gsites, reg_dev, n_wide, regions, slab_count, n_split):
    solves, cap = w_slots.shape[1:]
    n_own, _, gpts = gsites.shape
    kernel, window = make_grid_kernel(regions // slab_count, reg_dev, n_wide, cap, regions, n_split)
    vmem = pl.BlockSpec(memory_space=pltpu.VMEM)
    smem = pl.BlockSpec(memory_space=pltpu.SMEM)
    max_groups = n_own * (window // GROUP + 1) + 4 * n_split
    return pl.pallas_call(
        kernel,
        out_shape=jax.ShapeDtypeStruct((n_own, solves, gpts), jnp.float32),
        in_specs=[smem, smem, smem, vmem, vmem, vmem],
        out_specs=vmem,
        scratch_shapes=[
            pltpu.SMEM((max_groups * GROUP,), jnp.int32),
            pltpu.SMEM((max_groups,), jnp.int32),
            pltpu.VMEM((gpts, GROUP * cap), jnp.float32),
            pltpu.VMEM((gpts, GROUP * cap), jnp.float32),
        ],
    )(me, own_slabs, list_slots, site_slots, w_slots, gsites)


def to_canonical(slots, axis, count):
    me = lax.axis_index(axis)
    idx = lax.rem(me - jnp.arange(count, dtype=jnp.int32) + count, count)
    return jnp.take(slots, idx, axis=0)


def body(
    obs_latitude,
    obs_offset,
    innovation,
    obs_error,
    region_sizes,
    tile_columns,
    slab_list,
    slab_order,
    grid_latitude,
    grid_offset,
    ridge_weight,
    huber_cut,
    step_size,
):
    reg_dev, capacity = innovation.shape
    n_wide = lax.axis_size("wide")
    regions = reg_dev * n_wide
    margin = reg_dev // 2
    me = lax.axis_index("wide")
    first_row = me * reg_dev
    row_ids = first_row + jnp.arange(reg_dev, dtype=jnp.int32)
    obs_lon = FULL_TURN * (row_ids[:, None].astype(jnp.float32) + obs_offset) / regions
    obs_sites = unit_rows(obs_latitude, obs_lon)
    gpr = slab_list.shape[1]
    packed = jnp.concatenate(
        [
            obs_sites[:, :4, :],
            jnp.pad(slab_list.astype(jnp.float32), ((0, 0), (0, capacity - gpr)))[:, None, :],
        ],
        axis=1,
    )
    slots = gather_slots(packed, "wide")
    spare = jnp.zeros((ROWS, ROWS, capacity), jnp.float32)
    site_slots = jnp.concatenate(
        [jnp.pad(slots[:, :3, :], ((0, 0), (0, ROWS - 3), (0, 0))), spare], axis=0
    )
    list_slots = slots[:, 4, :gpr].astype(jnp.int32).reshape(-1)
    left = site_slots[2 * reg_dev - margin : 2 * reg_dev]
    right = site_slots[(n_wide - 1) * reg_dev : (n_wide - 1) * reg_dev + margin]
    sites_wide = jnp.concatenate([left, obs_sites, right], axis=0)
    live_mask = (jnp.arange(capacity, dtype=jnp.int32)[None, :] < region_sizes[:, None]).astype(
        jnp.float32
    )
    solves = ridge_weight.shape[0]
    diagonal = (obs_error * obs_error)[:, None, :] + ridge_weight[None, :, None]
    observed = (innovation * live_mask)[:, None, :]
    threshold = huber_cut[None, :, None] * obs_error[:, None, :]
    obs_weights = observed / diagonal
    live = live_mask[:, None, :]
    step = jnp.broadcast_to(step_size[:, None], (solves, capacity))
    local_cols = ((tile_columns - first_row + margin) % regions).reshape(-1)
    tile_scale = 2.0 / (capacity * tile_columns.shape[1])
    n_slab = lax.axis_size("slab")
    assert n_slab == 2 and margin * n_slab == reg_dev
    sidx = lax.axis_index("slab")
    sub = reg_dev // n_slab
    base = (sidx * sub).astype(jnp.int32).reshape(1)
    blocks = n_wide * n_slab
    pairs = ("wide", "slab")
    other_pairs = [(b, b ^ 1) for b in range(blocks)]
    q1_pairs = [(b, (b - 2) % blocks) if b % 2 == 0 else (b, (b + 2) % blocks) for b in range(blocks)]
    q2_pairs = [(b, (b - 1) % blocks) if b % 2 == 0 else (b, (b + 1) % blocks) for b in range(blocks)]
    first = sidx == 0

    def own_rows(mine):
        other = lax.ppermute(mine, pairs, other_pairs)
        return jnp.where(first, jnp.concatenate([mine, other]), jnp.concatenate([other, mine]))

    weights_wide = with_halo(obs_weights, "wide", margin)
    n_split = lax.axis_size("narrow")
    solves = obs_weights.shape[1]
    for sweep_index in range(ITERS):
        mine = update(
            base, sub, local_cols, obs_sites, sites_wide, weights_wide, observed, diagonal,
            threshold, live, step, margin, tile_scale,
        )
        if sweep_index + 1 < ITERS:
            obs_weights = own_rows(mine)
            q1 = lax.ppermute(mine, pairs, q1_pairs)
            q2 = lax.ppermute(mine, pairs, q2_pairs)
            left = jnp.where(first, q2, q1)
            right = jnp.where(first, q1, q2)
            weights_wide = jnp.concatenate([left, obs_weights, right])
    spread = ("narrow", "slab")
    pieces = to_canonical(gather_slots(mine[None], spread), spread, n_split * n_slab)
    pieces = pieces.reshape((n_split, n_slab * sub, solves, capacity))
    obs_weights = pieces[lax.axis_index("narrow")]
    all_solves = jnp.transpose(pieces, (1, 0, 2, 3)).reshape(
        (reg_dev, n_split * solves, capacity)
    )
    w_slots = jnp.concatenate(
        [gather_slots(all_solves, "wide"), jnp.zeros((ROWS, n_split * solves, capacity), jnp.float32)],
        axis=0,
    )

    slab_count = slab_order.shape[0]
    n_own = slab_count // (n_wide * n_slab)
    pos0 = (me * n_slab + lax.axis_index("slab")) * n_own
    own_slabs = lax.dynamic_slice_in_dim(slab_order, pos0, n_own, 0)
    g_lat = grid_latitude[own_slabs]
    g_lon = FULL_TURN * (own_slabs[:, None].astype(jnp.float32) + grid_offset[own_slabs]) / slab_count
    gsites = unit_rows(g_lat, g_lon)
    nidx = lax.axis_index("narrow")
    partial = grid_stage(
        jnp.stack([me, nidx]).astype(jnp.int32),
        own_slabs,
        list_slots,
        site_slots,
        w_slots,
        gsites,
        reg_dev,
        n_wide,
        regions,
        slab_count,
        n_split,
    )
    chunks = partial.reshape((n_own, n_split, solves, -1))
    grid_increment = lax.dynamic_index_in_dim(chunks, nidx, axis=1, keepdims=False)
    for s in range(1, n_split):
        send = lax.dynamic_index_in_dim(chunks, lax.rem(nidx + s, n_split), axis=1, keepdims=False)
        grid_increment = grid_increment + lax.ppermute(
            send, "narrow", [(i, (i + s) % n_split) for i in range(n_split)]
        )
    return (obs_weights, grid_increment)


def solution(mesh):
    in_specs = (
        P(("groups", "wide"), None),
        P(("groups", "wide"), None),
        P(("groups", "wide"), None),
        P(("groups", "wide"), None),
        P(("groups", "wide")),
        P(("groups", "wide"), None),
        P(("groups", "wide"), None),
        P("groups"),
        P(),
        P(),
        P("narrow"),
        P("narrow"),
        P("narrow"),
    )
    out_specs = (
        P(("groups", "wide"), "narrow", None),
        P(("groups", "wide", "slab"), "narrow", None),
    )
    return jax.shard_map(body, mesh=mesh, in_specs=in_specs, out_specs=out_specs, check_vma=False)
```

```python
import jax
import jax.numpy as jnp
from jax import lax
from jax.experimental import pallas as pl
from jax.experimental.pallas import tpu as pltpu
from jax.sharding import PartitionSpec as P

ITERS = 2
SLAB_REACH = 4

DECAY_RATE = 1.0 / 0.15
FULL_TURN = 6.283185307179586
HIGHEST = lax.Precision.HIGHEST
ROWS = 8
GROUP = 4


def with_halo(cells, axis, width):
    count = lax.axis_size(axis)
    head = lax.slice_in_dim(cells, 0, width, axis=0)
    tail = lax.slice_in_dim(cells, cells.shape[0] - width, cells.shape[0], axis=0)
    return jnp.concatenate(
        [
            lax.ppermute(tail, axis, [(i, (i + 1) % count) for i in range(count)]),
            cells,
            lax.ppermute(head, axis, [((i + 1) % count, i) for i in range(count)]),
        ],
        axis=0,
    )


def gather_slots(x, axis):
    count = lax.axis_size(axis)
    parts = [x]
    for s in range(1, count):
        parts.append(lax.ppermute(x, axis, [(i, (i + s) % count) for i in range(count)]))
    return jnp.concatenate(parts, axis=0)


def unit_rows(latitude, longitude):
    c = jnp.cos(latitude)
    zero = jnp.zeros_like(latitude)
    return jnp.stack(
        [c * jnp.cos(longitude), c * jnp.sin(longitude), jnp.sin(latitude)] + [zero] * (ROWS - 3),
        axis=-2,
    )


def corr_block(col_t, row):
    dx = col_t[:, 0:1] - row[0:1, :]
    dy = col_t[:, 1:2] - row[1:2, :]
    dz = col_t[:, 2:3] - row[2:3, :]
    d2 = dx * dx + dy * dy + dz * dz
    return jnp.exp(jnp.sqrt(d2) * (-DECAY_RATE))


def contract_lanes(w, c):
    return lax.dot_general(
        w, c, (((1,), (1,)), ((), ())), precision=HIGHEST, preferred_element_type=jnp.float32
    )


def make_update_kernel(margin, tile_scale):
    def update_kernel(
        base_ref, cols_ref, own_ref, halo_ref, w_ref, obs_ref, diag_ref, thr_ref, live_ref,
        step_ref, out_ref, buf0, buf1,
    ):
        reg_dev, _, cap = own_ref.shape
        count = out_ref.shape[0]
        tiles = cols_ref.shape[0] // reg_dev
        base = base_ref[0]

        def fill(i, buf):
            a = i + base
            own_t = own_ref[a].T
            for t in range(tiles):
                b = cols_ref[a * tiles + t]
                buf[:, t * cap : (t + 1) * cap] = corr_block(own_t, halo_ref[b])

        def use(i, buf):
            a = i + base
            weights = jnp.concatenate(
                [w_ref[cols_ref[a * tiles + t]] for t in range(tiles)], axis=1
            )
            cov = contract_lanes(weights, buf[...])
            current = w_ref[a + margin]
            diag = diag_ref[a]
            thr = thr_ref[a]
            applied = cov * tile_scale + diag * current
            residual = (obs_ref[a] - applied) * live_ref[a]
            factor = thr / jnp.maximum(jnp.abs(residual), thr)
            out_ref[i] = current + step_ref[...] * factor * residual / diag

        fill(0, buf0)

        def pair(i, carry):
            a = 2 * i
            use(a, buf0)
            fill(a + 1, buf1)
            use(a + 1, buf1)
            fill(jnp.minimum(a + 2, count - 1), buf0)
            return carry

        lax.fori_loop(0, count // 2, pair, 0)

    return update_kernel


def update(base, count, cols, own_sites, halo_sites, halo_w, observed, diagonal, threshold, live, step, margin, tile_scale):
    reg_dev, _, cap = own_sites.shape
    assert count % 2 == 0
    tiles = cols.shape[0] // reg_dev
    vmem = pl.BlockSpec(memory_space=pltpu.VMEM)
    smem = pl.BlockSpec(memory_space=pltpu.SMEM)
    return pl.pallas_call(
        make_update_kernel(margin, tile_scale),
        out_shape=jax.ShapeDtypeStruct((count,) + diagonal.shape[1:], jnp.float32),
        in_specs=[smem, smem] + [vmem] * 8,
        out_specs=vmem,
        scratch_shapes=[pltpu.VMEM((cap, tiles * cap), jnp.float32)] * 2,
    )(base, cols, own_sites, halo_sites, halo_w, observed, diagonal, threshold, live, step)


def make_grid_kernel(per_slab, reg_dev, n_wide, cap, regions):
    window = (2 * SLAB_REACH + 1) * per_slab

    def grid_kernel(
        me_ref, own_slabs_ref, list_ref, sites_ref, w_ref, gsites_ref, out_ref,
        sel_ref, slab_ref, buf0, buf1,
    ):
        n_own = out_ref.shape[0]
        gpr = list_ref.shape[0] // regions
        me = me_ref[0]
        total = jnp.int32(0)
        for j in range(n_own):
            slab = own_slabs_ref[j]
            start = (slab - SLAB_REACH) * per_slab + regions

            def scan(r, count):
                a = lax.rem(start + r, regions)
                owner = a // reg_dev
                slot = lax.rem(me - owner + n_wide, n_wide) * reg_dev + lax.rem(a, reg_dev)
                listed = list_ref[slot * gpr] == slab
                for e in range(1, gpr):
                    listed = jnp.logical_or(listed, list_ref[slot * gpr + e] == slab)
                sel_ref[count] = slot
                return count + listed.astype(jnp.int32)

            first_group = total // GROUP
            total = lax.fori_loop(0, window, scan, total)
            for e in range(GROUP):
                sel_ref[total + e] = regions
            total = (total + GROUP - 1) // GROUP * GROUP

            def mark(g, carry):
                slab_ref[g] = j
                return carry

            lax.fori_loop(first_group, total // GROUP, mark, 0)
        n_groups = total // GROUP
        for e in range(GROUP):
            sel_ref[total + e] = regions
        slab_ref[n_groups] = 0
        n_pairs = (n_groups + 1) // 2
        last = 2 * n_pairs - 1
        out_ref[...] = jnp.zeros(out_ref.shape, jnp.float32)

        def fill(g, buf):
            g_t = gsites_ref[slab_ref[g]].T
            for e in range(GROUP):
                slot = sel_ref[g * GROUP + e]
                buf[:, e * cap : (e + 1) * cap] = corr_block(g_t, sites_ref[slot])

        def use(g, buf):
            j = slab_ref[g]
            weights = jnp.concatenate(
                [w_ref[sel_ref[g * GROUP + e]] for e in range(GROUP)], axis=1
            )
            out_ref[j] = out_ref[j] + contract_lanes(weights, buf[...])

        fill(0, buf0)

        def pair(i, carry):
            g = 2 * i
            use(g, buf0)
            fill(g + 1, buf1)
            use(g + 1, buf1)
            fill(jnp.minimum(g + 2, last), buf0)
            return carry

        lax.fori_loop(0, n_pairs, pair, 0)
        out_ref[...] = out_ref[...] / cap

    return grid_kernel, window


def grid_stage(me, own_slabs, list_slots, site_slots, w_slots, gsites, reg_dev, n_wide, regions, slab_count):
    solves, cap = w_slots.shape[1:]
    n_own, _, gpts = gsites.shape
    kernel, window = make_grid_kernel(regions // slab_count, reg_dev, n_wide, cap, regions)
    vmem = pl.BlockSpec(memory_space=pltpu.VMEM)
    smem = pl.BlockSpec(memory_space=pltpu.SMEM)
    sel_len = n_own * (window + GROUP) + 2 * GROUP
    return pl.pallas_call(
        kernel,
        out_shape=jax.ShapeDtypeStruct((n_own, solves, gpts), jnp.float32),
        in_specs=[smem, smem, smem, vmem, vmem, vmem],
        out_specs=vmem,
        scratch_shapes=[
            pltpu.SMEM((sel_len,), jnp.int32),
            pltpu.SMEM((sel_len // GROUP + 2,), jnp.int32),
            pltpu.VMEM((gpts, GROUP * cap), jnp.float32),
            pltpu.VMEM((gpts, GROUP * cap), jnp.float32),
        ],
    )(me, own_slabs, list_slots, site_slots, w_slots, gsites)


def body(
    obs_latitude,
    obs_offset,
    innovation,
    obs_error,
    region_sizes,
    tile_columns,
    slab_list,
    slab_order,
    grid_latitude,
    grid_offset,
    ridge_weight,
    huber_cut,
    step_size,
):
    reg_dev, capacity = innovation.shape
    n_wide = lax.axis_size("wide")
    regions = reg_dev * n_wide
    margin = reg_dev // 2
    me = lax.axis_index("wide")
    first_row = me * reg_dev
    row_ids = first_row + jnp.arange(reg_dev, dtype=jnp.int32)
    obs_lon = FULL_TURN * (row_ids[:, None].astype(jnp.float32) + obs_offset) / regions
    obs_sites = unit_rows(obs_latitude, obs_lon)
    gpr = slab_list.shape[1]
    n_slab = lax.axis_size("slab")
    assert n_slab == 2 and margin * n_slab == reg_dev
    sidx = lax.axis_index("slab")
    sub = reg_dev // n_slab
    base = (sidx * sub).astype(jnp.int32).reshape(1)
    blocks = n_wide * n_slab
    pairs = ("wide", "slab")
    first = sidx == 0
    bid = me * n_slab + sidx

    live_mask = (jnp.arange(capacity, dtype=jnp.int32)[None, :] < region_sizes[:, None]).astype(
        jnp.float32
    )
    masked = innovation * live_mask
    packed = jnp.concatenate(
        [
            obs_sites[:, :4, :],
            jnp.pad(slab_list.astype(jnp.float32), ((0, 0), (0, capacity - gpr)))[:, None, :],
            masked[:, None, :],
            obs_error[:, None, :],
        ],
        axis=1,
    )
    slots = gather_slots(lax.dynamic_slice_in_dim(packed, sidx * sub, sub, 0), pairs)

    left_rows = jnp.where(
        first, slots[1 * sub : 2 * sub], slots[2 * sub : 3 * sub]
    )
    right_rows = jnp.where(
        first,
        slots[(blocks - 2) * sub : (blocks - 1) * sub],
        slots[(blocks - 1) * sub : blocks * sub],
    )
    spare = jnp.zeros((ROWS, ROWS, capacity), jnp.float32)
    site_slots = jnp.concatenate(
        [jnp.pad(slots[:, :3, :], ((0, 0), (0, ROWS - 3), (0, 0))), spare], axis=0
    )
    list_slots = slots[:, 4, :gpr].astype(jnp.int32).reshape(-1)

    def sites_of(rows):
        return jnp.pad(rows[:, :3, :], ((0, 0), (0, ROWS - 3), (0, 0)))

    sites_wide = jnp.concatenate([sites_of(left_rows), obs_sites, sites_of(right_rows)], axis=0)
    solves = ridge_weight.shape[0]

    def start_weights(masked_rows, error_rows):
        return masked_rows[:, None, :] / ((error_rows * error_rows)[:, None, :] + ridge_weight[None, :, None])

    diagonal = (obs_error * obs_error)[:, None, :] + ridge_weight[None, :, None]
    observed = masked[:, None, :]
    threshold = huber_cut[None, :, None] * obs_error[:, None, :]
    obs_weights = observed / diagonal
    live = live_mask[:, None, :]
    step = jnp.broadcast_to(step_size[:, None], (solves, capacity))
    local_cols = ((tile_columns - first_row + margin) % regions).reshape(-1)
    tile_scale = 2.0 / (capacity * tile_columns.shape[1])
    q1_pairs = [(b, (b - 2) % blocks) if b % 2 == 0 else (b, (b + 2) % blocks) for b in range(blocks)]
    q2_pairs = [(b, (b - 1) % blocks) if b % 2 == 0 else (b, (b + 1) % blocks) for b in range(blocks)]
    other_pairs = [(b, b ^ 1) for b in range(blocks)]

    weights_wide = jnp.concatenate(
        [
            start_weights(left_rows[:, 5, :], left_rows[:, 6, :]),
            obs_weights,
            start_weights(right_rows[:, 5, :], right_rows[:, 6, :]),
        ]
    )
    for sweep_index in range(ITERS):
        mine = update(
            base, sub, local_cols, obs_sites, sites_wide, weights_wide, observed, diagonal,
            threshold, live, step, margin, tile_scale,
        )
        if sweep_index + 1 < ITERS:
            other = lax.ppermute(mine, pairs, other_pairs)
            obs_weights = jnp.where(
                first, jnp.concatenate([mine, other]), jnp.concatenate([other, mine])
            )
            q1 = lax.ppermute(mine, pairs, q1_pairs)
            q2 = lax.ppermute(mine, pairs, q2_pairs)
            left = jnp.where(first, q2, q1)
            right = jnp.where(first, q1, q2)
            weights_wide = jnp.concatenate([left, obs_weights, right])
    w_gathered = gather_slots(mine, pairs)
    obs_weights = jnp.where(
        first,
        jnp.concatenate([w_gathered[:sub], w_gathered[(blocks - 1) * sub :]]),
        jnp.concatenate([w_gathered[sub : 2 * sub], w_gathered[:sub]]),
    )
    w_slots = jnp.concatenate(
        [w_gathered, jnp.zeros((ROWS, solves, capacity), jnp.float32)], axis=0
    )

    slab_count = slab_order.shape[0]
    n_own = slab_count // (n_wide * n_slab)
    pos0 = (me * n_slab + lax.axis_index("slab")) * n_own
    own_slabs = lax.dynamic_slice_in_dim(slab_order, pos0, n_own, 0)
    g_lat = grid_latitude[own_slabs]
    g_lon = FULL_TURN * (own_slabs[:, None].astype(jnp.float32) + grid_offset[own_slabs]) / slab_count
    gsites = unit_rows(g_lat, g_lon)
    grid_increment = grid_stage(
        bid.astype(jnp.int32).reshape(1),
        own_slabs,
        list_slots,
        site_slots,
        w_slots,
        gsites,
        sub,
        blocks,
        regions,
        slab_count,
    )
    return (obs_weights, grid_increment)


def solution(mesh):
    in_specs = (
        P(("groups", "wide"), None),
        P(("groups", "wide"), None),
        P(("groups", "wide"), None),
        P(("groups", "wide"), None),
        P(("groups", "wide")),
        P(("groups", "wide"), None),
        P(("groups", "wide"), None),
        P("groups"),
        P(),
        P(),
        P("narrow"),
        P("narrow"),
        P("narrow"),
    )
    out_specs = (
        P(("groups", "wide"), "narrow", None),
        P(("groups", "wide", "slab"), "narrow", None),
    )
    return jax.shard_map(body, mesh=mesh, in_specs=in_specs, out_specs=out_specs, check_vma=False)
```

```python
import jax
import jax.numpy as jnp
from jax import lax
from jax.experimental import pallas as pl
from jax.experimental.pallas import tpu as pltpu
from jax.sharding import PartitionSpec as P

ITERS = 2
SLAB_REACH = 4

DECAY_RATE = 1.0 / 0.15
FULL_TURN = 6.283185307179586
HIGHEST = lax.Precision.HIGHEST
ROWS = 8
GROUP = 4


def with_halo(cells, axis, width):
    count = lax.axis_size(axis)
    head = lax.slice_in_dim(cells, 0, width, axis=0)
    tail = lax.slice_in_dim(cells, cells.shape[0] - width, cells.shape[0], axis=0)
    return jnp.concatenate(
        [
            lax.ppermute(tail, axis, [(i, (i + 1) % count) for i in range(count)]),
            cells,
            lax.ppermute(head, axis, [((i + 1) % count, i) for i in range(count)]),
        ],
        axis=0,
    )


def gather_slots(x, axis):
    count = lax.axis_size(axis)
    parts = [x]
    for s in range(1, count):
        parts.append(lax.ppermute(x, axis, [(i, (i + s) % count) for i in range(count)]))
    return jnp.concatenate(parts, axis=0)


def unit_rows(latitude, longitude):
    c = jnp.cos(latitude)
    zero = jnp.zeros_like(latitude)
    return jnp.stack(
        [c * jnp.cos(longitude), c * jnp.sin(longitude), jnp.sin(latitude)] + [zero] * (ROWS - 3),
        axis=-2,
    )


def corr_cols(cx, cy, cz, row):
    dx = cx - row[0:1, :]
    dy = cy - row[1:2, :]
    dz = cz - row[2:3, :]
    d2 = dx * dx + dy * dy + dz * dz
    return jnp.exp(jnp.sqrt(d2) * (-DECAY_RATE))


def corr_block(col_t, row):
    dx = col_t[:, 0:1] - row[0:1, :]
    dy = col_t[:, 1:2] - row[1:2, :]
    dz = col_t[:, 2:3] - row[2:3, :]
    d2 = dx * dx + dy * dy + dz * dz
    return jnp.exp(jnp.sqrt(d2) * (-DECAY_RATE))


def contract_lanes(w, c):
    return lax.dot_general(
        w, c, (((1,), (1,)), ((), ())), precision=HIGHEST, preferred_element_type=jnp.float32
    )


def make_update_kernel(margin, tile_scale):
    def update_kernel(
        base_ref, cols_ref, own_ref, halo_ref, w_ref, obs_ref, diag_ref, thr_ref, live_ref,
        step_ref, out_ref, buf0, buf1,
    ):
        reg_dev, _, cap = own_ref.shape
        count = out_ref.shape[0]
        tiles = cols_ref.shape[0] // reg_dev
        base = base_ref[0]

        def fill(i, buf):
            a = i + base
            own_t = own_ref[a].T
            for t in range(tiles):
                b = cols_ref[a * tiles + t]
                buf[:, t * cap : (t + 1) * cap] = corr_block(own_t, halo_ref[b])

        def use(i, buf):
            a = i + base
            weights = jnp.concatenate(
                [w_ref[cols_ref[a * tiles + t]] for t in range(tiles)], axis=1
            )
            cov = contract_lanes(weights, buf[...])
            current = w_ref[a + margin]
            diag = diag_ref[a]
            thr = thr_ref[a]
            applied = cov * tile_scale + diag * current
            residual = (obs_ref[a] - applied) * live_ref[a]
            factor = thr / jnp.maximum(jnp.abs(residual), thr)
            out_ref[i] = current + step_ref[...] * factor * residual / diag

        fill(0, buf0)

        def pair(i, carry):
            a = 2 * i
            use(a, buf0)
            fill(a + 1, buf1)
            use(a + 1, buf1)
            fill(jnp.minimum(a + 2, count - 1), buf0)
            return carry

        lax.fori_loop(0, count // 2, pair, 0)

    return update_kernel


def update(base, count, cols, own_sites, halo_sites, halo_w, observed, diagonal, threshold, live, step, margin, tile_scale):
    reg_dev, _, cap = own_sites.shape
    assert count % 2 == 0
    tiles = cols.shape[0] // reg_dev
    vmem = pl.BlockSpec(memory_space=pltpu.VMEM)
    smem = pl.BlockSpec(memory_space=pltpu.SMEM)
    return pl.pallas_call(
        make_update_kernel(margin, tile_scale),
        out_shape=jax.ShapeDtypeStruct((count,) + diagonal.shape[1:], jnp.float32),
        in_specs=[smem, smem] + [vmem] * 8,
        out_specs=vmem,
        scratch_shapes=[pltpu.VMEM((cap, tiles * cap), jnp.float32)] * 2,
    )(base, cols, own_sites, halo_sites, halo_w, observed, diagonal, threshold, live, step)


def make_grid_kernel(per_slab, reg_dev, n_wide, cap, regions):
    window = (2 * SLAB_REACH + 1) * per_slab

    def grid_kernel(
        me_ref, own_slabs_ref, list_ref, sites_ref, w_ref, gsites_ref, out_ref,
        sel_ref, slab_ref, buf0, buf1, cols_ref,
    ):
        n_own = out_ref.shape[0]
        gpr = list_ref.shape[0] // regions
        me = me_ref[0]
        total = jnp.int32(0)
        for j in range(n_own):
            slab = own_slabs_ref[j]
            start = (slab - SLAB_REACH) * per_slab + regions

            def scan(r, count):
                a = lax.rem(start + r, regions)
                owner = a // reg_dev
                slot = lax.rem(me - owner + n_wide, n_wide) * reg_dev + lax.rem(a, reg_dev)
                listed = list_ref[slot * gpr] == slab
                for e in range(1, gpr):
                    listed = jnp.logical_or(listed, list_ref[slot * gpr + e] == slab)
                sel_ref[count] = slot
                return count + listed.astype(jnp.int32)

            first_group = total // GROUP
            total = lax.fori_loop(0, window, scan, total)
            for e in range(GROUP):
                sel_ref[total + e] = regions
            total = (total + GROUP - 1) // GROUP * GROUP

            def mark(g, carry):
                slab_ref[g] = j
                return carry

            lax.fori_loop(first_group, total // GROUP, mark, 0)
        n_groups = total // GROUP
        for e in range(GROUP):
            sel_ref[total + e] = regions
        slab_ref[n_groups] = 0
        n_pairs = (n_groups + 1) // 2
        last = 2 * n_pairs - 1
        out_ref[...] = jnp.zeros(out_ref.shape, jnp.float32)
        gpts = out_ref.shape[2]
        for j in range(n_own):
            g_t = gsites_ref[j].T
            for c in range(3):
                cols_ref[3 * j + c] = jnp.broadcast_to(g_t[:, c : c + 1], (gpts, cap))

        def fill(g, buf):
            j = slab_ref[g]
            cx = cols_ref[3 * j]
            cy = cols_ref[3 * j + 1]
            cz = cols_ref[3 * j + 2]
            for e in range(GROUP):
                slot = sel_ref[g * GROUP + e]
                buf[:, e * cap : (e + 1) * cap] = corr_cols(cx, cy, cz, sites_ref[slot])

        def use(g, buf):
            j = slab_ref[g]
            weights = jnp.concatenate(
                [w_ref[sel_ref[g * GROUP + e]] for e in range(GROUP)], axis=1
            )
            out_ref[j] = out_ref[j] + contract_lanes(weights, buf[...])

        fill(0, buf0)

        def pair(i, carry):
            g = 2 * i
            use(g, buf0)
            fill(g + 1, buf1)
            use(g + 1, buf1)
            fill(jnp.minimum(g + 2, last), buf0)
            return carry

        lax.fori_loop(0, n_pairs, pair, 0)
        out_ref[...] = out_ref[...] / cap

    return grid_kernel, window


def grid_stage(me, own_slabs, list_slots, site_slots, w_slots, gsites, reg_dev, n_wide, regions, slab_count):
    solves, cap = w_slots.shape[1:]
    n_own, _, gpts = gsites.shape
    kernel, window = make_grid_kernel(regions // slab_count, reg_dev, n_wide, cap, regions)
    vmem = pl.BlockSpec(memory_space=pltpu.VMEM)
    smem = pl.BlockSpec(memory_space=pltpu.SMEM)
    sel_len = n_own * (window + GROUP) + 2 * GROUP
    return pl.pallas_call(
        kernel,
        out_shape=jax.ShapeDtypeStruct((n_own, solves, gpts), jnp.float32),
        in_specs=[smem, smem, smem, vmem, vmem, vmem],
        out_specs=vmem,
        scratch_shapes=[
            pltpu.SMEM((sel_len,), jnp.int32),
            pltpu.SMEM((sel_len // GROUP + 2,), jnp.int32),
            pltpu.VMEM((gpts, GROUP * cap), jnp.float32),
            pltpu.VMEM((gpts, GROUP * cap), jnp.float32),
            pltpu.VMEM((3 * n_own, gpts, cap), jnp.float32),
        ],
    )(me, own_slabs, list_slots, site_slots, w_slots, gsites)


def body(
    obs_latitude,
    obs_offset,
    innovation,
    obs_error,
    region_sizes,
    tile_columns,
    slab_list,
    slab_order,
    grid_latitude,
    grid_offset,
    ridge_weight,
    huber_cut,
    step_size,
):
    reg_dev, capacity = innovation.shape
    n_wide = lax.axis_size("wide")
    regions = reg_dev * n_wide
    margin = reg_dev // 2
    me = lax.axis_index("wide")
    first_row = me * reg_dev
    row_ids = first_row + jnp.arange(reg_dev, dtype=jnp.int32)
    obs_lon = FULL_TURN * (row_ids[:, None].astype(jnp.float32) + obs_offset) / regions
    obs_sites = unit_rows(obs_latitude, obs_lon)
    gpr = slab_list.shape[1]
    packed = jnp.concatenate(
        [
            obs_sites[:, :4, :],
            jnp.pad(slab_list.astype(jnp.float32), ((0, 0), (0, capacity - gpr)))[:, None, :],
        ],
        axis=1,
    )
    slots = gather_slots(packed, "wide")
    spare = jnp.zeros((ROWS, ROWS, capacity), jnp.float32)
    site_slots = jnp.concatenate(
        [jnp.pad(slots[:, :3, :], ((0, 0), (0, ROWS - 3), (0, 0))), spare], axis=0
    )
    list_slots = slots[:, 4, :gpr].astype(jnp.int32).reshape(-1)
    left = site_slots[2 * reg_dev - margin : 2 * reg_dev]
    right = site_slots[(n_wide - 1) * reg_dev : (n_wide - 1) * reg_dev + margin]
    sites_wide = jnp.concatenate([left, obs_sites, right], axis=0)
    live_mask = (jnp.arange(capacity, dtype=jnp.int32)[None, :] < region_sizes[:, None]).astype(
        jnp.float32
    )
    solves = ridge_weight.shape[0]
    diagonal = (obs_error * obs_error)[:, None, :] + ridge_weight[None, :, None]
    observed = (innovation * live_mask)[:, None, :]
    threshold = huber_cut[None, :, None] * obs_error[:, None, :]
    obs_weights = observed / diagonal
    live = live_mask[:, None, :]
    step = jnp.broadcast_to(step_size[:, None], (solves, capacity))
    local_cols = ((tile_columns - first_row + margin) % regions).reshape(-1)
    tile_scale = 2.0 / (capacity * tile_columns.shape[1])
    n_slab = lax.axis_size("slab")
    assert n_slab == 2 and margin * n_slab == reg_dev
    sidx = lax.axis_index("slab")
    sub = reg_dev // n_slab
    base = (sidx * sub).astype(jnp.int32).reshape(1)
    blocks = n_wide * n_slab
    pairs = ("wide", "slab")
    other_pairs = [(b, b ^ 1) for b in range(blocks)]
    q1_pairs = [(b, (b - 2) % blocks) if b % 2 == 0 else (b, (b + 2) % blocks) for b in range(blocks)]
    q2_pairs = [(b, (b - 1) % blocks) if b % 2 == 0 else (b, (b + 1) % blocks) for b in range(blocks)]
    first = sidx == 0

    def own_rows(mine):
        other = lax.ppermute(mine, pairs, other_pairs)
        return jnp.where(first, jnp.concatenate([mine, other]), jnp.concatenate([other, mine]))

    weights_wide = with_halo(obs_weights, "wide", margin)
    for sweep_index in range(ITERS):
        mine = update(
            base, sub, local_cols, obs_sites, sites_wide, weights_wide, observed, diagonal,
            threshold, live, step, margin, tile_scale,
        )
        obs_weights = own_rows(mine)
        if sweep_index + 1 < ITERS:
            q1 = lax.ppermute(mine, pairs, q1_pairs)
            q2 = lax.ppermute(mine, pairs, q2_pairs)
            left = jnp.where(first, q2, q1)
            right = jnp.where(first, q1, q2)
            weights_wide = jnp.concatenate([left, obs_weights, right])
    w_slots = jnp.concatenate(
        [gather_slots(obs_weights, "wide"), jnp.zeros((ROWS, solves, capacity), jnp.float32)], axis=0
    )

    slab_count = slab_order.shape[0]
    n_own = slab_count // (n_wide * n_slab)
    pos0 = (me * n_slab + lax.axis_index("slab")) * n_own
    own_slabs = lax.dynamic_slice_in_dim(slab_order, pos0, n_own, 0)
    g_lat = grid_latitude[own_slabs]
    g_lon = FULL_TURN * (own_slabs[:, None].astype(jnp.float32) + grid_offset[own_slabs]) / slab_count
    gsites = unit_rows(g_lat, g_lon)
    grid_increment = grid_stage(
        me.astype(jnp.int32).reshape(1),
        own_slabs,
        list_slots,
        site_slots,
        w_slots,
        gsites,
        reg_dev,
        n_wide,
        regions,
        slab_count,
    )
    return (obs_weights, grid_increment)


def solution(mesh):
    in_specs = (
        P(("groups", "wide"), None),
        P(("groups", "wide"), None),
        P(("groups", "wide"), None),
        P(("groups", "wide"), None),
        P(("groups", "wide")),
        P(("groups", "wide"), None),
        P(("groups", "wide"), None),
        P("groups"),
        P(),
        P(),
        P("narrow"),
        P("narrow"),
        P("narrow"),
    )
    out_specs = (
        P(("groups", "wide"), "narrow", None),
        P(("groups", "wide", "slab"), "narrow", None),
    )
    return jax.shard_map(body, mesh=mesh, in_specs=in_specs, out_specs=out_specs, check_vma=False)
```

```python
import jax
import jax.numpy as jnp
from jax import lax
from jax.experimental import pallas as pl
from jax.experimental.pallas import tpu as pltpu
from jax.sharding import PartitionSpec as P

ITERS = 2
SLAB_REACH = 4

DECAY_RATE = 1.0 / 0.15
FULL_TURN = 6.283185307179586
HIGHEST = lax.Precision.HIGHEST
ROWS = 8
GROUP = 2


def with_halo(cells, axis, width):
    count = lax.axis_size(axis)
    head = lax.slice_in_dim(cells, 0, width, axis=0)
    tail = lax.slice_in_dim(cells, cells.shape[0] - width, cells.shape[0], axis=0)
    return jnp.concatenate(
        [
            lax.ppermute(tail, axis, [(i, (i + 1) % count) for i in range(count)]),
            cells,
            lax.ppermute(head, axis, [((i + 1) % count, i) for i in range(count)]),
        ],
        axis=0,
    )


def gather_slots(x, axis):
    count = lax.axis_size(axis)
    parts = [x]
    for s in range(1, count):
        parts.append(lax.ppermute(x, axis, [(i, (i + s) % count) for i in range(count)]))
    return jnp.concatenate(parts, axis=0)


def unit_rows(latitude, longitude):
    c = jnp.cos(latitude)
    zero = jnp.zeros_like(latitude)
    return jnp.stack(
        [c * jnp.cos(longitude), c * jnp.sin(longitude), jnp.sin(latitude)] + [zero] * (ROWS - 3),
        axis=-2,
    )


def corr_block(col_t, row):
    dx = col_t[:, 0:1] - row[0:1, :]
    dy = col_t[:, 1:2] - row[1:2, :]
    dz = col_t[:, 2:3] - row[2:3, :]
    d2 = dx * dx + dy * dy + dz * dz
    return jnp.exp(jnp.sqrt(d2) * (-DECAY_RATE))


def contract_lanes(w, c):
    return lax.dot_general(
        w, c, (((1,), (1,)), ((), ())), precision=HIGHEST, preferred_element_type=jnp.float32
    )


def make_update_kernel(margin, tile_scale):
    def update_kernel(
        base_ref, cols_ref, own_ref, halo_ref, w_ref, obs_ref, diag_ref, thr_ref, live_ref,
        step_ref, out_ref, buf0, buf1,
    ):
        reg_dev, _, cap = own_ref.shape
        count = out_ref.shape[0]
        tiles = cols_ref.shape[0] // reg_dev
        base = base_ref[0]

        def fill(i, buf):
            a = i + base
            own_t = own_ref[a].T
            for t in range(tiles):
                b = cols_ref[a * tiles + t]
                buf[:, t * cap : (t + 1) * cap] = corr_block(own_t, halo_ref[b])

        def use(i, buf):
            a = i + base
            weights = jnp.concatenate(
                [w_ref[cols_ref[a * tiles + t]] for t in range(tiles)], axis=1
            )
            cov = contract_lanes(weights, buf[...])
            current = w_ref[a + margin]
            diag = diag_ref[a]
            thr = thr_ref[a]
            applied = cov * tile_scale + diag * current
            residual = (obs_ref[a] - applied) * live_ref[a]
            factor = thr / jnp.maximum(jnp.abs(residual), thr)
            out_ref[i] = current + step_ref[...] * factor * residual / diag

        fill(0, buf0)

        def pair(i, carry):
            a = 2 * i
            use(a, buf0)
            fill(a + 1, buf1)
            use(a + 1, buf1)
            fill(jnp.minimum(a + 2, count - 1), buf0)
            return carry

        lax.fori_loop(0, count // 2, pair, 0)

    return update_kernel


def update(base, count, cols, own_sites, halo_sites, halo_w, observed, diagonal, threshold, live, step, margin, tile_scale):
    reg_dev, _, cap = own_sites.shape
    assert count % 2 == 0
    tiles = cols.shape[0] // reg_dev
    vmem = pl.BlockSpec(memory_space=pltpu.VMEM)
    smem = pl.BlockSpec(memory_space=pltpu.SMEM)
    return pl.pallas_call(
        make_update_kernel(margin, tile_scale),
        out_shape=jax.ShapeDtypeStruct((count,) + diagonal.shape[1:], jnp.float32),
        in_specs=[smem, smem] + [vmem] * 8,
        out_specs=vmem,
        scratch_shapes=[pltpu.VMEM((cap, tiles * cap), jnp.float32)] * 2,
    )(base, cols, own_sites, halo_sites, halo_w, observed, diagonal, threshold, live, step)


def make_grid_kernel(per_slab, reg_dev, n_wide, cap, regions):
    window = (2 * SLAB_REACH + 1) * per_slab

    def grid_kernel(
        me_ref, own_slabs_ref, list_ref, sites_ref, w_ref, gsites_ref, out_ref,
        sel_ref, slab_ref, buf0, buf1,
    ):
        n_own = out_ref.shape[0]
        gpr = list_ref.shape[0] // regions
        me = me_ref[0]
        total = jnp.int32(0)
        for j in range(n_own):
            slab = own_slabs_ref[j]
            start = (slab - SLAB_REACH) * per_slab + regions

            def scan(r, count):
                a = lax.rem(start + r, regions)
                owner = a // reg_dev
                slot = lax.rem(me - owner + n_wide, n_wide) * reg_dev + lax.rem(a, reg_dev)
                listed = list_ref[slot * gpr] == slab
                for e in range(1, gpr):
                    listed = jnp.logical_or(listed, list_ref[slot * gpr + e] == slab)
                sel_ref[count] = slot
                return count + listed.astype(jnp.int32)

            first_group = total // GROUP
            total = lax.fori_loop(0, window, scan, total)
            for e in range(GROUP):
                sel_ref[total + e] = regions
            total = (total + GROUP - 1) // GROUP * GROUP

            def mark(g, carry):
                slab_ref[g] = j
                return carry

            lax.fori_loop(first_group, total // GROUP, mark, 0)
        n_groups = total // GROUP
        for e in range(GROUP):
            sel_ref[total + e] = regions
        slab_ref[n_groups] = 0
        n_pairs = (n_groups + 1) // 2
        last = 2 * n_pairs - 1
        out_ref[...] = jnp.zeros(out_ref.shape, jnp.float32)

        def fill(g, buf):
            g_t = gsites_ref[slab_ref[g]].T
            for e in range(GROUP):
                slot = sel_ref[g * GROUP + e]
                buf[:, e * cap : (e + 1) * cap] = corr_block(g_t, sites_ref[slot])

        def use(g, buf):
            j = slab_ref[g]
            weights = jnp.concatenate(
                [w_ref[sel_ref[g * GROUP + e]] for e in range(GROUP)], axis=1
            )
            out_ref[j] = out_ref[j] + contract_lanes(weights, buf[...])

        fill(0, buf0)

        def pair(i, carry):
            g = 2 * i
            use(g, buf0)
            fill(g + 1, buf1)
            use(g + 1, buf1)
            fill(jnp.minimum(g + 2, last), buf0)
            return carry

        lax.fori_loop(0, n_pairs, pair, 0)
        out_ref[...] = out_ref[...] / cap

    return grid_kernel, window


def grid_stage(me, own_slabs, list_slots, site_slots, w_slots, gsites, reg_dev, n_wide, regions, slab_count):
    solves, cap = w_slots.shape[1:]
    n_own, _, gpts = gsites.shape
    kernel, window = make_grid_kernel(regions // slab_count, reg_dev, n_wide, cap, regions)
    vmem = pl.BlockSpec(memory_space=pltpu.VMEM)
    smem = pl.BlockSpec(memory_space=pltpu.SMEM)
    sel_len = n_own * (window + GROUP) + 2 * GROUP
    return pl.pallas_call(
        kernel,
        out_shape=jax.ShapeDtypeStruct((n_own, solves, gpts), jnp.float32),
        in_specs=[smem, smem, smem, vmem, vmem, vmem],
        out_specs=vmem,
        scratch_shapes=[
            pltpu.SMEM((sel_len,), jnp.int32),
            pltpu.SMEM((sel_len // GROUP + 2,), jnp.int32),
            pltpu.VMEM((gpts, GROUP * cap), jnp.float32),
            pltpu.VMEM((gpts, GROUP * cap), jnp.float32),
        ],
    )(me, own_slabs, list_slots, site_slots, w_slots, gsites)


def body(
    obs_latitude,
    obs_offset,
    innovation,
    obs_error,
    region_sizes,
    tile_columns,
    slab_list,
    slab_order,
    grid_latitude,
    grid_offset,
    ridge_weight,
    huber_cut,
    step_size,
):
    reg_dev, capacity = innovation.shape
    n_wide = lax.axis_size("wide")
    regions = reg_dev * n_wide
    margin = reg_dev // 2
    me = lax.axis_index("wide")
    first_row = me * reg_dev
    row_ids = first_row + jnp.arange(reg_dev, dtype=jnp.int32)
    obs_lon = FULL_TURN * (row_ids[:, None].astype(jnp.float32) + obs_offset) / regions
    obs_sites = unit_rows(obs_latitude, obs_lon)
    gpr = slab_list.shape[1]
    packed = jnp.concatenate(
        [
            obs_sites[:, :4, :],
            jnp.pad(slab_list.astype(jnp.float32), ((0, 0), (0, capacity - gpr)))[:, None, :],
        ],
        axis=1,
    )
    slots = gather_slots(packed, "wide")
    spare = jnp.zeros((ROWS, ROWS, capacity), jnp.float32)
    site_slots = jnp.concatenate(
        [jnp.pad(slots[:, :3, :], ((0, 0), (0, ROWS - 3), (0, 0))), spare], axis=0
    )
    list_slots = slots[:, 4, :gpr].astype(jnp.int32).reshape(-1)
    left = site_slots[2 * reg_dev - margin : 2 * reg_dev]
    right = site_slots[(n_wide - 1) * reg_dev : (n_wide - 1) * reg_dev + margin]
    sites_wide = jnp.concatenate([left, obs_sites, right], axis=0)
    live_mask = (jnp.arange(capacity, dtype=jnp.int32)[None, :] < region_sizes[:, None]).astype(
        jnp.float32
    )
    solves = ridge_weight.shape[0]
    diagonal = (obs_error * obs_error)[:, None, :] + ridge_weight[None, :, None]
    observed = (innovation * live_mask)[:, None, :]
    threshold = huber_cut[None, :, None] * obs_error[:, None, :]
    obs_weights = observed / diagonal
    live = live_mask[:, None, :]
    step = jnp.broadcast_to(step_size[:, None], (solves, capacity))
    local_cols = ((tile_columns - first_row + margin) % regions).reshape(-1)
    tile_scale = 2.0 / (capacity * tile_columns.shape[1])
    n_slab = lax.axis_size("slab")
    assert n_slab == 2 and margin * n_slab == reg_dev
    sidx = lax.axis_index("slab")
    sub = reg_dev // n_slab
    base = (sidx * sub).astype(jnp.int32).reshape(1)
    blocks = n_wide * n_slab
    pairs = ("wide", "slab")
    other_pairs = [(b, b ^ 1) for b in range(blocks)]
    q1_pairs = [(b, (b - 2) % blocks) if b % 2 == 0 else (b, (b + 2) % blocks) for b in range(blocks)]
    q2_pairs = [(b, (b - 1) % blocks) if b % 2 == 0 else (b, (b + 1) % blocks) for b in range(blocks)]
    first = sidx == 0

    def own_rows(mine):
        other = lax.ppermute(mine, pairs, other_pairs)
        return jnp.where(first, jnp.concatenate([mine, other]), jnp.concatenate([other, mine]))

    weights_wide = with_halo(obs_weights, "wide", margin)
    for sweep_index in range(ITERS):
        mine = update(
            base, sub, local_cols, obs_sites, sites_wide, weights_wide, observed, diagonal,
            threshold, live, step, margin, tile_scale,
        )
        obs_weights = own_rows(mine)
        if sweep_index + 1 < ITERS:
            q1 = lax.ppermute(mine, pairs, q1_pairs)
            q2 = lax.ppermute(mine, pairs, q2_pairs)
            left = jnp.where(first, q2, q1)
            right = jnp.where(first, q1, q2)
            weights_wide = jnp.concatenate([left, obs_weights, right])
    w_slots = jnp.concatenate(
        [gather_slots(obs_weights, "wide"), jnp.zeros((ROWS, solves, capacity), jnp.float32)], axis=0
    )

    slab_count = slab_order.shape[0]
    n_own = slab_count // (n_wide * n_slab)
    pos0 = (me * n_slab + lax.axis_index("slab")) * n_own
    own_slabs = lax.dynamic_slice_in_dim(slab_order, pos0, n_own, 0)
    g_lat = grid_latitude[own_slabs]
    g_lon = FULL_TURN * (own_slabs[:, None].astype(jnp.float32) + grid_offset[own_slabs]) / slab_count
    gsites = unit_rows(g_lat, g_lon)
    grid_increment = grid_stage(
        me.astype(jnp.int32).reshape(1),
        own_slabs,
        list_slots,
        site_slots,
        w_slots,
        gsites,
        reg_dev,
        n_wide,
        regions,
        slab_count,
    )
    return (obs_weights, grid_increment)


def solution(mesh):
    in_specs = (
        P(("groups", "wide"), None),
        P(("groups", "wide"), None),
        P(("groups", "wide"), None),
        P(("groups", "wide"), None),
        P(("groups", "wide")),
        P(("groups", "wide"), None),
        P(("groups", "wide"), None),
        P("groups"),
        P(),
        P(),
        P("narrow"),
        P("narrow"),
        P("narrow"),
    )
    out_specs = (
        P(("groups", "wide"), "narrow", None),
        P(("groups", "wide", "slab"), "narrow", None),
    )
    return jax.shard_map(body, mesh=mesh, in_specs=in_specs, out_specs=out_specs, check_vma=False)
```

```python
import jax
import jax.numpy as jnp
from jax import lax
from jax.experimental import pallas as pl
from jax.experimental.pallas import tpu as pltpu
from jax.sharding import PartitionSpec as P

ITERS = 2
SLAB_REACH = 4

DECAY_RATE = 1.0 / 0.15
FULL_TURN = 6.283185307179586
HIGHEST = lax.Precision.HIGHEST
ROWS = 8
GROUP = 4


def with_halo(cells, axis, width):
    count = lax.axis_size(axis)
    head = lax.slice_in_dim(cells, 0, width, axis=0)
    tail = lax.slice_in_dim(cells, cells.shape[0] - width, cells.shape[0], axis=0)
    return jnp.concatenate(
        [
            lax.ppermute(tail, axis, [(i, (i + 1) % count) for i in range(count)]),
            cells,
            lax.ppermute(head, axis, [((i + 1) % count, i) for i in range(count)]),
        ],
        axis=0,
    )


def gather_slots(x, axis):
    count = lax.axis_size(axis)
    parts = [x]
    for s in range(1, count):
        parts.append(lax.ppermute(x, axis, [(i, (i + s) % count) for i in range(count)]))
    return jnp.concatenate(parts, axis=0)


def unit_rows(latitude, longitude):
    c = jnp.cos(latitude)
    zero = jnp.zeros_like(latitude)
    return jnp.stack(
        [c * jnp.cos(longitude), c * jnp.sin(longitude), jnp.sin(latitude)] + [zero] * (ROWS - 3),
        axis=-2,
    )


def corr_block(col_t, row):
    dx = col_t[:, 0:1] - row[0:1, :]
    dy = col_t[:, 1:2] - row[1:2, :]
    dz = col_t[:, 2:3] - row[2:3, :]
    d2 = dx * dx + dy * dy + dz * dz
    return jnp.exp(jnp.sqrt(d2) * (-DECAY_RATE))


def contract_lanes(w, c):
    return lax.dot_general(
        w, c, (((1,), (1,)), ((), ())), precision=HIGHEST, preferred_element_type=jnp.float32
    )


def make_update_kernel(margin, tile_scale, cached):
    def update_kernel(
        base_ref, cols_ref, own_ref, halo_ref, w_ref, obs_ref, diag_ref, thr_ref, live_ref,
        step_ref, *rest,
    ):
        if cached:
            cache_ref, out_ref = rest
        else:
            out_ref, cache_ref = rest
        reg_dev, _, cap = own_ref.shape
        count = out_ref.shape[0]
        tiles = cols_ref.shape[0] // reg_dev
        base = base_ref[0]

        def fill(i):
            a = i + base
            own_t = own_ref[a].T
            for t in range(tiles):
                b = cols_ref[a * tiles + t]
                cache_ref[i, :, t * cap : (t + 1) * cap] = corr_block(own_t, halo_ref[b])

        def use(i):
            a = i + base
            weights = jnp.concatenate(
                [w_ref[cols_ref[a * tiles + t]] for t in range(tiles)], axis=1
            )
            cov = contract_lanes(weights, cache_ref[i])
            current = w_ref[a + margin]
            diag = diag_ref[a]
            thr = thr_ref[a]
            applied = cov * tile_scale + diag * current
            residual = (obs_ref[a] - applied) * live_ref[a]
            factor = thr / jnp.maximum(jnp.abs(residual), thr)
            out_ref[i] = current + step_ref[...] * factor * residual / diag

        if cached:
            def one(i, carry):
                use(i)
                return carry

            lax.fori_loop(0, count, one, 0)
        else:
            fill(0)

            def pair(i, carry):
                a = 2 * i
                use(a)
                fill(a + 1)
                use(a + 1)
                fill(jnp.minimum(a + 2, count - 1))
                return carry

            lax.fori_loop(0, count // 2, pair, 0)

    return update_kernel


def update(base, count, cols, own_sites, halo_sites, halo_w, observed, diagonal, threshold, live, step, margin, tile_scale, cache=None):
    reg_dev, _, cap = own_sites.shape
    assert count % 2 == 0
    tiles = cols.shape[0] // reg_dev
    vmem = pl.BlockSpec(memory_space=pltpu.VMEM)
    smem = pl.BlockSpec(memory_space=pltpu.SMEM)
    new_w = jax.ShapeDtypeStruct((count,) + diagonal.shape[1:], jnp.float32)
    args = [base, cols, own_sites, halo_sites, halo_w, observed, diagonal, threshold, live, step]
    if cache is None:
        out_shape = (new_w, jax.ShapeDtypeStruct((count, cap, tiles * cap), jnp.float32))
        out_specs = (vmem, vmem)
    else:
        args.append(cache)
        out_shape = new_w
        out_specs = vmem
    return pl.pallas_call(
        make_update_kernel(margin, tile_scale, cache is not None),
        out_shape=out_shape,
        in_specs=[smem, smem] + [vmem] * (len(args) - 2),
        out_specs=out_specs,
    )(*args)


def make_grid_kernel(per_slab, reg_dev, n_wide, cap, regions):
    window = (2 * SLAB_REACH + 1) * per_slab

    def grid_kernel(
        me_ref, own_slabs_ref, list_ref, sites_ref, w_ref, gsites_ref, out_ref,
        sel_ref, slab_ref, buf0, buf1,
    ):
        n_own = out_ref.shape[0]
        gpr = list_ref.shape[0] // regions
        me = me_ref[0]
        total = jnp.int32(0)
        for j in range(n_own):
            slab = own_slabs_ref[j]
            start = (slab - SLAB_REACH) * per_slab + regions

            def scan(r, count):
                a = lax.rem(start + r, regions)
                owner = a // reg_dev
                slot = lax.rem(me - owner + n_wide, n_wide) * reg_dev + lax.rem(a, reg_dev)
                listed = list_ref[slot * gpr] == slab
                for e in range(1, gpr):
                    listed = jnp.logical_or(listed, list_ref[slot * gpr + e] == slab)
                sel_ref[count] = slot
                return count + listed.astype(jnp.int32)

            first_group = total // GROUP
            total = lax.fori_loop(0, window, scan, total)
            for e in range(GROUP):
                sel_ref[total + e] = regions
            total = (total + GROUP - 1) // GROUP * GROUP

            def mark(g, carry):
                slab_ref[g] = j
                return carry

            lax.fori_loop(first_group, total // GROUP, mark, 0)
        n_groups = total // GROUP
        for e in range(GROUP):
            sel_ref[total + e] = regions
        slab_ref[n_groups] = 0
        n_pairs = (n_groups + 1) // 2
        last = 2 * n_pairs - 1
        out_ref[...] = jnp.zeros(out_ref.shape, jnp.float32)

        def fill(g, buf):
            g_t = gsites_ref[slab_ref[g]].T
            for e in range(GROUP):
                slot = sel_ref[g * GROUP + e]
                buf[:, e * cap : (e + 1) * cap] = corr_block(g_t, sites_ref[slot])

        def use(g, buf):
            j = slab_ref[g]
            weights = jnp.concatenate(
                [w_ref[sel_ref[g * GROUP + e]] for e in range(GROUP)], axis=1
            )
            out_ref[j] = out_ref[j] + contract_lanes(weights, buf[...])

        fill(0, buf0)

        def pair(i, carry):
            g = 2 * i
            use(g, buf0)
            fill(g + 1, buf1)
            use(g + 1, buf1)
            fill(jnp.minimum(g + 2, last), buf0)
            return carry

        lax.fori_loop(0, n_pairs, pair, 0)
        out_ref[...] = out_ref[...] / cap

    return grid_kernel, window


def grid_stage(me, own_slabs, list_slots, site_slots, w_slots, gsites, reg_dev, n_wide, regions, slab_count):
    solves, cap = w_slots.shape[1:]
    n_own, _, gpts = gsites.shape
    kernel, window = make_grid_kernel(regions // slab_count, reg_dev, n_wide, cap, regions)
    vmem = pl.BlockSpec(memory_space=pltpu.VMEM)
    smem = pl.BlockSpec(memory_space=pltpu.SMEM)
    sel_len = n_own * (window + GROUP) + 2 * GROUP
    return pl.pallas_call(
        kernel,
        out_shape=jax.ShapeDtypeStruct((n_own, solves, gpts), jnp.float32),
        in_specs=[smem, smem, smem, vmem, vmem, vmem],
        out_specs=vmem,
        scratch_shapes=[
            pltpu.SMEM((sel_len,), jnp.int32),
            pltpu.SMEM((sel_len // GROUP + 2,), jnp.int32),
            pltpu.VMEM((gpts, GROUP * cap), jnp.float32),
            pltpu.VMEM((gpts, GROUP * cap), jnp.float32),
        ],
    )(me, own_slabs, list_slots, site_slots, w_slots, gsites)


def body(
    obs_latitude,
    obs_offset,
    innovation,
    obs_error,
    region_sizes,
    tile_columns,
    slab_list,
    slab_order,
    grid_latitude,
    grid_offset,
    ridge_weight,
    huber_cut,
    step_size,
):
    reg_dev, capacity = innovation.shape
    n_wide = lax.axis_size("wide")
    regions = reg_dev * n_wide
    margin = reg_dev // 2
    me = lax.axis_index("wide")
    first_row = me * reg_dev
    row_ids = first_row + jnp.arange(reg_dev, dtype=jnp.int32)
    obs_lon = FULL_TURN * (row_ids[:, None].astype(jnp.float32) + obs_offset) / regions
    obs_sites = unit_rows(obs_latitude, obs_lon)
    gpr = slab_list.shape[1]
    packed = jnp.concatenate(
        [
            obs_sites[:, :4, :],
            jnp.pad(slab_list.astype(jnp.float32), ((0, 0), (0, capacity - gpr)))[:, None, :],
        ],
        axis=1,
    )
    slots = gather_slots(packed, "wide")
    spare = jnp.zeros((ROWS, ROWS, capacity), jnp.float32)
    site_slots = jnp.concatenate(
        [jnp.pad(slots[:, :3, :], ((0, 0), (0, ROWS - 3), (0, 0))), spare], axis=0
    )
    list_slots = slots[:, 4, :gpr].astype(jnp.int32).reshape(-1)
    left = site_slots[2 * reg_dev - margin : 2 * reg_dev]
    right = site_slots[(n_wide - 1) * reg_dev : (n_wide - 1) * reg_dev + margin]
    sites_wide = jnp.concatenate([left, obs_sites, right], axis=0)
    live_mask = (jnp.arange(capacity, dtype=jnp.int32)[None, :] < region_sizes[:, None]).astype(
        jnp.float32
    )
    solves = ridge_weight.shape[0]
    diagonal = (obs_error * obs_error)[:, None, :] + ridge_weight[None, :, None]
    observed = (innovation * live_mask)[:, None, :]
    threshold = huber_cut[None, :, None] * obs_error[:, None, :]
    obs_weights = observed / diagonal
    live = live_mask[:, None, :]
    step = jnp.broadcast_to(step_size[:, None], (solves, capacity))
    local_cols = ((tile_columns - first_row + margin) % regions).reshape(-1)
    tile_scale = 2.0 / (capacity * tile_columns.shape[1])
    n_slab = lax.axis_size("slab")
    assert n_slab == 2 and margin * n_slab == reg_dev
    sidx = lax.axis_index("slab")
    sub = reg_dev // n_slab
    base = (sidx * sub).astype(jnp.int32).reshape(1)
    blocks = n_wide * n_slab
    pairs = ("wide", "slab")
    other_pairs = [(b, b ^ 1) for b in range(blocks)]
    q1_pairs = [(b, (b - 2) % blocks) if b % 2 == 0 else (b, (b + 2) % blocks) for b in range(blocks)]
    q2_pairs = [(b, (b - 1) % blocks) if b % 2 == 0 else (b, (b + 1) % blocks) for b in range(blocks)]
    first = sidx == 0

    def own_rows(mine):
        other = lax.ppermute(mine, pairs, other_pairs)
        return jnp.where(first, jnp.concatenate([mine, other]), jnp.concatenate([other, mine]))

    weights_wide = with_halo(obs_weights, "wide", margin)
    cache = None
    for sweep_index in range(ITERS):
        result = update(
            base, sub, local_cols, obs_sites, sites_wide, weights_wide, observed, diagonal,
            threshold, live, step, margin, tile_scale, cache,
        )
        if cache is None:
            mine, cache = result
        else:
            mine = result
        obs_weights = own_rows(mine)
        if sweep_index + 1 < ITERS:
            q1 = lax.ppermute(mine, pairs, q1_pairs)
            q2 = lax.ppermute(mine, pairs, q2_pairs)
            left = jnp.where(first, q2, q1)
            right = jnp.where(first, q1, q2)
            weights_wide = jnp.concatenate([left, obs_weights, right])
    w_slots = jnp.concatenate(
        [gather_slots(obs_weights, "wide"), jnp.zeros((ROWS, solves, capacity), jnp.float32)], axis=0
    )

    slab_count = slab_order.shape[0]
    n_own = slab_count // (n_wide * n_slab)
    pos0 = (me * n_slab + lax.axis_index("slab")) * n_own
    own_slabs = lax.dynamic_slice_in_dim(slab_order, pos0, n_own, 0)
    g_lat = grid_latitude[own_slabs]
    g_lon = FULL_TURN * (own_slabs[:, None].astype(jnp.float32) + grid_offset[own_slabs]) / slab_count
    gsites = unit_rows(g_lat, g_lon)
    grid_increment = grid_stage(
        me.astype(jnp.int32).reshape(1),
        own_slabs,
        list_slots,
        site_slots,
        w_slots,
        gsites,
        reg_dev,
        n_wide,
        regions,
        slab_count,
    )
    return (obs_weights, grid_increment)


def solution(mesh):
    in_specs = (
        P(("groups", "wide"), None),
        P(("groups", "wide"), None),
        P(("groups", "wide"), None),
        P(("groups", "wide"), None),
        P(("groups", "wide")),
        P(("groups", "wide"), None),
        P(("groups", "wide"), None),
        P("groups"),
        P(),
        P(),
        P("narrow"),
        P("narrow"),
        P("narrow"),
    )
    out_specs = (
        P(("groups", "wide"), "narrow", None),
        P(("groups", "wide", "slab"), "narrow", None),
    )
    return jax.shard_map(body, mesh=mesh, in_specs=in_specs, out_specs=out_specs, check_vma=False)
```

```python
import jax
import jax.numpy as jnp
from jax import lax
from jax.experimental import pallas as pl
from jax.experimental.pallas import tpu as pltpu
from jax.sharding import PartitionSpec as P

ITERS = 2
SLAB_REACH = 4

DECAY_RATE = 1.0 / 0.15
FULL_TURN = 6.283185307179586
HIGHEST = lax.Precision.HIGHEST
MATMUL_PRECISION = lax.Precision.HIGH
ROWS = 8
GROUP = 4


def with_halo(cells, axis, width):
    count = lax.axis_size(axis)
    head = lax.slice_in_dim(cells, 0, width, axis=0)
    tail = lax.slice_in_dim(cells, cells.shape[0] - width, cells.shape[0], axis=0)
    return jnp.concatenate(
        [
            lax.ppermute(tail, axis, [(i, (i + 1) % count) for i in range(count)]),
            cells,
            lax.ppermute(head, axis, [((i + 1) % count, i) for i in range(count)]),
        ],
        axis=0,
    )


def gather_slots(x, axis):
    count = lax.axis_size(axis)
    parts = [x]
    for s in range(1, count):
        parts.append(lax.ppermute(x, axis, [(i, (i + s) % count) for i in range(count)]))
    return jnp.concatenate(parts, axis=0)


def unit_rows(latitude, longitude):
    c = jnp.cos(latitude)
    zero = jnp.zeros_like(latitude)
    return jnp.stack(
        [c * jnp.cos(longitude), c * jnp.sin(longitude), jnp.sin(latitude)] + [zero] * (ROWS - 3),
        axis=-2,
    )


def corr_block(col_t, row):
    dx = col_t[:, 0:1] - row[0:1, :]
    dy = col_t[:, 1:2] - row[1:2, :]
    dz = col_t[:, 2:3] - row[2:3, :]
    d2 = dx * dx + dy * dy + dz * dz
    return jnp.exp(jnp.sqrt(d2) * (-DECAY_RATE))


def contract_lanes(w, c):
    return lax.dot_general(
        w, c, (((1,), (1,)), ((), ())), precision=MATMUL_PRECISION, preferred_element_type=jnp.float32
    )


def make_update_kernel(margin, tile_scale):
    def update_kernel(
        base_ref, cols_ref, own_ref, halo_ref, w_ref, obs_ref, diag_ref, thr_ref, live_ref,
        step_ref, out_ref, buf0, buf1,
    ):
        reg_dev, _, cap = own_ref.shape
        count = out_ref.shape[0]
        tiles = cols_ref.shape[0] // reg_dev
        base = base_ref[0]

        def fill(i, buf):
            a = i + base
            own_t = own_ref[a].T
            for t in range(tiles):
                b = cols_ref[a * tiles + t]
                buf[:, t * cap : (t + 1) * cap] = corr_block(own_t, halo_ref[b])

        def use(i, buf):
            a = i + base
            weights = jnp.concatenate(
                [w_ref[cols_ref[a * tiles + t]] for t in range(tiles)], axis=1
            )
            cov = contract_lanes(weights, buf[...])
            current = w_ref[a + margin]
            diag = diag_ref[a]
            thr = thr_ref[a]
            applied = cov * tile_scale + diag * current
            residual = (obs_ref[a] - applied) * live_ref[a]
            factor = thr / jnp.maximum(jnp.abs(residual), thr)
            out_ref[i] = current + step_ref[...] * factor * residual / diag

        fill(0, buf0)

        def pair(i, carry):
            a = 2 * i
            use(a, buf0)
            fill(a + 1, buf1)
            use(a + 1, buf1)
            fill(jnp.minimum(a + 2, count - 1), buf0)
            return carry

        lax.fori_loop(0, count // 2, pair, 0)

    return update_kernel


def update(base, count, cols, own_sites, halo_sites, halo_w, observed, diagonal, threshold, live, step, margin, tile_scale):
    reg_dev, _, cap = own_sites.shape
    assert count % 2 == 0
    tiles = cols.shape[0] // reg_dev
    vmem = pl.BlockSpec(memory_space=pltpu.VMEM)
    smem = pl.BlockSpec(memory_space=pltpu.SMEM)
    return pl.pallas_call(
        make_update_kernel(margin, tile_scale),
        out_shape=jax.ShapeDtypeStruct((count,) + diagonal.shape[1:], jnp.float32),
        in_specs=[smem, smem] + [vmem] * 8,
        out_specs=vmem,
        scratch_shapes=[pltpu.VMEM((cap, tiles * cap), jnp.float32)] * 2,
    )(base, cols, own_sites, halo_sites, halo_w, observed, diagonal, threshold, live, step)


def make_grid_kernel(per_slab, reg_dev, n_wide, cap, regions):
    window = (2 * SLAB_REACH + 1) * per_slab

    def grid_kernel(
        me_ref, own_slabs_ref, list_ref, sites_ref, w_ref, gsites_ref, out_ref,
        sel_ref, slab_ref, buf0, buf1,
    ):
        n_own = out_ref.shape[0]
        gpr = list_ref.shape[0] // regions
        me = me_ref[0]
        total = jnp.int32(0)
        for j in range(n_own):
            slab = own_slabs_ref[j]
            start = (slab - SLAB_REACH) * per_slab + regions

            def scan(r, count):
                a = lax.rem(start + r, regions)
                owner = a // reg_dev
                slot = lax.rem(me - owner + n_wide, n_wide) * reg_dev + lax.rem(a, reg_dev)
                listed = list_ref[slot * gpr] == slab
                for e in range(1, gpr):
                    listed = jnp.logical_or(listed, list_ref[slot * gpr + e] == slab)
                sel_ref[count] = slot
                return count + listed.astype(jnp.int32)

            first_group = total // GROUP
            total = lax.fori_loop(0, window, scan, total)
            for e in range(GROUP):
                sel_ref[total + e] = regions
            total = (total + GROUP - 1) // GROUP * GROUP

            def mark(g, carry):
                slab_ref[g] = j
                return carry

            lax.fori_loop(first_group, total // GROUP, mark, 0)
        n_groups = total // GROUP
        for e in range(GROUP):
            sel_ref[total + e] = regions
        slab_ref[n_groups] = 0
        n_pairs = (n_groups + 1) // 2
        last = 2 * n_pairs - 1
        out_ref[...] = jnp.zeros(out_ref.shape, jnp.float32)

        def fill(g, buf):
            g_t = gsites_ref[slab_ref[g]].T
            for e in range(GROUP):
                slot = sel_ref[g * GROUP + e]
                buf[:, e * cap : (e + 1) * cap] = corr_block(g_t, sites_ref[slot])

        def use(g, buf):
            j = slab_ref[g]
            weights = jnp.concatenate(
                [w_ref[sel_ref[g * GROUP + e]] for e in range(GROUP)], axis=1
            )
            out_ref[j] = out_ref[j] + contract_lanes(weights, buf[...])

        fill(0, buf0)

        def pair(i, carry):
            g = 2 * i
            use(g, buf0)
            fill(g + 1, buf1)
            use(g + 1, buf1)
            fill(jnp.minimum(g + 2, last), buf0)
            return carry

        lax.fori_loop(0, n_pairs, pair, 0)
        out_ref[...] = out_ref[...] / cap

    return grid_kernel, window


def grid_stage(me, own_slabs, list_slots, site_slots, w_slots, gsites, reg_dev, n_wide, regions, slab_count):
    solves, cap = w_slots.shape[1:]
    n_own, _, gpts = gsites.shape
    kernel, window = make_grid_kernel(regions // slab_count, reg_dev, n_wide, cap, regions)
    vmem = pl.BlockSpec(memory_space=pltpu.VMEM)
    smem = pl.BlockSpec(memory_space=pltpu.SMEM)
    sel_len = n_own * (window + GROUP) + 2 * GROUP
    return pl.pallas_call(
        kernel,
        out_shape=jax.ShapeDtypeStruct((n_own, solves, gpts), jnp.float32),
        in_specs=[smem, smem, smem, vmem, vmem, vmem],
        out_specs=vmem,
        scratch_shapes=[
            pltpu.SMEM((sel_len,), jnp.int32),
            pltpu.SMEM((sel_len // GROUP + 2,), jnp.int32),
            pltpu.VMEM((gpts, GROUP * cap), jnp.float32),
            pltpu.VMEM((gpts, GROUP * cap), jnp.float32),
        ],
    )(me, own_slabs, list_slots, site_slots, w_slots, gsites)


def body(
    obs_latitude,
    obs_offset,
    innovation,
    obs_error,
    region_sizes,
    tile_columns,
    slab_list,
    slab_order,
    grid_latitude,
    grid_offset,
    ridge_weight,
    huber_cut,
    step_size,
):
    reg_dev, capacity = innovation.shape
    n_wide = lax.axis_size("wide")
    regions = reg_dev * n_wide
    margin = reg_dev // 2
    me = lax.axis_index("wide")
    first_row = me * reg_dev
    row_ids = first_row + jnp.arange(reg_dev, dtype=jnp.int32)
    obs_lon = FULL_TURN * (row_ids[:, None].astype(jnp.float32) + obs_offset) / regions
    obs_sites = unit_rows(obs_latitude, obs_lon)
    gpr = slab_list.shape[1]
    packed = jnp.concatenate(
        [
            obs_sites[:, :4, :],
            jnp.pad(slab_list.astype(jnp.float32), ((0, 0), (0, capacity - gpr)))[:, None, :],
        ],
        axis=1,
    )
    slots = gather_slots(packed, "wide")
    spare = jnp.zeros((ROWS, ROWS, capacity), jnp.float32)
    site_slots = jnp.concatenate(
        [jnp.pad(slots[:, :3, :], ((0, 0), (0, ROWS - 3), (0, 0))), spare], axis=0
    )
    list_slots = slots[:, 4, :gpr].astype(jnp.int32).reshape(-1)
    left = site_slots[2 * reg_dev - margin : 2 * reg_dev]
    right = site_slots[(n_wide - 1) * reg_dev : (n_wide - 1) * reg_dev + margin]
    sites_wide = jnp.concatenate([left, obs_sites, right], axis=0)
    live_mask = (jnp.arange(capacity, dtype=jnp.int32)[None, :] < region_sizes[:, None]).astype(
        jnp.float32
    )
    solves = ridge_weight.shape[0]
    diagonal = (obs_error * obs_error)[:, None, :] + ridge_weight[None, :, None]
    observed = (innovation * live_mask)[:, None, :]
    threshold = huber_cut[None, :, None] * obs_error[:, None, :]
    obs_weights = observed / diagonal
    live = live_mask[:, None, :]
    step = jnp.broadcast_to(step_size[:, None], (solves, capacity))
    local_cols = ((tile_columns - first_row + margin) % regions).reshape(-1)
    tile_scale = 2.0 / (capacity * tile_columns.shape[1])
    n_slab = lax.axis_size("slab")
    assert n_slab == 2 and margin * n_slab == reg_dev
    sidx = lax.axis_index("slab")
    sub = reg_dev // n_slab
    base = (sidx * sub).astype(jnp.int32).reshape(1)
    blocks = n_wide * n_slab
    pairs = ("wide", "slab")
    other_pairs = [(b, b ^ 1) for b in range(blocks)]
    q1_pairs = [(b, (b - 2) % blocks) if b % 2 == 0 else (b, (b + 2) % blocks) for b in range(blocks)]
    q2_pairs = [(b, (b - 1) % blocks) if b % 2 == 0 else (b, (b + 1) % blocks) for b in range(blocks)]
    first = sidx == 0

    def own_rows(mine):
        other = lax.ppermute(mine, pairs, other_pairs)
        return jnp.where(first, jnp.concatenate([mine, other]), jnp.concatenate([other, mine]))

    weights_wide = with_halo(obs_weights, "wide", margin)
    for sweep_index in range(ITERS):
        mine = update(
            base, sub, local_cols, obs_sites, sites_wide, weights_wide, observed, diagonal,
            threshold, live, step, margin, tile_scale,
        )
        obs_weights = own_rows(mine)
        if sweep_index + 1 < ITERS:
            q1 = lax.ppermute(mine, pairs, q1_pairs)
            q2 = lax.ppermute(mine, pairs, q2_pairs)
            left = jnp.where(first, q2, q1)
            right = jnp.where(first, q1, q2)
            weights_wide = jnp.concatenate([left, obs_weights, right])
    w_slots = jnp.concatenate(
        [gather_slots(obs_weights, "wide"), jnp.zeros((ROWS, solves, capacity), jnp.float32)], axis=0
    )

    slab_count = slab_order.shape[0]
    n_own = slab_count // (n_wide * n_slab)
    pos0 = (me * n_slab + lax.axis_index("slab")) * n_own
    own_slabs = lax.dynamic_slice_in_dim(slab_order, pos0, n_own, 0)
    g_lat = grid_latitude[own_slabs]
    g_lon = FULL_TURN * (own_slabs[:, None].astype(jnp.float32) + grid_offset[own_slabs]) / slab_count
    gsites = unit_rows(g_lat, g_lon)
    grid_increment = grid_stage(
        me.astype(jnp.int32).reshape(1),
        own_slabs,
        list_slots,
        site_slots,
        w_slots,
        gsites,
        reg_dev,
        n_wide,
        regions,
        slab_count,
    )
    return (obs_weights, grid_increment)


def solution(mesh):
    in_specs = (
        P(("groups", "wide"), None),
        P(("groups", "wide"), None),
        P(("groups", "wide"), None),
        P(("groups", "wide"), None),
        P(("groups", "wide")),
        P(("groups", "wide"), None),
        P(("groups", "wide"), None),
        P("groups"),
        P(),
        P(),
        P("narrow"),
        P("narrow"),
        P("narrow"),
    )
    out_specs = (
        P(("groups", "wide"), "narrow", None),
        P(("groups", "wide", "slab"), "narrow", None),
    )
    return jax.shard_map(body, mesh=mesh, in_specs=in_specs, out_specs=out_specs, check_vma=False)
```

```python
import jax
import jax.numpy as jnp
from jax import lax
from jax.experimental import pallas as pl
from jax.experimental.pallas import tpu as pltpu
from jax.sharding import PartitionSpec as P

ITERS = 2
SLAB_REACH = 4

DECAY_RATE = 1.0 / 0.15
FULL_TURN = 6.283185307179586
HIGHEST = lax.Precision.HIGHEST
MATMUL_PRECISION = lax.Precision.HIGH
ROWS = 8
GROUP = 4


def with_halo(cells, axis, width):
    count = lax.axis_size(axis)
    head = lax.slice_in_dim(cells, 0, width, axis=0)
    tail = lax.slice_in_dim(cells, cells.shape[0] - width, cells.shape[0], axis=0)
    return jnp.concatenate(
        [
            lax.ppermute(tail, axis, [(i, (i + 1) % count) for i in range(count)]),
            cells,
            lax.ppermute(head, axis, [((i + 1) % count, i) for i in range(count)]),
        ],
        axis=0,
    )


def gather_slots(x, axis):
    count = lax.axis_size(axis)
    parts = [x]
    for s in range(1, count):
        parts.append(lax.ppermute(x, axis, [(i, (i + s) % count) for i in range(count)]))
    return jnp.concatenate(parts, axis=0)


def unit_rows(latitude, longitude):
    c = jnp.cos(latitude)
    zero = jnp.zeros_like(latitude)
    return jnp.stack(
        [c * jnp.cos(longitude), c * jnp.sin(longitude), jnp.sin(latitude)] + [zero] * (ROWS - 3),
        axis=-2,
    )


def corr_block(col_t, row):
    dx = col_t[:, 0:1] - row[0:1, :]
    dy = col_t[:, 1:2] - row[1:2, :]
    dz = col_t[:, 2:3] - row[2:3, :]
    d2 = dx * dx + dy * dy + dz * dz
    return jnp.exp(jnp.sqrt(d2) * (-DECAY_RATE))


def contract_lanes(w, c):
    return lax.dot_general(
        w, c, (((1,), (1,)), ((), ())), precision=MATMUL_PRECISION, preferred_element_type=jnp.float32
    )


def make_update_kernel(margin, tile_scale, regions, first_sweep):
    def update_kernel(scal_ref, tc_ref, sizes_ref, ridge_ref, huber_ref, step_ref, *refs):
        if first_sweep:
            own_ref, sl_ref, sr_ref, innov_ref, err_ref, wl_ref, wo_ref, wr_ref = refs[:8]
        else:
            own_ref, sl_ref, sr_ref, innov_ref, err_ref, q1_ref, q2_ref, mine_ref, other_ref = refs[:9]
        out_ref, buf0, buf1, hs_ref, hw_ref = refs[-5:]
        reg_dev, _, cap = own_ref.shape
        count, solves, _ = out_ref.shape
        tiles = tc_ref.shape[1]
        base = scal_ref[0]
        first_row = scal_ref[1]

        hs_ref[0:margin] = sl_ref[...]
        hs_ref[margin : margin + reg_dev] = own_ref[...]
        hs_ref[margin + reg_dev :] = sr_ref[...]
        if first_sweep:
            hw_ref[0:margin] = wl_ref[...]
            hw_ref[margin : margin + reg_dev] = wo_ref[...]
            hw_ref[margin + reg_dev :] = wr_ref[...]
        else:
            sel = scal_ref[2] == 1
            q1 = q1_ref[...]
            q2 = q2_ref[...]
            mine = mine_ref[...]
            other = other_ref[...]
            hw_ref[0:margin] = jnp.where(sel, q2, q1)
            hw_ref[margin : margin + count] = jnp.where(sel, mine, other)
            hw_ref[margin + count : margin + 2 * count] = jnp.where(sel, other, mine)
            hw_ref[margin + reg_dev :] = jnp.where(sel, q1, q2)

        rows = lax.broadcasted_iota(jnp.int32, (solves, cap), 0)
        ridge_b = jnp.zeros((solves, cap), jnp.float32)
        huber_b = jnp.zeros((solves, cap), jnp.float32)
        step_b = jnp.zeros((solves, cap), jnp.float32)
        for k in range(solves):
            ridge_b = jnp.where(rows == k, ridge_ref[k], ridge_b)
            huber_b = jnp.where(rows == k, huber_ref[k], huber_b)
            step_b = jnp.where(rows == k, step_ref[k], step_b)
        lanes = lax.broadcasted_iota(jnp.int32, (1, cap), 1)

        def column(a, t):
            return lax.rem(tc_ref[a, t] - first_row + margin + regions, regions)

        def fill(i, buf):
            a = i + base
            own_t = own_ref[a].T
            for t in range(tiles):
                buf[:, t * cap : (t + 1) * cap] = corr_block(own_t, hs_ref[column(a, t)])

        def use(i, buf):
            a = i + base
            weights = jnp.concatenate([hw_ref[column(a, t)] for t in range(tiles)], axis=1)
            cov = contract_lanes(weights, buf[...])
            current = hw_ref[a + margin]
            err = err_ref[pl.ds(a, 1), :]
            live = (lanes < sizes_ref[a]).astype(jnp.float32)
            diag = err * err + ridge_b
            thr = huber_b * err
            applied = cov * tile_scale + diag * current
            residual = (innov_ref[pl.ds(a, 1), :] * live - applied) * live
            factor = thr / jnp.maximum(jnp.abs(residual), thr)
            out_ref[i] = current + step_b * factor * residual / diag

        fill(0, buf0)

        def pair(i, carry):
            a = 2 * i
            use(a, buf0)
            fill(a + 1, buf1)
            use(a + 1, buf1)
            fill(jnp.minimum(a + 2, count - 1), buf0)
            return carry

        lax.fori_loop(0, count // 2, pair, 0)

    return update_kernel


def update(scal, count, tc, sizes, ridge, huber, step, vectors, margin, tile_scale, regions, first_sweep):
    own_sites = vectors[0]
    reg_dev, _, cap = own_sites.shape
    solves = ridge.shape[0]
    assert count % 2 == 0
    tiles = tc.shape[1]
    vmem = pl.BlockSpec(memory_space=pltpu.VMEM)
    smem = pl.BlockSpec(memory_space=pltpu.SMEM)
    halo_n = reg_dev + 2 * margin
    return pl.pallas_call(
        make_update_kernel(margin, tile_scale, regions, first_sweep),
        out_shape=jax.ShapeDtypeStruct((count, solves, cap), jnp.float32),
        in_specs=[smem] * 6 + [vmem] * len(vectors),
        out_specs=vmem,
        scratch_shapes=[
            pltpu.VMEM((cap, tiles * cap), jnp.float32),
            pltpu.VMEM((cap, tiles * cap), jnp.float32),
            pltpu.VMEM((halo_n, ROWS, cap), jnp.float32),
            pltpu.VMEM((halo_n, solves, cap), jnp.float32),
        ],
    )(scal, tc, sizes, ridge, huber, step, *vectors)


def make_grid_kernel(per_slab, reg_dev, n_wide, cap, regions):
    window = (2 * SLAB_REACH + 1) * per_slab

    def grid_kernel(
        me_ref, own_slabs_ref, list_ref, sites_ref, w_ref, gsites_ref, out_ref,
        sel_ref, slab_ref, buf0, buf1,
    ):
        n_own = out_ref.shape[0]
        gpr = list_ref.shape[0] // regions
        me = me_ref[0]
        total = jnp.int32(0)
        for j in range(n_own):
            slab = own_slabs_ref[j]
            start = (slab - SLAB_REACH) * per_slab + regions

            def scan(r, count):
                a = lax.rem(start + r, regions)
                owner = a // reg_dev
                slot = lax.rem(me - owner + n_wide, n_wide) * reg_dev + lax.rem(a, reg_dev)
                listed = list_ref[slot * gpr] == slab
                for e in range(1, gpr):
                    listed = jnp.logical_or(listed, list_ref[slot * gpr + e] == slab)
                sel_ref[count] = slot
                return count + listed.astype(jnp.int32)

            first_group = total // GROUP
            total = lax.fori_loop(0, window, scan, total)
            for e in range(GROUP):
                sel_ref[total + e] = regions
            total = (total + GROUP - 1) // GROUP * GROUP

            def mark(g, carry):
                slab_ref[g] = j
                return carry

            lax.fori_loop(first_group, total // GROUP, mark, 0)
        n_groups = total // GROUP
        for e in range(GROUP):
            sel_ref[total + e] = regions
        slab_ref[n_groups] = 0
        n_pairs = (n_groups + 1) // 2
        last = 2 * n_pairs - 1
        out_ref[...] = jnp.zeros(out_ref.shape, jnp.float32)

        def fill(g, buf):
            g_t = gsites_ref[slab_ref[g]].T
            for e in range(GROUP):
                slot = sel_ref[g * GROUP + e]
                buf[:, e * cap : (e + 1) * cap] = corr_block(g_t, sites_ref[slot])

        def use(g, buf):
            j = slab_ref[g]
            weights = jnp.concatenate(
                [w_ref[sel_ref[g * GROUP + e]] for e in range(GROUP)], axis=1
            )
            out_ref[j] = out_ref[j] + contract_lanes(weights, buf[...])

        fill(0, buf0)

        def pair(i, carry):
            g = 2 * i
            use(g, buf0)
            fill(g + 1, buf1)
            use(g + 1, buf1)
            fill(jnp.minimum(g + 2, last), buf0)
            return carry

        lax.fori_loop(0, n_pairs, pair, 0)
        out_ref[...] = out_ref[...] / cap

    return grid_kernel, window


def grid_stage(me, own_slabs, list_slots, site_slots, w_slots, gsites, reg_dev, n_wide, regions, slab_count):
    solves, cap = w_slots.shape[1:]
    n_own, _, gpts = gsites.shape
    kernel, window = make_grid_kernel(regions // slab_count, reg_dev, n_wide, cap, regions)
    vmem = pl.BlockSpec(memory_space=pltpu.VMEM)
    smem = pl.BlockSpec(memory_space=pltpu.SMEM)
    sel_len = n_own * (window + GROUP) + 2 * GROUP
    return pl.pallas_call(
        kernel,
        out_shape=jax.ShapeDtypeStruct((n_own, solves, gpts), jnp.float32),
        in_specs=[smem, smem, smem, vmem, vmem, vmem],
        out_specs=vmem,
        scratch_shapes=[
            pltpu.SMEM((sel_len,), jnp.int32),
            pltpu.SMEM((sel_len // GROUP + 2,), jnp.int32),
            pltpu.VMEM((gpts, GROUP * cap), jnp.float32),
            pltpu.VMEM((gpts, GROUP * cap), jnp.float32),
        ],
    )(me, own_slabs, list_slots, site_slots, w_slots, gsites)


def body(
    obs_latitude,
    obs_offset,
    innovation,
    obs_error,
    region_sizes,
    tile_columns,
    slab_list,
    slab_order,
    grid_latitude,
    grid_offset,
    ridge_weight,
    huber_cut,
    step_size,
):
    reg_dev, capacity = innovation.shape
    n_wide = lax.axis_size("wide")
    regions = reg_dev * n_wide
    margin = reg_dev // 2
    me = lax.axis_index("wide")
    first_row = me * reg_dev
    row_ids = first_row + jnp.arange(reg_dev, dtype=jnp.int32)
    obs_lon = FULL_TURN * (row_ids[:, None].astype(jnp.float32) + obs_offset) / regions
    obs_sites = unit_rows(obs_latitude, obs_lon)
    gpr = slab_list.shape[1]
    packed = jnp.concatenate(
        [
            obs_sites[:, :4, :],
            jnp.pad(slab_list.astype(jnp.float32), ((0, 0), (0, capacity - gpr)))[:, None, :],
        ],
        axis=1,
    )
    slots = gather_slots(packed, "wide")
    spare = jnp.zeros((ROWS, ROWS, capacity), jnp.float32)
    site_slots = jnp.concatenate(
        [jnp.pad(slots[:, :3, :], ((0, 0), (0, ROWS - 3), (0, 0))), spare], axis=0
    )
    list_slots = slots[:, 4, :gpr].astype(jnp.int32).reshape(-1)
    left_sites = site_slots[2 * reg_dev - margin : 2 * reg_dev]
    right_sites = site_slots[(n_wide - 1) * reg_dev : (n_wide - 1) * reg_dev + margin]
    live_mask = (jnp.arange(capacity, dtype=jnp.int32)[None, :] < region_sizes[:, None]).astype(
        jnp.float32
    )
    solves = ridge_weight.shape[0]
    diagonal = (obs_error * obs_error)[:, None, :] + ridge_weight[None, :, None]
    observed = (innovation * live_mask)[:, None, :]
    obs_weights = observed / diagonal
    tile_scale = 2.0 / (capacity * tile_columns.shape[1])
    n_slab = lax.axis_size("slab")
    assert n_slab == 2 and margin * n_slab == reg_dev
    sidx = lax.axis_index("slab")
    sub = reg_dev // n_slab
    blocks = n_wide * n_slab
    pairs = ("wide", "slab")
    other_pairs = [(b, b ^ 1) for b in range(blocks)]
    q1_pairs = [(b, (b - 2) % blocks) if b % 2 == 0 else (b, (b + 2) % blocks) for b in range(blocks)]
    q2_pairs = [(b, (b - 1) % blocks) if b % 2 == 0 else (b, (b + 1) % blocks) for b in range(blocks)]
    first = sidx == 0
    scal = jnp.stack([sidx * sub, first_row, first.astype(jnp.int32)]).astype(jnp.int32)
    common = (obs_sites, left_sites, right_sites, innovation, obs_error)

    def own_rows(mine):
        other = lax.ppermute(mine, pairs, other_pairs)
        return other, jnp.where(first, jnp.concatenate([mine, other]), jnp.concatenate([other, mine]))

    count = lax.axis_size("wide")
    w_tail = lax.slice_in_dim(obs_weights, reg_dev - margin, reg_dev, axis=0)
    w_head = lax.slice_in_dim(obs_weights, 0, margin, axis=0)
    w_left = lax.ppermute(w_tail, "wide", [(i, (i + 1) % count) for i in range(count)])
    w_right = lax.ppermute(w_head, "wide", [((i + 1) % count, i) for i in range(count)])
    vectors = common + (w_left, obs_weights, w_right)
    for sweep_index in range(ITERS):
        mine = update(
            scal, sub, tile_columns, region_sizes, ridge_weight, huber_cut, step_size, vectors,
            margin, tile_scale, regions, sweep_index == 0,
        )
        if sweep_index + 1 < ITERS:
            other = lax.ppermute(mine, pairs, other_pairs)
            q1 = lax.ppermute(mine, pairs, q1_pairs)
            q2 = lax.ppermute(mine, pairs, q2_pairs)
            vectors = common + (q1, q2, mine, other)
    other, obs_weights = own_rows(mine)
    w_slots = jnp.concatenate(
        [gather_slots(obs_weights, "wide"), jnp.zeros((ROWS, solves, capacity), jnp.float32)], axis=0
    )

    slab_count = slab_order.shape[0]
    n_own = slab_count // (n_wide * n_slab)
    pos0 = (me * n_slab + lax.axis_index("slab")) * n_own
    own_slabs = lax.dynamic_slice_in_dim(slab_order, pos0, n_own, 0)
    g_lat = grid_latitude[own_slabs]
    g_lon = FULL_TURN * (own_slabs[:, None].astype(jnp.float32) + grid_offset[own_slabs]) / slab_count
    gsites = unit_rows(g_lat, g_lon)
    grid_increment = grid_stage(
        me.astype(jnp.int32).reshape(1),
        own_slabs,
        list_slots,
        site_slots,
        w_slots,
        gsites,
        reg_dev,
        n_wide,
        regions,
        slab_count,
    )
    return (obs_weights, grid_increment)


def solution(mesh):
    in_specs = (
        P(("groups", "wide"), None),
        P(("groups", "wide"), None),
        P(("groups", "wide"), None),
        P(("groups", "wide"), None),
        P(("groups", "wide")),
        P(("groups", "wide"), None),
        P(("groups", "wide"), None),
        P("groups"),
        P(),
        P(),
        P("narrow"),
        P("narrow"),
        P("narrow"),
    )
    out_specs = (
        P(("groups", "wide"), "narrow", None),
        P(("groups", "wide", "slab"), "narrow", None),
    )
    return jax.shard_map(body, mesh=mesh, in_specs=in_specs, out_specs=out_specs, check_vma=False)
```

```python
import jax
import jax.numpy as jnp
from jax import lax
from jax.experimental import pallas as pl
from jax.experimental.pallas import tpu as pltpu
from jax.sharding import PartitionSpec as P

ITERS = 2
SLAB_REACH = 4

DECAY_RATE = 1.0 / 0.15
FULL_TURN = 6.283185307179586
HIGHEST = lax.Precision.HIGHEST
MATMUL_PRECISION = lax.Precision.HIGH
ROWS = 8
GROUP = 4


def with_halo(cells, axis, width):
    count = lax.axis_size(axis)
    head = lax.slice_in_dim(cells, 0, width, axis=0)
    tail = lax.slice_in_dim(cells, cells.shape[0] - width, cells.shape[0], axis=0)
    return jnp.concatenate(
        [
            lax.ppermute(tail, axis, [(i, (i + 1) % count) for i in range(count)]),
            cells,
            lax.ppermute(head, axis, [((i + 1) % count, i) for i in range(count)]),
        ],
        axis=0,
    )


def gather_slots(x, axis):
    count = lax.axis_size(axis)
    parts = [x]
    for s in range(1, count):
        parts.append(lax.ppermute(x, axis, [(i, (i + s) % count) for i in range(count)]))
    return jnp.concatenate(parts, axis=0)


def unit_rows(latitude, longitude):
    c = jnp.cos(latitude)
    zero = jnp.zeros_like(latitude)
    return jnp.stack(
        [c * jnp.cos(longitude), c * jnp.sin(longitude), jnp.sin(latitude)] + [zero] * (ROWS - 3),
        axis=-2,
    )


def corr_block(col_t, row):
    dx = col_t[:, 0:1] - row[0:1, :]
    dy = col_t[:, 1:2] - row[1:2, :]
    dz = col_t[:, 2:3] - row[2:3, :]
    d2 = dx * dx + dy * dy + dz * dz
    return jnp.exp(jnp.sqrt(d2) * (-DECAY_RATE))


def contract_lanes(w, c):
    return lax.dot_general(
        w, c, (((1,), (1,)), ((), ())), precision=MATMUL_PRECISION, preferred_element_type=jnp.float32
    )


def make_update_kernel(margin, tile_scale, regions, first_sweep):
    def update_kernel(scal_ref, tc_ref, sizes_ref, ridge_ref, huber_ref, step_ref, *refs):
        if first_sweep:
            own_ref, sl_ref, sr_ref, innov_ref, err_ref, wo_ref = refs[:6]
        else:
            own_ref, sl_ref, sr_ref, innov_ref, err_ref, q1_ref, q2_ref, mine_ref, other_ref = refs[:9]
        out_ref, buf0, buf1, hs_ref, hw_ref = refs[-5:]
        reg_dev, _, cap = own_ref.shape
        count, solves, _ = out_ref.shape
        tiles = tc_ref.shape[1]
        base = scal_ref[0]
        first_row = scal_ref[1]

        hs_ref[0:margin] = sl_ref[:, 0:ROWS, :]
        hs_ref[margin : margin + reg_dev] = own_ref[...]
        hs_ref[margin + reg_dev :] = sr_ref[:, 0:ROWS, :]
        if first_sweep:
            hw_ref[0:margin] = sl_ref[:, ROWS:, :]
            hw_ref[margin : margin + reg_dev] = wo_ref[...]
            hw_ref[margin + reg_dev :] = sr_ref[:, ROWS:, :]
        else:
            sel = scal_ref[2] == 1
            q1 = q1_ref[...]
            q2 = q2_ref[...]
            mine = mine_ref[...]
            other = other_ref[...]
            hw_ref[0:margin] = jnp.where(sel, q2, q1)
            hw_ref[margin : margin + count] = jnp.where(sel, mine, other)
            hw_ref[margin + count : margin + 2 * count] = jnp.where(sel, other, mine)
            hw_ref[margin + reg_dev :] = jnp.where(sel, q1, q2)

        rows = lax.broadcasted_iota(jnp.int32, (solves, cap), 0)
        ridge_b = jnp.zeros((solves, cap), jnp.float32)
        huber_b = jnp.zeros((solves, cap), jnp.float32)
        step_b = jnp.zeros((solves, cap), jnp.float32)
        for k in range(solves):
            ridge_b = jnp.where(rows == k, ridge_ref[k], ridge_b)
            huber_b = jnp.where(rows == k, huber_ref[k], huber_b)
            step_b = jnp.where(rows == k, step_ref[k], step_b)
        lanes = lax.broadcasted_iota(jnp.int32, (1, cap), 1)

        def column(a, t):
            return lax.rem(tc_ref[a, t] - first_row + margin + regions, regions)

        def fill(i, buf):
            a = i + base
            own_t = own_ref[a].T
            for t in range(tiles):
                buf[:, t * cap : (t + 1) * cap] = corr_block(own_t, hs_ref[column(a, t)])

        def use(i, buf):
            a = i + base
            weights = jnp.concatenate([hw_ref[column(a, t)] for t in range(tiles)], axis=1)
            cov = contract_lanes(weights, buf[...])
            current = hw_ref[a + margin]
            err = err_ref[pl.ds(a, 1), :]
            live = (lanes < sizes_ref[a]).astype(jnp.float32)
            diag = err * err + ridge_b
            thr = huber_b * err
            applied = cov * tile_scale + diag * current
            residual = (innov_ref[pl.ds(a, 1), :] * live - applied) * live
            factor = thr / jnp.maximum(jnp.abs(residual), thr)
            out_ref[i] = current + step_b * factor * residual / diag

        fill(0, buf0)

        def pair(i, carry):
            a = 2 * i
            use(a, buf0)
            fill(a + 1, buf1)
            use(a + 1, buf1)
            fill(jnp.minimum(a + 2, count - 1), buf0)
            return carry

        lax.fori_loop(0, count // 2, pair, 0)

    return update_kernel


def update(scal, count, tc, sizes, ridge, huber, step, vectors, margin, tile_scale, regions, first_sweep):
    own_sites = vectors[0]
    reg_dev, _, cap = own_sites.shape
    solves = ridge.shape[0]
    assert count % 2 == 0
    tiles = tc.shape[1]
    vmem = pl.BlockSpec(memory_space=pltpu.VMEM)
    smem = pl.BlockSpec(memory_space=pltpu.SMEM)
    halo_n = reg_dev + 2 * margin
    return pl.pallas_call(
        make_update_kernel(margin, tile_scale, regions, first_sweep),
        out_shape=jax.ShapeDtypeStruct((count, solves, cap), jnp.float32),
        in_specs=[smem] * 6 + [vmem] * len(vectors),
        out_specs=vmem,
        scratch_shapes=[
            pltpu.VMEM((cap, tiles * cap), jnp.float32),
            pltpu.VMEM((cap, tiles * cap), jnp.float32),
            pltpu.VMEM((halo_n, ROWS, cap), jnp.float32),
            pltpu.VMEM((halo_n, solves, cap), jnp.float32),
        ],
    )(scal, tc, sizes, ridge, huber, step, *vectors)


def make_grid_kernel(per_slab, reg_dev, n_wide, cap, regions):
    window = (2 * SLAB_REACH + 1) * per_slab

    def grid_kernel(
        me_ref, own_slabs_ref, list_ref, sites_ref, w_ref, gsites_ref, out_ref,
        sel_ref, slab_ref, buf0, buf1,
    ):
        n_own = out_ref.shape[0]
        gpr = list_ref.shape[0] // regions
        me = me_ref[0]
        total = jnp.int32(0)
        for j in range(n_own):
            slab = own_slabs_ref[j]
            start = (slab - SLAB_REACH) * per_slab + regions

            def scan(r, count):
                a = lax.rem(start + r, regions)
                owner = a // reg_dev
                slot = lax.rem(me - owner + n_wide, n_wide) * reg_dev + lax.rem(a, reg_dev)
                listed = list_ref[slot * gpr] == slab
                for e in range(1, gpr):
                    listed = jnp.logical_or(listed, list_ref[slot * gpr + e] == slab)
                sel_ref[count] = slot
                return count + listed.astype(jnp.int32)

            first_group = total // GROUP
            total = lax.fori_loop(0, window, scan, total)
            for e in range(GROUP):
                sel_ref[total + e] = regions
            total = (total + GROUP - 1) // GROUP * GROUP

            def mark(g, carry):
                slab_ref[g] = j
                return carry

            lax.fori_loop(first_group, total // GROUP, mark, 0)
        n_groups = total // GROUP
        for e in range(GROUP):
            sel_ref[total + e] = regions
        slab_ref[n_groups] = 0
        n_pairs = (n_groups + 1) // 2
        last = 2 * n_pairs - 1
        out_ref[...] = jnp.zeros(out_ref.shape, jnp.float32)

        def fill(g, buf):
            g_t = gsites_ref[slab_ref[g]].T
            for e in range(GROUP):
                slot = sel_ref[g * GROUP + e]
                buf[:, e * cap : (e + 1) * cap] = corr_block(g_t, sites_ref[slot])

        def use(g, buf):
            j = slab_ref[g]
            weights = jnp.concatenate(
                [w_ref[sel_ref[g * GROUP + e]] for e in range(GROUP)], axis=1
            )
            out_ref[j] = out_ref[j] + contract_lanes(weights, buf[...])

        fill(0, buf0)

        def pair(i, carry):
            g = 2 * i
            use(g, buf0)
            fill(g + 1, buf1)
            use(g + 1, buf1)
            fill(jnp.minimum(g + 2, last), buf0)
            return carry

        lax.fori_loop(0, n_pairs, pair, 0)
        out_ref[...] = out_ref[...] / cap

    return grid_kernel, window


def grid_stage(me, own_slabs, list_slots, site_slots, w_slots, gsites, reg_dev, n_wide, regions, slab_count):
    solves, cap = w_slots.shape[1:]
    n_own, _, gpts = gsites.shape
    kernel, window = make_grid_kernel(regions // slab_count, reg_dev, n_wide, cap, regions)
    vmem = pl.BlockSpec(memory_space=pltpu.VMEM)
    smem = pl.BlockSpec(memory_space=pltpu.SMEM)
    sel_len = n_own * (window + GROUP) + 2 * GROUP
    return pl.pallas_call(
        kernel,
        out_shape=jax.ShapeDtypeStruct((n_own, solves, gpts), jnp.float32),
        in_specs=[smem, smem, smem, vmem, vmem, vmem],
        out_specs=vmem,
        scratch_shapes=[
            pltpu.SMEM((sel_len,), jnp.int32),
            pltpu.SMEM((sel_len // GROUP + 2,), jnp.int32),
            pltpu.VMEM((gpts, GROUP * cap), jnp.float32),
            pltpu.VMEM((gpts, GROUP * cap), jnp.float32),
        ],
    )(me, own_slabs, list_slots, site_slots, w_slots, gsites)


def body(
    obs_latitude,
    obs_offset,
    innovation,
    obs_error,
    region_sizes,
    tile_columns,
    slab_list,
    slab_order,
    grid_latitude,
    grid_offset,
    ridge_weight,
    huber_cut,
    step_size,
):
    reg_dev, capacity = innovation.shape
    n_wide = lax.axis_size("wide")
    regions = reg_dev * n_wide
    margin = reg_dev // 2
    me = lax.axis_index("wide")
    first_row = me * reg_dev
    row_ids = first_row + jnp.arange(reg_dev, dtype=jnp.int32)
    obs_lon = FULL_TURN * (row_ids[:, None].astype(jnp.float32) + obs_offset) / regions
    obs_sites = unit_rows(obs_latitude, obs_lon)
    gpr = slab_list.shape[1]
    packed = jnp.concatenate(
        [
            obs_sites[:, :4, :],
            jnp.pad(slab_list.astype(jnp.float32), ((0, 0), (0, capacity - gpr)))[:, None, :],
        ],
        axis=1,
    )
    slots = gather_slots(packed, "wide")
    spare = jnp.zeros((ROWS, ROWS, capacity), jnp.float32)
    site_slots = jnp.concatenate(
        [jnp.pad(slots[:, :3, :], ((0, 0), (0, ROWS - 3), (0, 0))), spare], axis=0
    )
    list_slots = slots[:, 4, :gpr].astype(jnp.int32).reshape(-1)
    live_mask = (jnp.arange(capacity, dtype=jnp.int32)[None, :] < region_sizes[:, None]).astype(
        jnp.float32
    )
    solves = ridge_weight.shape[0]
    diagonal = (obs_error * obs_error)[:, None, :] + ridge_weight[None, :, None]
    observed = (innovation * live_mask)[:, None, :]
    obs_weights = observed / diagonal
    tile_scale = 2.0 / (capacity * tile_columns.shape[1])
    n_slab = lax.axis_size("slab")
    assert n_slab == 2 and margin * n_slab == reg_dev
    sidx = lax.axis_index("slab")
    sub = reg_dev // n_slab
    blocks = n_wide * n_slab
    pairs = ("wide", "slab")
    other_pairs = [(b, b ^ 1) for b in range(blocks)]
    q1_pairs = [(b, (b - 2) % blocks) if b % 2 == 0 else (b, (b + 2) % blocks) for b in range(blocks)]
    q2_pairs = [(b, (b - 1) % blocks) if b % 2 == 0 else (b, (b + 1) % blocks) for b in range(blocks)]
    first = sidx == 0
    scal = jnp.stack([sidx * sub, first_row, first.astype(jnp.int32)]).astype(jnp.int32)
    count = lax.axis_size("wide")
    both = jnp.concatenate([obs_sites, obs_weights], axis=1)
    tail = lax.slice_in_dim(both, reg_dev - margin, reg_dev, axis=0)
    head = lax.slice_in_dim(both, 0, margin, axis=0)
    left_pack = lax.ppermute(tail, "wide", [(i, (i + 1) % count) for i in range(count)])
    right_pack = lax.ppermute(head, "wide", [((i + 1) % count, i) for i in range(count)])
    common = (obs_sites, left_pack, right_pack, innovation, obs_error)

    def own_rows(mine):
        other = lax.ppermute(mine, pairs, other_pairs)
        return other, jnp.where(first, jnp.concatenate([mine, other]), jnp.concatenate([other, mine]))

    vectors = common + (obs_weights,)
    for sweep_index in range(ITERS):
        mine = update(
            scal, sub, tile_columns, region_sizes, ridge_weight, huber_cut, step_size, vectors,
            margin, tile_scale, regions, sweep_index == 0,
        )
        if sweep_index + 1 < ITERS:
            other = lax.ppermute(mine, pairs, other_pairs)
            q1 = lax.ppermute(mine, pairs, q1_pairs)
            q2 = lax.ppermute(mine, pairs, q2_pairs)
            vectors = common + (q1, q2, mine, other)
    other, obs_weights = own_rows(mine)
    w_slots = jnp.concatenate(
        [gather_slots(obs_weights, "wide"), jnp.zeros((ROWS, solves, capacity), jnp.float32)], axis=0
    )

    slab_count = slab_order.shape[0]
    n_own = slab_count // (n_wide * n_slab)
    pos0 = (me * n_slab + lax.axis_index("slab")) * n_own
    own_slabs = lax.dynamic_slice_in_dim(slab_order, pos0, n_own, 0)
    g_lat = grid_latitude[own_slabs]
    g_lon = FULL_TURN * (own_slabs[:, None].astype(jnp.float32) + grid_offset[own_slabs]) / slab_count
    gsites = unit_rows(g_lat, g_lon)
    grid_increment = grid_stage(
        me.astype(jnp.int32).reshape(1),
        own_slabs,
        list_slots,
        site_slots,
        w_slots,
        gsites,
        reg_dev,
        n_wide,
        regions,
        slab_count,
    )
    return (obs_weights, grid_increment)


def solution(mesh):
    in_specs = (
        P(("groups", "wide"), None),
        P(("groups", "wide"), None),
        P(("groups", "wide"), None),
        P(("groups", "wide"), None),
        P(("groups", "wide")),
        P(("groups", "wide"), None),
        P(("groups", "wide"), None),
        P("groups"),
        P(),
        P(),
        P("narrow"),
        P("narrow"),
        P("narrow"),
    )
    out_specs = (
        P(("groups", "wide"), "narrow", None),
        P(("groups", "wide", "slab"), "narrow", None),
    )
    return jax.shard_map(body, mesh=mesh, in_specs=in_specs, out_specs=out_specs, check_vma=False)
```

```python
import jax
import jax.numpy as jnp
from jax import lax
from jax.experimental import pallas as pl
from jax.experimental.pallas import tpu as pltpu
from jax.sharding import PartitionSpec as P

ITERS = 2
SLAB_REACH = 4

DECAY_RATE = 1.0 / 0.15
FULL_TURN = 6.283185307179586
HIGHEST = lax.Precision.HIGHEST
MATMUL_PRECISION = lax.Precision.HIGH
ROWS = 8
GROUP = 4


def with_halo(cells, axis, width):
    count = lax.axis_size(axis)
    head = lax.slice_in_dim(cells, 0, width, axis=0)
    tail = lax.slice_in_dim(cells, cells.shape[0] - width, cells.shape[0], axis=0)
    return jnp.concatenate(
        [
            lax.ppermute(tail, axis, [(i, (i + 1) % count) for i in range(count)]),
            cells,
            lax.ppermute(head, axis, [((i + 1) % count, i) for i in range(count)]),
        ],
        axis=0,
    )


def gather_slots(x, axis):
    count = lax.axis_size(axis)
    parts = [x]
    for s in range(1, count):
        parts.append(lax.ppermute(x, axis, [(i, (i + s) % count) for i in range(count)]))
    return jnp.concatenate(parts, axis=0)


def unit_rows(latitude, longitude):
    c = jnp.cos(latitude)
    zero = jnp.zeros_like(latitude)
    return jnp.stack(
        [c * jnp.cos(longitude), c * jnp.sin(longitude), jnp.sin(latitude)] + [zero] * (ROWS - 3),
        axis=-2,
    )


def corr_block(col_t, row):
    dx = col_t[:, 0:1] - row[0:1, :]
    dy = col_t[:, 1:2] - row[1:2, :]
    dz = col_t[:, 2:3] - row[2:3, :]
    d2 = dx * dx + dy * dy + dz * dz
    return jnp.exp(jnp.sqrt(d2) * (-DECAY_RATE))


def contract_lanes(w, c):
    return lax.dot_general(
        w, c, (((1,), (1,)), ((), ())), precision=MATMUL_PRECISION, preferred_element_type=jnp.float32
    )


def make_update_kernel(margin, tile_scale, regions, first_sweep):
    def update_kernel(scal_ref, tc_ref, sizes_ref, ridge_ref, huber_ref, step_ref, *refs):
        if first_sweep:
            own_ref, sl_ref, sr_ref, innov_ref, err_ref, wo_ref = refs[:6]
        else:
            own_ref, sl_ref, sr_ref, innov_ref, err_ref, q1_ref, q2_ref, mine_ref, other_ref = refs[:9]
        out_ref, buf0, buf1, hs_ref, hw_ref = refs[-5:]
        reg_dev, _, cap = own_ref.shape
        count, solves, _ = out_ref.shape
        tiles = tc_ref.shape[1]
        base = scal_ref[0]
        first_row = scal_ref[1]

        hs_ref[0:margin] = sl_ref[:, 0:ROWS, :]
        hs_ref[margin : margin + reg_dev] = own_ref[...]
        hs_ref[margin + reg_dev :] = sr_ref[:, 0:ROWS, :]
        if first_sweep:
            hw_ref[0:margin] = sl_ref[:, ROWS:, :]
            hw_ref[margin : margin + reg_dev] = wo_ref[...]
            hw_ref[margin + reg_dev :] = sr_ref[:, ROWS:, :]
        else:
            sel = scal_ref[2] == 1
            q1 = q1_ref[...]
            q2 = q2_ref[...]
            mine = mine_ref[...]
            other = other_ref[...]
            hw_ref[0:margin] = jnp.where(sel, q2, q1)
            hw_ref[margin : margin + count] = jnp.where(sel, mine, other)
            hw_ref[margin + count : margin + 2 * count] = jnp.where(sel, other, mine)
            hw_ref[margin + reg_dev :] = jnp.where(sel, q1, q2)

        rows = lax.broadcasted_iota(jnp.int32, (solves, cap), 0)
        ridge_b = jnp.zeros((solves, cap), jnp.float32)
        huber_b = jnp.zeros((solves, cap), jnp.float32)
        step_b = jnp.zeros((solves, cap), jnp.float32)
        for k in range(solves):
            ridge_b = jnp.where(rows == k, ridge_ref[k], ridge_b)
            huber_b = jnp.where(rows == k, huber_ref[k], huber_b)
            step_b = jnp.where(rows == k, step_ref[k], step_b)
        lanes = lax.broadcasted_iota(jnp.int32, (1, cap), 1)

        def column(a, t):
            return lax.rem(tc_ref[a, t] - first_row + margin + regions, regions)

        def fill(i, buf):
            a = i + base
            own_t = own_ref[a].T
            for t in range(tiles):
                buf[:, t * cap : (t + 1) * cap] = corr_block(own_t, hs_ref[column(a, t)])

        def use(i, buf):
            a = i + base
            weights = jnp.concatenate([hw_ref[column(a, t)] for t in range(tiles)], axis=1)
            cov = contract_lanes(weights, buf[...])
            current = hw_ref[a + margin]
            err = err_ref[pl.ds(a, 1), :]
            live = (lanes < sizes_ref[a]).astype(jnp.float32)
            diag = err * err + ridge_b
            thr = huber_b * err
            applied = cov * tile_scale + diag * current
            residual = (innov_ref[pl.ds(a, 1), :] * live - applied) * live
            factor = thr / jnp.maximum(jnp.abs(residual), thr)
            out_ref[i] = current + step_b * factor * residual / diag

        fill(0, buf0)

        def pair(i, carry):
            a = 2 * i
            use(a, buf0)
            fill(a + 1, buf1)
            use(a + 1, buf1)
            fill(jnp.minimum(a + 2, count - 1), buf0)
            return carry

        lax.fori_loop(0, count // 2, pair, 0)

    return update_kernel


def update(scal, count, tc, sizes, ridge, huber, step, vectors, margin, tile_scale, regions, first_sweep):
    own_sites = vectors[0]
    reg_dev, _, cap = own_sites.shape
    solves = ridge.shape[0]
    assert count % 2 == 0
    tiles = tc.shape[1]
    vmem = pl.BlockSpec(memory_space=pltpu.VMEM)
    smem = pl.BlockSpec(memory_space=pltpu.SMEM)
    halo_n = reg_dev + 2 * margin
    return pl.pallas_call(
        make_update_kernel(margin, tile_scale, regions, first_sweep),
        out_shape=jax.ShapeDtypeStruct((count, solves, cap), jnp.float32),
        in_specs=[smem] * 6 + [vmem] * len(vectors),
        out_specs=vmem,
        scratch_shapes=[
            pltpu.VMEM((cap, tiles * cap), jnp.float32),
            pltpu.VMEM((cap, tiles * cap), jnp.float32),
            pltpu.VMEM((halo_n, ROWS, cap), jnp.float32),
            pltpu.VMEM((halo_n, solves, cap), jnp.float32),
        ],
    )(scal, tc, sizes, ridge, huber, step, *vectors)


def make_grid_kernel(per_slab, reg_dev, n_wide, cap, regions, sub, blocks):
    window = (2 * SLAB_REACH + 1) * per_slab

    def grid_kernel(
        me_ref, own_slabs_ref, list_ref, sites_ref, w_ref, gsites_ref, out_ref,
        sel_ref, selw_ref, slab_ref, buf0, buf1,
    ):
        n_own = out_ref.shape[0]
        gpr = list_ref.shape[0] // regions
        me = me_ref[0]
        bid = me_ref[1]
        total = jnp.int32(0)
        for j in range(n_own):
            slab = own_slabs_ref[j]
            start = (slab - SLAB_REACH) * per_slab + regions

            def scan(r, count):
                a = lax.rem(start + r, regions)
                owner = a // reg_dev
                slot = lax.rem(me - owner + n_wide, n_wide) * reg_dev + lax.rem(a, reg_dev)
                listed = list_ref[slot * gpr] == slab
                for e in range(1, gpr):
                    listed = jnp.logical_or(listed, list_ref[slot * gpr + e] == slab)
                sel_ref[count] = slot
                selw_ref[count] = lax.rem(bid - a // sub + blocks, blocks) * sub + lax.rem(a, sub)
                return count + listed.astype(jnp.int32)

            first_group = total // GROUP
            total = lax.fori_loop(0, window, scan, total)
            for e in range(GROUP):
                sel_ref[total + e] = regions
                selw_ref[total + e] = regions
            total = (total + GROUP - 1) // GROUP * GROUP

            def mark(g, carry):
                slab_ref[g] = j
                return carry

            lax.fori_loop(first_group, total // GROUP, mark, 0)
        n_groups = total // GROUP
        for e in range(GROUP):
            sel_ref[total + e] = regions
            selw_ref[total + e] = regions
        slab_ref[n_groups] = 0
        n_pairs = (n_groups + 1) // 2
        last = 2 * n_pairs - 1
        out_ref[...] = jnp.zeros(out_ref.shape, jnp.float32)

        def fill(g, buf):
            g_t = gsites_ref[slab_ref[g]].T
            for e in range(GROUP):
                slot = sel_ref[g * GROUP + e]
                buf[:, e * cap : (e + 1) * cap] = corr_block(g_t, sites_ref[slot])

        def use(g, buf):
            j = slab_ref[g]
            weights = jnp.concatenate(
                [w_ref[selw_ref[g * GROUP + e]] for e in range(GROUP)], axis=1
            )
            out_ref[j] = out_ref[j] + contract_lanes(weights, buf[...])

        fill(0, buf0)

        def pair(i, carry):
            g = 2 * i
            use(g, buf0)
            fill(g + 1, buf1)
            use(g + 1, buf1)
            fill(jnp.minimum(g + 2, last), buf0)
            return carry

        lax.fori_loop(0, n_pairs, pair, 0)
        out_ref[...] = out_ref[...] / cap

    return grid_kernel, window


def grid_stage(me, own_slabs, list_slots, site_slots, w_slots, gsites, reg_dev, n_wide, regions, slab_count, sub, blocks):
    solves, cap = w_slots.shape[1:]
    n_own, _, gpts = gsites.shape
    kernel, window = make_grid_kernel(regions // slab_count, reg_dev, n_wide, cap, regions, sub, blocks)
    vmem = pl.BlockSpec(memory_space=pltpu.VMEM)
    smem = pl.BlockSpec(memory_space=pltpu.SMEM)
    sel_len = n_own * (window + GROUP) + 2 * GROUP
    return pl.pallas_call(
        kernel,
        out_shape=jax.ShapeDtypeStruct((n_own, solves, gpts), jnp.float32),
        in_specs=[smem, smem, smem, vmem, vmem, vmem],
        out_specs=vmem,
        scratch_shapes=[
            pltpu.SMEM((sel_len,), jnp.int32),
            pltpu.SMEM((sel_len,), jnp.int32),
            pltpu.SMEM((sel_len // GROUP + 2,), jnp.int32),
            pltpu.VMEM((gpts, GROUP * cap), jnp.float32),
            pltpu.VMEM((gpts, GROUP * cap), jnp.float32),
        ],
    )(me, own_slabs, list_slots, site_slots, w_slots, gsites)


def body(
    obs_latitude,
    obs_offset,
    innovation,
    obs_error,
    region_sizes,
    tile_columns,
    slab_list,
    slab_order,
    grid_latitude,
    grid_offset,
    ridge_weight,
    huber_cut,
    step_size,
):
    reg_dev, capacity = innovation.shape
    n_wide = lax.axis_size("wide")
    regions = reg_dev * n_wide
    margin = reg_dev // 2
    me = lax.axis_index("wide")
    first_row = me * reg_dev
    row_ids = first_row + jnp.arange(reg_dev, dtype=jnp.int32)
    obs_lon = FULL_TURN * (row_ids[:, None].astype(jnp.float32) + obs_offset) / regions
    obs_sites = unit_rows(obs_latitude, obs_lon)
    gpr = slab_list.shape[1]
    packed = jnp.concatenate(
        [
            obs_sites[:, :4, :],
            jnp.pad(slab_list.astype(jnp.float32), ((0, 0), (0, capacity - gpr)))[:, None, :],
        ],
        axis=1,
    )
    slots = gather_slots(packed, "wide")
    spare = jnp.zeros((ROWS, ROWS, capacity), jnp.float32)
    site_slots = jnp.concatenate(
        [jnp.pad(slots[:, :3, :], ((0, 0), (0, ROWS - 3), (0, 0))), spare], axis=0
    )
    list_slots = slots[:, 4, :gpr].astype(jnp.int32).reshape(-1)
    live_mask = (jnp.arange(capacity, dtype=jnp.int32)[None, :] < region_sizes[:, None]).astype(
        jnp.float32
    )
    solves = ridge_weight.shape[0]
    diagonal = (obs_error * obs_error)[:, None, :] + ridge_weight[None, :, None]
    observed = (innovation * live_mask)[:, None, :]
    obs_weights = observed / diagonal
    tile_scale = 2.0 / (capacity * tile_columns.shape[1])
    n_slab = lax.axis_size("slab")
    assert n_slab == 2 and margin * n_slab == reg_dev
    sidx = lax.axis_index("slab")
    sub = reg_dev // n_slab
    blocks = n_wide * n_slab
    pairs = ("wide", "slab")
    other_pairs = [(b, b ^ 1) for b in range(blocks)]
    q1_pairs = [(b, (b - 2) % blocks) if b % 2 == 0 else (b, (b + 2) % blocks) for b in range(blocks)]
    q2_pairs = [(b, (b - 1) % blocks) if b % 2 == 0 else (b, (b + 1) % blocks) for b in range(blocks)]
    first = sidx == 0
    scal = jnp.stack([sidx * sub, first_row, first.astype(jnp.int32)]).astype(jnp.int32)
    count = lax.axis_size("wide")
    both = jnp.concatenate([obs_sites, obs_weights], axis=1)
    tail = lax.slice_in_dim(both, reg_dev - margin, reg_dev, axis=0)
    head = lax.slice_in_dim(both, 0, margin, axis=0)
    left_pack = lax.ppermute(tail, "wide", [(i, (i + 1) % count) for i in range(count)])
    right_pack = lax.ppermute(head, "wide", [((i + 1) % count, i) for i in range(count)])
    common = (obs_sites, left_pack, right_pack, innovation, obs_error)

    def own_rows(mine):
        other = lax.ppermute(mine, pairs, other_pairs)
        return other, jnp.where(first, jnp.concatenate([mine, other]), jnp.concatenate([other, mine]))

    vectors = common + (obs_weights,)
    for sweep_index in range(ITERS):
        mine = update(
            scal, sub, tile_columns, region_sizes, ridge_weight, huber_cut, step_size, vectors,
            margin, tile_scale, regions, sweep_index == 0,
        )
        if sweep_index + 1 < ITERS:
            other = lax.ppermute(mine, pairs, other_pairs)
            q1 = lax.ppermute(mine, pairs, q1_pairs)
            q2 = lax.ppermute(mine, pairs, q2_pairs)
            vectors = common + (q1, q2, mine, other)
    w_gathered = gather_slots(mine, pairs)
    obs_weights = jnp.where(
        first,
        jnp.concatenate([w_gathered[:sub], w_gathered[(blocks - 1) * sub :]]),
        jnp.concatenate([w_gathered[sub : 2 * sub], w_gathered[:sub]]),
    )
    w_slots = jnp.concatenate(
        [w_gathered, jnp.zeros((ROWS, solves, capacity), jnp.float32)], axis=0
    )

    slab_count = slab_order.shape[0]
    n_own = slab_count // (n_wide * n_slab)
    pos0 = (me * n_slab + lax.axis_index("slab")) * n_own
    own_slabs = lax.dynamic_slice_in_dim(slab_order, pos0, n_own, 0)
    g_lat = grid_latitude[own_slabs]
    g_lon = FULL_TURN * (own_slabs[:, None].astype(jnp.float32) + grid_offset[own_slabs]) / slab_count
    gsites = unit_rows(g_lat, g_lon)
    grid_increment = grid_stage(
        jnp.stack([me, me * n_slab + sidx]).astype(jnp.int32),
        own_slabs,
        list_slots,
        site_slots,
        w_slots,
        gsites,
        reg_dev,
        n_wide,
        regions,
        slab_count,
        sub,
        blocks,
    )
    return (obs_weights, grid_increment)


def solution(mesh):
    in_specs = (
        P(("groups", "wide"), None),
        P(("groups", "wide"), None),
        P(("groups", "wide"), None),
        P(("groups", "wide"), None),
        P(("groups", "wide")),
        P(("groups", "wide"), None),
        P(("groups", "wide"), None),
        P("groups"),
        P(),
        P(),
        P("narrow"),
        P("narrow"),
        P("narrow"),
    )
    out_specs = (
        P(("groups", "wide"), "narrow", None),
        P(("groups", "wide", "slab"), "narrow", None),
    )
    return jax.shard_map(body, mesh=mesh, in_specs=in_specs, out_specs=out_specs, check_vma=False)
```

```python
import jax
import jax.numpy as jnp
from jax import lax
from jax.experimental import pallas as pl
from jax.experimental.pallas import tpu as pltpu
from jax.sharding import PartitionSpec as P

ITERS = 2
SLAB_REACH = 4

DECAY_RATE = 1.0 / 0.15
FULL_TURN = 6.283185307179586
HIGHEST = lax.Precision.HIGHEST
MATMUL_PRECISION = lax.Precision.HIGH
ROWS = 8
GROUP = 4


def with_halo(cells, axis, width):
    count = lax.axis_size(axis)
    head = lax.slice_in_dim(cells, 0, width, axis=0)
    tail = lax.slice_in_dim(cells, cells.shape[0] - width, cells.shape[0], axis=0)
    return jnp.concatenate(
        [
            lax.ppermute(tail, axis, [(i, (i + 1) % count) for i in range(count)]),
            cells,
            lax.ppermute(head, axis, [((i + 1) % count, i) for i in range(count)]),
        ],
        axis=0,
    )


def gather_slots(x, axis):
    count = lax.axis_size(axis)
    parts = [x]
    for s in range(1, count):
        parts.append(lax.ppermute(x, axis, [(i, (i + s) % count) for i in range(count)]))
    return jnp.concatenate(parts, axis=0)


def unit_rows(latitude, longitude):
    c = jnp.cos(latitude)
    zero = jnp.zeros_like(latitude)
    return jnp.stack(
        [c * jnp.cos(longitude), c * jnp.sin(longitude), jnp.sin(latitude)] + [zero] * (ROWS - 3),
        axis=-2,
    )


def corr_block(col_t, row):
    dx = col_t[:, 0:1] - row[0:1, :]
    dy = col_t[:, 1:2] - row[1:2, :]
    dz = col_t[:, 2:3] - row[2:3, :]
    d2 = dx * dx + dy * dy + dz * dz
    return jnp.exp(jnp.sqrt(d2) * (-DECAY_RATE))


def contract_lanes(w, c):
    return lax.dot_general(
        w, c, (((1,), (1,)), ((), ())), precision=MATMUL_PRECISION, preferred_element_type=jnp.float32
    )


def make_update_kernel(margin, tile_scale, regions, first_sweep):
    def update_kernel(scal_ref, tc_ref, sizes_ref, ridge_ref, huber_ref, step_ref, *refs):
        if first_sweep:
            own_ref, sl_ref, sr_ref, innov_ref, err_ref, wo_ref = refs[:6]
        else:
            own_ref, sl_ref, sr_ref, innov_ref, err_ref, q1_ref, q2_ref, mine_ref, other_ref = refs[:9]
        out_ref, buf0, buf1, hs_ref, hw_ref = refs[-5:]
        reg_dev, _, cap = own_ref.shape
        count, solves, _ = out_ref.shape
        tiles = tc_ref.shape[1]
        base = scal_ref[0]
        first_row = scal_ref[1]

        hs_ref[0:margin] = sl_ref[:, 0:ROWS, :]
        hs_ref[margin : margin + reg_dev] = own_ref[...]
        hs_ref[margin + reg_dev :] = sr_ref[:, 0:ROWS, :]
        if first_sweep:
            hw_ref[0:margin] = sl_ref[:, ROWS:, :]
            hw_ref[margin : margin + reg_dev] = wo_ref[...]
            hw_ref[margin + reg_dev :] = sr_ref[:, ROWS:, :]
        else:
            sel = scal_ref[2] == 1
            q1 = q1_ref[...]
            q2 = q2_ref[...]
            mine = mine_ref[...]
            other = other_ref[...]
            hw_ref[0:margin] = jnp.where(sel, q2, q1)
            hw_ref[margin : margin + count] = jnp.where(sel, mine, other)
            hw_ref[margin + count : margin + 2 * count] = jnp.where(sel, other, mine)
            hw_ref[margin + reg_dev :] = jnp.where(sel, q1, q2)

        rows = lax.broadcasted_iota(jnp.int32, (solves, cap), 0)
        ridge_b = jnp.zeros((solves, cap), jnp.float32)
        huber_b = jnp.zeros((solves, cap), jnp.float32)
        step_b = jnp.zeros((solves, cap), jnp.float32)
        for k in range(solves):
            ridge_b = jnp.where(rows == k, ridge_ref[k], ridge_b)
            huber_b = jnp.where(rows == k, huber_ref[k], huber_b)
            step_b = jnp.where(rows == k, step_ref[k], step_b)
        lanes = lax.broadcasted_iota(jnp.int32, (1, cap), 1)

        def column(a, t):
            return lax.rem(tc_ref[a, t] - first_row + margin + regions, regions)

        def fill(i, buf):
            a = i + base
            own_t = own_ref[a].T
            for t in range(tiles):
                buf[:, t * cap : (t + 1) * cap] = corr_block(own_t, hs_ref[column(a, t)])

        def use(i, buf):
            a = i + base
            weights = jnp.concatenate([hw_ref[column(a, t)] for t in range(tiles)], axis=1)
            cov = contract_lanes(weights, buf[...])
            current = hw_ref[a + margin]
            err = err_ref[pl.ds(a, 1), :]
            live = (lanes < sizes_ref[a]).astype(jnp.float32)
            diag = err * err + ridge_b
            thr = huber_b * err
            applied = cov * tile_scale + diag * current
            residual = (innov_ref[pl.ds(a, 1), :] * live - applied) * live
            factor = thr / jnp.maximum(jnp.abs(residual), thr)
            out_ref[i] = current + step_b * factor * residual / diag

        fill(0, buf0)

        def pair(i, carry):
            a = 2 * i
            use(a, buf0)
            fill(a + 1, buf1)
            use(a + 1, buf1)
            fill(jnp.minimum(a + 2, count - 1), buf0)
            return carry

        lax.fori_loop(0, count // 2, pair, 0)

    return update_kernel


def update(scal, count, tc, sizes, ridge, huber, step, vectors, margin, tile_scale, regions, first_sweep):
    own_sites = vectors[0]
    reg_dev, _, cap = own_sites.shape
    solves = ridge.shape[0]
    assert count % 2 == 0
    tiles = tc.shape[1]
    vmem = pl.BlockSpec(memory_space=pltpu.VMEM)
    smem = pl.BlockSpec(memory_space=pltpu.SMEM)
    halo_n = reg_dev + 2 * margin
    return pl.pallas_call(
        make_update_kernel(margin, tile_scale, regions, first_sweep),
        out_shape=jax.ShapeDtypeStruct((count, solves, cap), jnp.float32),
        in_specs=[smem] * 6 + [vmem] * len(vectors),
        out_specs=vmem,
        scratch_shapes=[
            pltpu.VMEM((cap, tiles * cap), jnp.float32),
            pltpu.VMEM((cap, tiles * cap), jnp.float32),
            pltpu.VMEM((halo_n, ROWS, cap), jnp.float32),
            pltpu.VMEM((halo_n, solves, cap), jnp.float32),
        ],
    )(scal, tc, sizes, ridge, huber, step, *vectors)


def make_grid_kernel(per_slab, reg_dev, n_wide, cap, regions, local):
    window = (2 * SLAB_REACH + 1) * per_slab

    def grid_kernel(me_ref, own_slabs_ref, list_ref, sites_ref, w_ref, gsites_ref, *refs):
        if local:
            out_ref, sel_ref, slab_ref, buf0, buf1 = refs
        else:
            init_ref, out_ref, sel_ref, slab_ref, buf0, buf1 = refs
        n_own = out_ref.shape[0]
        gpr = list_ref.shape[0] // regions
        me = me_ref[0]
        total = jnp.int32(0)
        for j in range(n_own):
            slab = own_slabs_ref[j]
            start = (slab - SLAB_REACH) * per_slab + regions

            def scan(r, count):
                a = lax.rem(start + r, regions)
                owner = a // reg_dev
                slot = lax.rem(me - owner + n_wide, n_wide) * reg_dev + lax.rem(a, reg_dev)
                listed = list_ref[slot * gpr] == slab
                for e in range(1, gpr):
                    listed = jnp.logical_or(listed, list_ref[slot * gpr + e] == slab)
                if local:
                    listed = jnp.logical_and(listed, owner == me)
                else:
                    listed = jnp.logical_and(listed, owner != me)
                sel_ref[count] = slot
                return count + listed.astype(jnp.int32)

            first_group = total // GROUP
            total = lax.fori_loop(0, window, scan, total)
            for e in range(GROUP):
                sel_ref[total + e] = regions
            total = (total + GROUP - 1) // GROUP * GROUP

            def mark(g, carry):
                slab_ref[g] = j
                return carry

            lax.fori_loop(first_group, total // GROUP, mark, 0)
        n_groups = total // GROUP
        for e in range(GROUP):
            sel_ref[total + e] = regions
        slab_ref[n_groups] = 0
        n_pairs = (n_groups + 1) // 2
        last = 2 * n_pairs - 1
        if local:
            out_ref[...] = jnp.zeros(out_ref.shape, jnp.float32)
        else:
            out_ref[...] = init_ref[...]

        def weight_row(slot):
            if local:
                return w_ref[jnp.where(slot == regions, reg_dev, slot)]
            return w_ref[slot]

        def fill(g, buf):
            g_t = gsites_ref[slab_ref[g]].T
            for e in range(GROUP):
                slot = sel_ref[g * GROUP + e]
                buf[:, e * cap : (e + 1) * cap] = corr_block(g_t, sites_ref[slot])

        def use(g, buf):
            j = slab_ref[g]
            weights = jnp.concatenate(
                [weight_row(sel_ref[g * GROUP + e]) for e in range(GROUP)], axis=1
            )
            out_ref[j] = out_ref[j] + contract_lanes(weights, buf[...])

        fill(0, buf0)

        def pair(i, carry):
            g = 2 * i
            use(g, buf0)
            fill(g + 1, buf1)
            use(g + 1, buf1)
            fill(jnp.minimum(g + 2, last), buf0)
            return carry

        lax.fori_loop(0, n_pairs, pair, 0)
        if not local:
            out_ref[...] = out_ref[...] / cap

    return grid_kernel, window


def grid_stage(me, own_slabs, list_slots, site_slots, w_slots, gsites, reg_dev, n_wide, regions, slab_count, init=None):
    solves, cap = w_slots.shape[1:]
    n_own, _, gpts = gsites.shape
    local = init is None
    kernel, window = make_grid_kernel(regions // slab_count, reg_dev, n_wide, cap, regions, local)
    vmem = pl.BlockSpec(memory_space=pltpu.VMEM)
    smem = pl.BlockSpec(memory_space=pltpu.SMEM)
    sel_len = n_own * (window + GROUP) + 2 * GROUP
    extra = () if local else (init,)
    return pl.pallas_call(
        kernel,
        out_shape=jax.ShapeDtypeStruct((n_own, solves, gpts), jnp.float32),
        in_specs=[smem, smem, smem, vmem, vmem, vmem] + [vmem] * len(extra),
        out_specs=vmem,
        scratch_shapes=[
            pltpu.SMEM((sel_len,), jnp.int32),
            pltpu.SMEM((sel_len // GROUP + 2,), jnp.int32),
            pltpu.VMEM((gpts, GROUP * cap), jnp.float32),
            pltpu.VMEM((gpts, GROUP * cap), jnp.float32),
        ],
    )(me, own_slabs, list_slots, site_slots, w_slots, gsites, *extra)


def body(
    obs_latitude,
    obs_offset,
    innovation,
    obs_error,
    region_sizes,
    tile_columns,
    slab_list,
    slab_order,
    grid_latitude,
    grid_offset,
    ridge_weight,
    huber_cut,
    step_size,
):
    reg_dev, capacity = innovation.shape
    n_wide = lax.axis_size("wide")
    regions = reg_dev * n_wide
    margin = reg_dev // 2
    me = lax.axis_index("wide")
    first_row = me * reg_dev
    row_ids = first_row + jnp.arange(reg_dev, dtype=jnp.int32)
    obs_lon = FULL_TURN * (row_ids[:, None].astype(jnp.float32) + obs_offset) / regions
    obs_sites = unit_rows(obs_latitude, obs_lon)
    gpr = slab_list.shape[1]
    packed = jnp.concatenate(
        [
            obs_sites[:, :4, :],
            jnp.pad(slab_list.astype(jnp.float32), ((0, 0), (0, capacity - gpr)))[:, None, :],
        ],
        axis=1,
    )
    slots = gather_slots(packed, "wide")
    spare = jnp.zeros((ROWS, ROWS, capacity), jnp.float32)
    site_slots = jnp.concatenate(
        [jnp.pad(slots[:, :3, :], ((0, 0), (0, ROWS - 3), (0, 0))), spare], axis=0
    )
    list_slots = slots[:, 4, :gpr].astype(jnp.int32).reshape(-1)
    live_mask = (jnp.arange(capacity, dtype=jnp.int32)[None, :] < region_sizes[:, None]).astype(
        jnp.float32
    )
    solves = ridge_weight.shape[0]
    diagonal = (obs_error * obs_error)[:, None, :] + ridge_weight[None, :, None]
    observed = (innovation * live_mask)[:, None, :]
    obs_weights = observed / diagonal
    tile_scale = 2.0 / (capacity * tile_columns.shape[1])
    n_slab = lax.axis_size("slab")
    assert n_slab == 2 and margin * n_slab == reg_dev
    sidx = lax.axis_index("slab")
    sub = reg_dev // n_slab
    blocks = n_wide * n_slab
    pairs = ("wide", "slab")
    other_pairs = [(b, b ^ 1) for b in range(blocks)]
    q1_pairs = [(b, (b - 2) % blocks) if b % 2 == 0 else (b, (b + 2) % blocks) for b in range(blocks)]
    q2_pairs = [(b, (b - 1) % blocks) if b % 2 == 0 else (b, (b + 1) % blocks) for b in range(blocks)]
    first = sidx == 0
    scal = jnp.stack([sidx * sub, first_row, first.astype(jnp.int32)]).astype(jnp.int32)
    count = lax.axis_size("wide")
    both = jnp.concatenate([obs_sites, obs_weights], axis=1)
    tail = lax.slice_in_dim(both, reg_dev - margin, reg_dev, axis=0)
    head = lax.slice_in_dim(both, 0, margin, axis=0)
    left_pack = lax.ppermute(tail, "wide", [(i, (i + 1) % count) for i in range(count)])
    right_pack = lax.ppermute(head, "wide", [((i + 1) % count, i) for i in range(count)])
    common = (obs_sites, left_pack, right_pack, innovation, obs_error)

    def own_rows(mine):
        other = lax.ppermute(mine, pairs, other_pairs)
        return other, jnp.where(first, jnp.concatenate([mine, other]), jnp.concatenate([other, mine]))

    vectors = common + (obs_weights,)
    for sweep_index in range(ITERS):
        mine = update(
            scal, sub, tile_columns, region_sizes, ridge_weight, huber_cut, step_size, vectors,
            margin, tile_scale, regions, sweep_index == 0,
        )
        if sweep_index + 1 < ITERS:
            other = lax.ppermute(mine, pairs, other_pairs)
            q1 = lax.ppermute(mine, pairs, q1_pairs)
            q2 = lax.ppermute(mine, pairs, q2_pairs)
            vectors = common + (q1, q2, mine, other)
    other, obs_weights = own_rows(mine)
    w_slots = jnp.concatenate(
        [gather_slots(obs_weights, "wide"), jnp.zeros((ROWS, solves, capacity), jnp.float32)], axis=0
    )

    slab_count = slab_order.shape[0]
    n_own = slab_count // (n_wide * n_slab)
    pos0 = (me * n_slab + lax.axis_index("slab")) * n_own
    own_slabs = lax.dynamic_slice_in_dim(slab_order, pos0, n_own, 0)
    g_lat = grid_latitude[own_slabs]
    g_lon = FULL_TURN * (own_slabs[:, None].astype(jnp.float32) + grid_offset[own_slabs]) / slab_count
    gsites = unit_rows(g_lat, g_lon)
    me32 = me.astype(jnp.int32).reshape(1)
    spare_w = jnp.zeros((ROWS, solves, capacity), jnp.float32)
    near = grid_stage(
        me32, own_slabs, list_slots, site_slots, jnp.concatenate([obs_weights, spare_w]),
        gsites, reg_dev, n_wide, regions, slab_count,
    )
    grid_increment = grid_stage(
        me32, own_slabs, list_slots, site_slots, w_slots,
        gsites, reg_dev, n_wide, regions, slab_count, near,
    )
    return (obs_weights, grid_increment)


def solution(mesh):
    in_specs = (
        P(("groups", "wide"), None),
        P(("groups", "wide"), None),
        P(("groups", "wide"), None),
        P(("groups", "wide"), None),
        P(("groups", "wide")),
        P(("groups", "wide"), None),
        P(("groups", "wide"), None),
        P("groups"),
        P(),
        P(),
        P("narrow"),
        P("narrow"),
        P("narrow"),
    )
    out_specs = (
        P(("groups", "wide"), "narrow", None),
        P(("groups", "wide", "slab"), "narrow", None),
    )
    return jax.shard_map(body, mesh=mesh, in_specs=in_specs, out_specs=out_specs, check_vma=False)
```

```python
import jax
import jax.numpy as jnp
from jax import lax
from jax.experimental import pallas as pl
from jax.experimental.pallas import tpu as pltpu
from jax.sharding import PartitionSpec as P

ITERS = 2
SLAB_REACH = 4

DECAY_RATE = 1.0 / 0.15
FULL_TURN = 6.283185307179586
HIGHEST = lax.Precision.HIGHEST
MATMUL_PRECISION = lax.Precision.HIGH
ROWS = 8
GROUP = 4


def with_halo(cells, axis, width):
    count = lax.axis_size(axis)
    head = lax.slice_in_dim(cells, 0, width, axis=0)
    tail = lax.slice_in_dim(cells, cells.shape[0] - width, cells.shape[0], axis=0)
    return jnp.concatenate(
        [
            lax.ppermute(tail, axis, [(i, (i + 1) % count) for i in range(count)]),
            cells,
            lax.ppermute(head, axis, [((i + 1) % count, i) for i in range(count)]),
        ],
        axis=0,
    )


def gather_slots(x, axis):
    count = lax.axis_size(axis)
    parts = [x]
    for s in range(1, count):
        parts.append(lax.ppermute(x, axis, [(i, (i + s) % count) for i in range(count)]))
    return jnp.concatenate(parts, axis=0)


def unit_rows(latitude, longitude):
    c = jnp.cos(latitude)
    zero = jnp.zeros_like(latitude)
    return jnp.stack(
        [c * jnp.cos(longitude), c * jnp.sin(longitude), jnp.sin(latitude)] + [zero] * (ROWS - 3),
        axis=-2,
    )


def corr_block(col_t, row):
    dx = col_t[:, 0:1] - row[0:1, :]
    dy = col_t[:, 1:2] - row[1:2, :]
    dz = col_t[:, 2:3] - row[2:3, :]
    d2 = dx * dx + dy * dy + dz * dz
    return jnp.exp(jnp.sqrt(d2) * (-DECAY_RATE))


def contract_lanes(w, c):
    return lax.dot_general(
        w, c, (((1,), (1,)), ((), ())), precision=MATMUL_PRECISION, preferred_element_type=jnp.float32
    )


def make_update_kernel(margin, tile_scale, regions, first_sweep):
    def update_kernel(scal_ref, tc_ref, sizes_ref, ridge_ref, huber_ref, step_ref, *refs):
        if first_sweep:
            own_ref, sl_ref, sr_ref, innov_ref, err_ref, wo_ref = refs[:6]
        else:
            own_ref, sl_ref, sr_ref, innov_ref, err_ref, q1_ref, q2_ref, mine_ref, other_ref = refs[:9]
        if first_sweep:
            out_ref, cache_ref, hs_ref, hw_ref = refs[-4:]
        else:
            cache_ref, out_ref, hs_ref, hw_ref = refs[-4:]
        reg_dev, _, cap = own_ref.shape
        count, solves, _ = out_ref.shape
        tiles = tc_ref.shape[1]
        base = scal_ref[0]
        first_row = scal_ref[1]

        hs_ref[0:margin] = sl_ref[:, 0:ROWS, :]
        hs_ref[margin : margin + reg_dev] = own_ref[...]
        hs_ref[margin + reg_dev :] = sr_ref[:, 0:ROWS, :]
        if first_sweep:
            hw_ref[0:margin] = sl_ref[:, ROWS:, :]
            hw_ref[margin : margin + reg_dev] = wo_ref[...]
            hw_ref[margin + reg_dev :] = sr_ref[:, ROWS:, :]
        else:
            sel = scal_ref[2] == 1
            q1 = q1_ref[...]
            q2 = q2_ref[...]
            mine = mine_ref[...]
            other = other_ref[...]
            hw_ref[0:margin] = jnp.where(sel, q2, q1)
            hw_ref[margin : margin + count] = jnp.where(sel, mine, other)
            hw_ref[margin + count : margin + 2 * count] = jnp.where(sel, other, mine)
            hw_ref[margin + reg_dev :] = jnp.where(sel, q1, q2)

        rows = lax.broadcasted_iota(jnp.int32, (solves, cap), 0)
        ridge_b = jnp.zeros((solves, cap), jnp.float32)
        huber_b = jnp.zeros((solves, cap), jnp.float32)
        step_b = jnp.zeros((solves, cap), jnp.float32)
        for k in range(solves):
            ridge_b = jnp.where(rows == k, ridge_ref[k], ridge_b)
            huber_b = jnp.where(rows == k, huber_ref[k], huber_b)
            step_b = jnp.where(rows == k, step_ref[k], step_b)
        lanes = lax.broadcasted_iota(jnp.int32, (1, cap), 1)

        def column(a, t):
            return lax.rem(tc_ref[a, t] - first_row + margin + regions, regions)

        def fill(i):
            a = i + base
            own_t = own_ref[a].T
            for t in range(tiles):
                cache_ref[i, :, t * cap : (t + 1) * cap] = corr_block(own_t, hs_ref[column(a, t)])

        def use(i):
            a = i + base
            weights = jnp.concatenate([hw_ref[column(a, t)] for t in range(tiles)], axis=1)
            cov = contract_lanes(weights, cache_ref[i])
            current = hw_ref[a + margin]
            err = err_ref[pl.ds(a, 1), :]
            live = (lanes < sizes_ref[a]).astype(jnp.float32)
            diag = err * err + ridge_b
            thr = huber_b * err
            applied = cov * tile_scale + diag * current
            residual = (innov_ref[pl.ds(a, 1), :] * live - applied) * live
            factor = thr / jnp.maximum(jnp.abs(residual), thr)
            out_ref[i] = current + step_b * factor * residual / diag

        if first_sweep:
            fill(0)

            def pair(i, carry):
                a = 2 * i
                use(a)
                fill(a + 1)
                use(a + 1)
                fill(jnp.minimum(a + 2, count - 1))
                return carry

            lax.fori_loop(0, count // 2, pair, 0)
        else:
            def one(i, carry):
                use(i)
                return carry

            lax.fori_loop(0, count, one, 0)

    return update_kernel


def update(scal, count, tc, sizes, ridge, huber, step, vectors, margin, tile_scale, regions, first_sweep, cache=None):
    own_sites = vectors[0]
    reg_dev, _, cap = own_sites.shape
    solves = ridge.shape[0]
    assert count % 2 == 0
    tiles = tc.shape[1]
    vmem = pl.BlockSpec(memory_space=pltpu.VMEM)
    smem = pl.BlockSpec(memory_space=pltpu.SMEM)
    halo_n = reg_dev + 2 * margin
    new_w = jax.ShapeDtypeStruct((count, solves, cap), jnp.float32)
    if first_sweep:
        out_shape = (new_w, jax.ShapeDtypeStruct((count, cap, tiles * cap), jnp.float32))
        out_specs = (vmem, vmem)
    else:
        vectors = tuple(vectors) + (cache,)
        out_shape = new_w
        out_specs = vmem
    return pl.pallas_call(
        make_update_kernel(margin, tile_scale, regions, first_sweep),
        out_shape=out_shape,
        in_specs=[smem] * 6 + [vmem] * len(vectors),
        out_specs=out_specs,
        scratch_shapes=[
            pltpu.VMEM((halo_n, ROWS, cap), jnp.float32),
            pltpu.VMEM((halo_n, solves, cap), jnp.float32),
        ],
    )(scal, tc, sizes, ridge, huber, step, *vectors)


def make_grid_kernel(per_slab, reg_dev, n_wide, cap, regions):
    window = (2 * SLAB_REACH + 1) * per_slab

    def grid_kernel(
        me_ref, own_slabs_ref, list_ref, sites_ref, w_ref, gsites_ref, out_ref,
        sel_ref, slab_ref, buf0, buf1,
    ):
        n_own = out_ref.shape[0]
        gpr = list_ref.shape[0] // regions
        me = me_ref[0]
        total = jnp.int32(0)
        for j in range(n_own):
            slab = own_slabs_ref[j]
            start = (slab - SLAB_REACH) * per_slab + regions

            def scan(r, count):
                a = lax.rem(start + r, regions)
                owner = a // reg_dev
                slot = lax.rem(me - owner + n_wide, n_wide) * reg_dev + lax.rem(a, reg_dev)
                listed = list_ref[slot * gpr] == slab
                for e in range(1, gpr):
                    listed = jnp.logical_or(listed, list_ref[slot * gpr + e] == slab)
                sel_ref[count] = slot
                return count + listed.astype(jnp.int32)

            first_group = total // GROUP
            total = lax.fori_loop(0, window, scan, total)
            for e in range(GROUP):
                sel_ref[total + e] = regions
            total = (total + GROUP - 1) // GROUP * GROUP

            def mark(g, carry):
                slab_ref[g] = j
                return carry

            lax.fori_loop(first_group, total // GROUP, mark, 0)
        n_groups = total // GROUP
        for e in range(GROUP):
            sel_ref[total + e] = regions
        slab_ref[n_groups] = 0
        n_pairs = (n_groups + 1) // 2
        last = 2 * n_pairs - 1
        out_ref[...] = jnp.zeros(out_ref.shape, jnp.float32)

        def fill(g, buf):
            g_t = gsites_ref[slab_ref[g]].T
            for e in range(GROUP):
                slot = sel_ref[g * GROUP + e]
                buf[:, e * cap : (e + 1) * cap] = corr_block(g_t, sites_ref[slot])

        def use(g, buf):
            j = slab_ref[g]
            weights = jnp.concatenate(
                [w_ref[sel_ref[g * GROUP + e]] for e in range(GROUP)], axis=1
            )
            out_ref[j] = out_ref[j] + contract_lanes(weights, buf[...])

        fill(0, buf0)

        def pair(i, carry):
            g = 2 * i
            use(g, buf0)
            fill(g + 1, buf1)
            use(g + 1, buf1)
            fill(jnp.minimum(g + 2, last), buf0)
            return carry

        lax.fori_loop(0, n_pairs, pair, 0)
        out_ref[...] = out_ref[...] / cap

    return grid_kernel, window


def grid_stage(me, own_slabs, list_slots, site_slots, w_slots, gsites, reg_dev, n_wide, regions, slab_count):
    solves, cap = w_slots.shape[1:]
    n_own, _, gpts = gsites.shape
    kernel, window = make_grid_kernel(regions // slab_count, reg_dev, n_wide, cap, regions)
    vmem = pl.BlockSpec(memory_space=pltpu.VMEM)
    smem = pl.BlockSpec(memory_space=pltpu.SMEM)
    sel_len = n_own * (window + GROUP) + 2 * GROUP
    return pl.pallas_call(
        kernel,
        out_shape=jax.ShapeDtypeStruct((n_own, solves, gpts), jnp.float32),
        in_specs=[smem, smem, smem, vmem, vmem, vmem],
        out_specs=vmem,
        scratch_shapes=[
            pltpu.SMEM((sel_len,), jnp.int32),
            pltpu.SMEM((sel_len // GROUP + 2,), jnp.int32),
            pltpu.VMEM((gpts, GROUP * cap), jnp.float32),
            pltpu.VMEM((gpts, GROUP * cap), jnp.float32),
        ],
    )(me, own_slabs, list_slots, site_slots, w_slots, gsites)


def body(
    obs_latitude,
    obs_offset,
    innovation,
    obs_error,
    region_sizes,
    tile_columns,
    slab_list,
    slab_order,
    grid_latitude,
    grid_offset,
    ridge_weight,
    huber_cut,
    step_size,
):
    reg_dev, capacity = innovation.shape
    n_wide = lax.axis_size("wide")
    regions = reg_dev * n_wide
    margin = reg_dev // 2
    me = lax.axis_index("wide")
    first_row = me * reg_dev
    row_ids = first_row + jnp.arange(reg_dev, dtype=jnp.int32)
    obs_lon = FULL_TURN * (row_ids[:, None].astype(jnp.float32) + obs_offset) / regions
    obs_sites = unit_rows(obs_latitude, obs_lon)
    gpr = slab_list.shape[1]
    packed = jnp.concatenate(
        [
            obs_sites[:, :4, :],
            jnp.pad(slab_list.astype(jnp.float32), ((0, 0), (0, capacity - gpr)))[:, None, :],
        ],
        axis=1,
    )
    slots = gather_slots(packed, "wide")
    spare = jnp.zeros((ROWS, ROWS, capacity), jnp.float32)
    site_slots = jnp.concatenate(
        [jnp.pad(slots[:, :3, :], ((0, 0), (0, ROWS - 3), (0, 0))), spare], axis=0
    )
    list_slots = slots[:, 4, :gpr].astype(jnp.int32).reshape(-1)
    live_mask = (jnp.arange(capacity, dtype=jnp.int32)[None, :] < region_sizes[:, None]).astype(
        jnp.float32
    )
    solves = ridge_weight.shape[0]
    diagonal = (obs_error * obs_error)[:, None, :] + ridge_weight[None, :, None]
    observed = (innovation * live_mask)[:, None, :]
    obs_weights = observed / diagonal
    tile_scale = 2.0 / (capacity * tile_columns.shape[1])
    n_slab = lax.axis_size("slab")
    assert n_slab == 2 and margin * n_slab == reg_dev
    sidx = lax.axis_index("slab")
    sub = reg_dev // n_slab
    blocks = n_wide * n_slab
    pairs = ("wide", "slab")
    other_pairs = [(b, b ^ 1) for b in range(blocks)]
    q1_pairs = [(b, (b - 2) % blocks) if b % 2 == 0 else (b, (b + 2) % blocks) for b in range(blocks)]
    q2_pairs = [(b, (b - 1) % blocks) if b % 2 == 0 else (b, (b + 1) % blocks) for b in range(blocks)]
    first = sidx == 0
    scal = jnp.stack([sidx * sub, first_row, first.astype(jnp.int32)]).astype(jnp.int32)
    count = lax.axis_size("wide")
    both = jnp.concatenate([obs_sites, obs_weights], axis=1)
    tail = lax.slice_in_dim(both, reg_dev - margin, reg_dev, axis=0)
    head = lax.slice_in_dim(both, 0, margin, axis=0)
    left_pack = lax.ppermute(tail, "wide", [(i, (i + 1) % count) for i in range(count)])
    right_pack = lax.ppermute(head, "wide", [((i + 1) % count, i) for i in range(count)])
    common = (obs_sites, left_pack, right_pack, innovation, obs_error)

    def own_rows(mine):
        other = lax.ppermute(mine, pairs, other_pairs)
        return other, jnp.where(first, jnp.concatenate([mine, other]), jnp.concatenate([other, mine]))

    vectors = common + (obs_weights,)
    cache = None
    for sweep_index in range(ITERS):
        result = update(
            scal, sub, tile_columns, region_sizes, ridge_weight, huber_cut, step_size, vectors,
            margin, tile_scale, regions, sweep_index == 0, cache,
        )
        if cache is None:
            mine, cache = result
        else:
            mine = result
        if sweep_index + 1 < ITERS:
            other = lax.ppermute(mine, pairs, other_pairs)
            q1 = lax.ppermute(mine, pairs, q1_pairs)
            q2 = lax.ppermute(mine, pairs, q2_pairs)
            vectors = common + (q1, q2, mine, other)
    other, obs_weights = own_rows(mine)
    w_slots = jnp.concatenate(
        [gather_slots(obs_weights, "wide"), jnp.zeros((ROWS, solves, capacity), jnp.float32)], axis=0
    )

    slab_count = slab_order.shape[0]
    n_own = slab_count // (n_wide * n_slab)
    pos0 = (me * n_slab + lax.axis_index("slab")) * n_own
    own_slabs = lax.dynamic_slice_in_dim(slab_order, pos0, n_own, 0)
    g_lat = grid_latitude[own_slabs]
    g_lon = FULL_TURN * (own_slabs[:, None].astype(jnp.float32) + grid_offset[own_slabs]) / slab_count
    gsites = unit_rows(g_lat, g_lon)
    grid_increment = grid_stage(
        me.astype(jnp.int32).reshape(1),
        own_slabs,
        list_slots,
        site_slots,
        w_slots,
        gsites,
        reg_dev,
        n_wide,
        regions,
        slab_count,
    )
    return (obs_weights, grid_increment)


def solution(mesh):
    in_specs = (
        P(("groups", "wide"), None),
        P(("groups", "wide"), None),
        P(("groups", "wide"), None),
        P(("groups", "wide"), None),
        P(("groups", "wide")),
        P(("groups", "wide"), None),
        P(("groups", "wide"), None),
        P("groups"),
        P(),
        P(),
        P("narrow"),
        P("narrow"),
        P("narrow"),
    )
    out_specs = (
        P(("groups", "wide"), "narrow", None),
        P(("groups", "wide", "slab"), "narrow", None),
    )
    return jax.shard_map(body, mesh=mesh, in_specs=in_specs, out_specs=out_specs, check_vma=False)
```

```python
import jax
import jax.numpy as jnp
from jax import lax
from jax.experimental import pallas as pl
from jax.experimental.pallas import tpu as pltpu
from jax.sharding import PartitionSpec as P

ITERS = 2
SLAB_REACH = 4

DECAY_RATE = 1.0 / 0.15
FULL_TURN = 6.283185307179586
HIGHEST = lax.Precision.HIGHEST
MATMUL_PRECISION = lax.Precision.HIGH
ROWS = 8
GROUP = 4


def with_halo(cells, axis, width):
    count = lax.axis_size(axis)
    head = lax.slice_in_dim(cells, 0, width, axis=0)
    tail = lax.slice_in_dim(cells, cells.shape[0] - width, cells.shape[0], axis=0)
    return jnp.concatenate(
        [
            lax.ppermute(tail, axis, [(i, (i + 1) % count) for i in range(count)]),
            cells,
            lax.ppermute(head, axis, [((i + 1) % count, i) for i in range(count)]),
        ],
        axis=0,
    )


def gather_slots(x, axis):
    count = lax.axis_size(axis)
    parts = [x]
    for s in range(1, count):
        parts.append(lax.ppermute(x, axis, [(i, (i + s) % count) for i in range(count)]))
    return jnp.concatenate(parts, axis=0)


def unit_rows(latitude, longitude):
    c = jnp.cos(latitude)
    zero = jnp.zeros_like(latitude)
    return jnp.stack(
        [c * jnp.cos(longitude), c * jnp.sin(longitude), jnp.sin(latitude)] + [zero] * (ROWS - 3),
        axis=-2,
    )


def corr_block(col_t, row):
    dx = col_t[:, 0:1] - row[0:1, :]
    dy = col_t[:, 1:2] - row[1:2, :]
    dz = col_t[:, 2:3] - row[2:3, :]
    d2 = dx * dx + dy * dy + dz * dz
    return jnp.exp(jnp.sqrt(d2) * (-DECAY_RATE))


def contract_lanes(w, c):
    return lax.dot_general(
        w, c, (((1,), (1,)), ((), ())), precision=MATMUL_PRECISION, preferred_element_type=jnp.float32
    )


def make_update_kernel(margin, tile_scale, regions, first_sweep):
    def update_kernel(scal_ref, tc_ref, sizes_ref, ridge_ref, huber_ref, step_ref, *refs):
        if first_sweep:
            own_ref, sl_ref, sr_ref, innov_ref, err_ref, wo_ref = refs[:6]
        else:
            own_ref, sl_ref, sr_ref, innov_ref, err_ref, q1_ref, q2_ref, mine_ref, other_ref = refs[:9]
        out_ref, buf0, buf1, hs_ref, hw_ref = refs[-5:]
        reg_dev, _, cap = own_ref.shape
        count, solves, _ = out_ref.shape
        tiles = tc_ref.shape[1]
        base = scal_ref[0]
        first_row = scal_ref[1]

        hs_ref[0:margin] = sl_ref[:, 0:ROWS, :]
        hs_ref[margin : margin + reg_dev] = own_ref[...]
        hs_ref[margin + reg_dev :] = sr_ref[:, 0:ROWS, :]
        if first_sweep:
            hw_ref[0:margin] = sl_ref[:, ROWS:, :]
            hw_ref[margin : margin + reg_dev] = wo_ref[...]
            hw_ref[margin + reg_dev :] = sr_ref[:, ROWS:, :]
        else:
            sel = scal_ref[2] == 1
            q1 = q1_ref[...]
            q2 = q2_ref[...]
            mine = mine_ref[...]
            other = other_ref[...]
            hw_ref[0:margin] = jnp.where(sel, q2, q1)
            hw_ref[margin : margin + count] = jnp.where(sel, mine, other)
            hw_ref[margin + count : margin + 2 * count] = jnp.where(sel, other, mine)
            hw_ref[margin + reg_dev :] = jnp.where(sel, q1, q2)

        rows = lax.broadcasted_iota(jnp.int32, (solves, cap), 0)
        ridge_b = jnp.zeros((solves, cap), jnp.float32)
        huber_b = jnp.zeros((solves, cap), jnp.float32)
        step_b = jnp.zeros((solves, cap), jnp.float32)
        for k in range(solves):
            ridge_b = jnp.where(rows == k, ridge_ref[k], ridge_b)
            huber_b = jnp.where(rows == k, huber_ref[k], huber_b)
            step_b = jnp.where(rows == k, step_ref[k], step_b)
        lanes = lax.broadcasted_iota(jnp.int32, (1, cap), 1)

        def column(a, t):
            return lax.rem(tc_ref[a, t] - first_row + margin + regions, regions)

        def fill(i, buf):
            a = i + base
            own_t = own_ref[a].T
            for t in range(tiles):
                buf[:, t * cap : (t + 1) * cap] = corr_block(own_t, hs_ref[column(a, t)])

        def use(i, buf):
            a = i + base
            weights = jnp.concatenate([hw_ref[column(a, t)] for t in range(tiles)], axis=1)
            cov = contract_lanes(weights, buf[...])
            current = hw_ref[a + margin]
            err = err_ref[pl.ds(a, 1), :]
            live = (lanes < sizes_ref[a]).astype(jnp.float32)
            diag = err * err + ridge_b
            thr = huber_b * err
            applied = cov * tile_scale + diag * current
            residual = (innov_ref[pl.ds(a, 1), :] * live - applied) * live
            factor = thr / jnp.maximum(jnp.abs(residual), thr)
            out_ref[i] = current + step_b * factor * residual / diag

        fill(0, buf0)

        def pair(i, carry):
            a = 2 * i
            use(a, buf0)
            fill(a + 1, buf1)
            use(a + 1, buf1)
            fill(jnp.minimum(a + 2, count - 1), buf0)
            return carry

        lax.fori_loop(0, count // 2, pair, 0)

    return update_kernel


def update(scal, count, tc, sizes, ridge, huber, step, vectors, margin, tile_scale, regions, first_sweep):
    own_sites = vectors[0]
    reg_dev, _, cap = own_sites.shape
    solves = ridge.shape[0]
    assert count % 2 == 0
    tiles = tc.shape[1]
    vmem = pl.BlockSpec(memory_space=pltpu.VMEM)
    smem = pl.BlockSpec(memory_space=pltpu.SMEM)
    halo_n = reg_dev + 2 * margin
    return pl.pallas_call(
        make_update_kernel(margin, tile_scale, regions, first_sweep),
        out_shape=jax.ShapeDtypeStruct((count, solves, cap), jnp.float32),
        in_specs=[smem] * 6 + [vmem] * len(vectors),
        out_specs=vmem,
        scratch_shapes=[
            pltpu.VMEM((cap, tiles * cap), jnp.float32),
            pltpu.VMEM((cap, tiles * cap), jnp.float32),
            pltpu.VMEM((halo_n, ROWS, cap), jnp.float32),
            pltpu.VMEM((halo_n, solves, cap), jnp.float32),
        ],
    )(scal, tc, sizes, ridge, huber, step, *vectors)


def make_grid_kernel(per_slab, reg_dev, n_wide, cap, regions):
    window = (2 * SLAB_REACH + 1) * per_slab

    def grid_kernel(
        me_ref, own_slabs_ref, list_ref, sites_ref, w_ref, gsites_ref, out_ref,
        sel_ref, slab_ref, buf0, buf1, acc_ref,
    ):
        n_own = out_ref.shape[0]
        gpr = list_ref.shape[0] // regions
        me = me_ref[0]
        total = jnp.int32(0)
        for j in range(n_own):
            slab = own_slabs_ref[j]
            start = (slab - SLAB_REACH) * per_slab + regions

            def scan(r, count):
                a = lax.rem(start + r, regions)
                owner = a // reg_dev
                slot = lax.rem(me - owner + n_wide, n_wide) * reg_dev + lax.rem(a, reg_dev)
                listed = list_ref[slot * gpr] == slab
                for e in range(1, gpr):
                    listed = jnp.logical_or(listed, list_ref[slot * gpr + e] == slab)
                sel_ref[count] = slot
                return count + listed.astype(jnp.int32)

            first_group = total // GROUP
            total = lax.fori_loop(0, window, scan, total)
            for e in range(GROUP):
                sel_ref[total + e] = regions
            total = (total + GROUP - 1) // GROUP * GROUP

            def mark(g, carry):
                slab_ref[g] = j
                return carry

            lax.fori_loop(first_group, total // GROUP, mark, 0)
        n_groups = total // GROUP
        for e in range(GROUP):
            sel_ref[total + e] = regions
        slab_ref[n_groups] = 0
        n_pairs = (n_groups + 1) // 2
        last = 2 * n_pairs - 1
        acc_ref[...] = jnp.zeros(acc_ref.shape, jnp.float32)

        def fill(g, buf):
            g_t = gsites_ref[slab_ref[g]].T
            for e in range(GROUP):
                slot = sel_ref[g * GROUP + e]
                buf[:, e * cap : (e + 1) * cap] = corr_block(g_t, sites_ref[slot])

        def use(g, buf):
            j = slab_ref[g]
            columns = jnp.concatenate(
                [w_ref[sel_ref[g * GROUP + e]].T for e in range(GROUP)], axis=0
            )
            acc_ref[j] = acc_ref[j] + jnp.dot(
                buf[...], columns, precision=MATMUL_PRECISION, preferred_element_type=jnp.float32
            )

        fill(0, buf0)

        def pair(i, carry):
            g = 2 * i
            use(g, buf0)
            fill(g + 1, buf1)
            use(g + 1, buf1)
            fill(jnp.minimum(g + 2, last), buf0)
            return carry

        lax.fori_loop(0, n_pairs, pair, 0)
        for j in range(n_own):
            out_ref[j] = acc_ref[j].T / cap

    return grid_kernel, window


def grid_stage(me, own_slabs, list_slots, site_slots, w_slots, gsites, reg_dev, n_wide, regions, slab_count):
    solves, cap = w_slots.shape[1:]
    n_own, _, gpts = gsites.shape
    kernel, window = make_grid_kernel(regions // slab_count, reg_dev, n_wide, cap, regions)
    vmem = pl.BlockSpec(memory_space=pltpu.VMEM)
    smem = pl.BlockSpec(memory_space=pltpu.SMEM)
    sel_len = n_own * (window + GROUP) + 2 * GROUP
    return pl.pallas_call(
        kernel,
        out_shape=jax.ShapeDtypeStruct((n_own, solves, gpts), jnp.float32),
        in_specs=[smem, smem, smem, vmem, vmem, vmem],
        out_specs=vmem,
        scratch_shapes=[
            pltpu.SMEM((sel_len,), jnp.int32),
            pltpu.SMEM((sel_len // GROUP + 2,), jnp.int32),
            pltpu.VMEM((gpts, GROUP * cap), jnp.float32),
            pltpu.VMEM((gpts, GROUP * cap), jnp.float32),
            pltpu.VMEM((n_own, gpts, solves), jnp.float32),
        ],
    )(me, own_slabs, list_slots, site_slots, w_slots, gsites)


def body(
    obs_latitude,
    obs_offset,
    innovation,
    obs_error,
    region_sizes,
    tile_columns,
    slab_list,
    slab_order,
    grid_latitude,
    grid_offset,
    ridge_weight,
    huber_cut,
    step_size,
):
    reg_dev, capacity = innovation.shape
    n_wide = lax.axis_size("wide")
    regions = reg_dev * n_wide
    margin = reg_dev // 2
    me = lax.axis_index("wide")
    first_row = me * reg_dev
    row_ids = first_row + jnp.arange(reg_dev, dtype=jnp.int32)
    obs_lon = FULL_TURN * (row_ids[:, None].astype(jnp.float32) + obs_offset) / regions
    obs_sites = unit_rows(obs_latitude, obs_lon)
    gpr = slab_list.shape[1]
    packed = jnp.concatenate(
        [
            obs_sites[:, :4, :],
            jnp.pad(slab_list.astype(jnp.float32), ((0, 0), (0, capacity - gpr)))[:, None, :],
        ],
        axis=1,
    )
    slots = gather_slots(packed, "wide")
    spare = jnp.zeros((ROWS, ROWS, capacity), jnp.float32)
    site_slots = jnp.concatenate(
        [jnp.pad(slots[:, :3, :], ((0, 0), (0, ROWS - 3), (0, 0))), spare], axis=0
    )
    list_slots = slots[:, 4, :gpr].astype(jnp.int32).reshape(-1)
    live_mask = (jnp.arange(capacity, dtype=jnp.int32)[None, :] < region_sizes[:, None]).astype(
        jnp.float32
    )
    solves = ridge_weight.shape[0]
    diagonal = (obs_error * obs_error)[:, None, :] + ridge_weight[None, :, None]
    observed = (innovation * live_mask)[:, None, :]
    obs_weights = observed / diagonal
    tile_scale = 2.0 / (capacity * tile_columns.shape[1])
    n_slab = lax.axis_size("slab")
    assert n_slab == 2 and margin * n_slab == reg_dev
    sidx = lax.axis_index("slab")
    sub = reg_dev // n_slab
    blocks = n_wide * n_slab
    pairs = ("wide", "slab")
    other_pairs = [(b, b ^ 1) for b in range(blocks)]
    q1_pairs = [(b, (b - 2) % blocks) if b % 2 == 0 else (b, (b + 2) % blocks) for b in range(blocks)]
    q2_pairs = [(b, (b - 1) % blocks) if b % 2 == 0 else (b, (b + 1) % blocks) for b in range(blocks)]
    first = sidx == 0
    scal = jnp.stack([sidx * sub, first_row, first.astype(jnp.int32)]).astype(jnp.int32)
    count = lax.axis_size("wide")
    both = jnp.concatenate([obs_sites, obs_weights], axis=1)
    tail = lax.slice_in_dim(both, reg_dev - margin, reg_dev, axis=0)
    head = lax.slice_in_dim(both, 0, margin, axis=0)
    left_pack = lax.ppermute(tail, "wide", [(i, (i + 1) % count) for i in range(count)])
    right_pack = lax.ppermute(head, "wide", [((i + 1) % count, i) for i in range(count)])
    common = (obs_sites, left_pack, right_pack, innovation, obs_error)

    def own_rows(mine):
        other = lax.ppermute(mine, pairs, other_pairs)
        return other, jnp.where(first, jnp.concatenate([mine, other]), jnp.concatenate([other, mine]))

    vectors = common + (obs_weights,)
    for sweep_index in range(ITERS):
        mine = update(
            scal, sub, tile_columns, region_sizes, ridge_weight, huber_cut, step_size, vectors,
            margin, tile_scale, regions, sweep_index == 0,
        )
        if sweep_index + 1 < ITERS:
            other = lax.ppermute(mine, pairs, other_pairs)
            q1 = lax.ppermute(mine, pairs, q1_pairs)
            q2 = lax.ppermute(mine, pairs, q2_pairs)
            vectors = common + (q1, q2, mine, other)
    other, obs_weights = own_rows(mine)
    w_slots = jnp.concatenate(
        [gather_slots(obs_weights, "wide"), jnp.zeros((ROWS, solves, capacity), jnp.float32)], axis=0
    )

    slab_count = slab_order.shape[0]
    n_own = slab_count // (n_wide * n_slab)
    pos0 = (me * n_slab + lax.axis_index("slab")) * n_own
    own_slabs = lax.dynamic_slice_in_dim(slab_order, pos0, n_own, 0)
    g_lat = grid_latitude[own_slabs]
    g_lon = FULL_TURN * (own_slabs[:, None].astype(jnp.float32) + grid_offset[own_slabs]) / slab_count
    gsites = unit_rows(g_lat, g_lon)
    grid_increment = grid_stage(
        me.astype(jnp.int32).reshape(1),
        own_slabs,
        list_slots,
        site_slots,
        w_slots,
        gsites,
        reg_dev,
        n_wide,
        regions,
        slab_count,
    )
    return (obs_weights, grid_increment)


def solution(mesh):
    in_specs = (
        P(("groups", "wide"), None),
        P(("groups", "wide"), None),
        P(("groups", "wide"), None),
        P(("groups", "wide"), None),
        P(("groups", "wide")),
        P(("groups", "wide"), None),
        P(("groups", "wide"), None),
        P("groups"),
        P(),
        P(),
        P("narrow"),
        P("narrow"),
        P("narrow"),
    )
    out_specs = (
        P(("groups", "wide"), "narrow", None),
        P(("groups", "wide", "slab"), "narrow", None),
    )
    return jax.shard_map(body, mesh=mesh, in_specs=in_specs, out_specs=out_specs, check_vma=False)
```

```python
import jax
import jax.numpy as jnp
from jax import lax
from jax.experimental import pallas as pl
from jax.experimental.pallas import tpu as pltpu
from jax.sharding import PartitionSpec as P

ITERS = 2
SLAB_REACH = 4

DECAY_RATE = 1.0 / 0.15
FULL_TURN = 6.283185307179586
HIGHEST = lax.Precision.HIGHEST
MATMUL_PRECISION = lax.Precision.HIGH
ROWS = 8
GROUP = 4
KERNEL_PARAMS = pltpu.CompilerParams()


def with_halo(cells, axis, width):
    count = lax.axis_size(axis)
    head = lax.slice_in_dim(cells, 0, width, axis=0)
    tail = lax.slice_in_dim(cells, cells.shape[0] - width, cells.shape[0], axis=0)
    return jnp.concatenate(
        [
            lax.ppermute(tail, axis, [(i, (i + 1) % count) for i in range(count)]),
            cells,
            lax.ppermute(head, axis, [((i + 1) % count, i) for i in range(count)]),
        ],
        axis=0,
    )


def gather_slots(x, axis):
    count = lax.axis_size(axis)
    parts = [x]
    for s in range(1, count):
        parts.append(lax.ppermute(x, axis, [(i, (i + s) % count) for i in range(count)]))
    return jnp.concatenate(parts, axis=0)


def unit_rows(latitude, longitude):
    c = jnp.cos(latitude)
    zero = jnp.zeros_like(latitude)
    return jnp.stack(
        [c * jnp.cos(longitude), c * jnp.sin(longitude), jnp.sin(latitude)] + [zero] * (ROWS - 3),
        axis=-2,
    )


def corr_block(col_t, row):
    dx = col_t[:, 0:1] - row[0:1, :]
    dy = col_t[:, 1:2] - row[1:2, :]
    dz = col_t[:, 2:3] - row[2:3, :]
    d2 = dx * dx + dy * dy + dz * dz
    return jnp.exp(jnp.sqrt(d2) * (-DECAY_RATE))


def contract_lanes(w, c):
    return lax.dot_general(
        w, c, (((1,), (1,)), ((), ())), precision=MATMUL_PRECISION, preferred_element_type=jnp.float32
    )


def make_update_kernel(margin, tile_scale, regions, first_sweep):
    def update_kernel(scal_ref, tc_ref, sizes_ref, ridge_ref, huber_ref, step_ref, *refs):
        if first_sweep:
            own_ref, sl_ref, sr_ref, innov_ref, err_ref, wo_ref = refs[:6]
        else:
            own_ref, sl_ref, sr_ref, innov_ref, err_ref, q1_ref, q2_ref, mine_ref, other_ref = refs[:9]
        out_ref, buf0, buf1, hs_ref, hw_ref = refs[-5:]
        reg_dev, _, cap = own_ref.shape
        count, solves, _ = out_ref.shape
        tiles = tc_ref.shape[1]
        base = scal_ref[0]
        first_row = scal_ref[1]

        hs_ref[0:margin] = sl_ref[:, 0:ROWS, :]
        hs_ref[margin : margin + reg_dev] = own_ref[...]
        hs_ref[margin + reg_dev :] = sr_ref[:, 0:ROWS, :]
        if first_sweep:
            hw_ref[0:margin] = sl_ref[:, ROWS:, :]
            hw_ref[margin : margin + reg_dev] = wo_ref[...]
            hw_ref[margin + reg_dev :] = sr_ref[:, ROWS:, :]
        else:
            sel = scal_ref[2] == 1
            q1 = q1_ref[...]
            q2 = q2_ref[...]
            mine = mine_ref[...]
            other = other_ref[...]
            hw_ref[0:margin] = jnp.where(sel, q2, q1)
            hw_ref[margin : margin + count] = jnp.where(sel, mine, other)
            hw_ref[margin + count : margin + 2 * count] = jnp.where(sel, other, mine)
            hw_ref[margin + reg_dev :] = jnp.where(sel, q1, q2)

        rows = lax.broadcasted_iota(jnp.int32, (solves, cap), 0)
        ridge_b = jnp.zeros((solves, cap), jnp.float32)
        huber_b = jnp.zeros((solves, cap), jnp.float32)
        step_b = jnp.zeros((solves, cap), jnp.float32)
        for k in range(solves):
            ridge_b = jnp.where(rows == k, ridge_ref[k], ridge_b)
            huber_b = jnp.where(rows == k, huber_ref[k], huber_b)
            step_b = jnp.where(rows == k, step_ref[k], step_b)
        lanes = lax.broadcasted_iota(jnp.int32, (1, cap), 1)

        def column(a, t):
            return lax.rem(tc_ref[a, t] - first_row + margin + regions, regions)

        def fill(i, buf):
            a = i + base
            own_t = own_ref[a].T
            for t in range(tiles):
                buf[:, t * cap : (t + 1) * cap] = corr_block(own_t, hs_ref[column(a, t)])

        def use(i, buf):
            a = i + base
            weights = jnp.concatenate([hw_ref[column(a, t)] for t in range(tiles)], axis=1)
            cov = contract_lanes(weights, buf[...])
            current = hw_ref[a + margin]
            err = err_ref[pl.ds(a, 1), :]
            live = (lanes < sizes_ref[a]).astype(jnp.float32)
            diag = err * err + ridge_b
            thr = huber_b * err
            applied = cov * tile_scale + diag * current
            residual = (innov_ref[pl.ds(a, 1), :] * live - applied) * live
            factor = thr / jnp.maximum(jnp.abs(residual), thr)
            out_ref[i] = current + step_b * factor * residual / diag

        fill(0, buf0)

        def pair(i, carry):
            a = 2 * i
            use(a, buf0)
            fill(a + 1, buf1)
            use(a + 1, buf1)
            fill(jnp.minimum(a + 2, count - 1), buf0)
            return carry

        lax.fori_loop(0, count // 2, pair, 0)

    return update_kernel


def update(scal, count, tc, sizes, ridge, huber, step, vectors, margin, tile_scale, regions, first_sweep):
    own_sites = vectors[0]
    reg_dev, _, cap = own_sites.shape
    solves = ridge.shape[0]
    assert count % 2 == 0
    tiles = tc.shape[1]
    vmem = pl.BlockSpec(memory_space=pltpu.VMEM)
    smem = pl.BlockSpec(memory_space=pltpu.SMEM)
    halo_n = reg_dev + 2 * margin
    return pl.pallas_call(
        make_update_kernel(margin, tile_scale, regions, first_sweep),
        out_shape=jax.ShapeDtypeStruct((count, solves, cap), jnp.float32),
        in_specs=[smem] * 6 + [vmem] * len(vectors),
        out_specs=vmem,
        compiler_params=KERNEL_PARAMS,
        scratch_shapes=[
            pltpu.VMEM((cap, tiles * cap), jnp.float32),
            pltpu.VMEM((cap, tiles * cap), jnp.float32),
            pltpu.VMEM((halo_n, ROWS, cap), jnp.float32),
            pltpu.VMEM((halo_n, solves, cap), jnp.float32),
        ],
    )(scal, tc, sizes, ridge, huber, step, *vectors)


def make_grid_kernel(per_slab, reg_dev, n_wide, cap, regions):
    window = (2 * SLAB_REACH + 1) * per_slab

    def grid_kernel(
        me_ref, own_slabs_ref, list_ref, sites_ref, w_ref, gsites_ref, out_ref,
        sel_ref, slab_ref, buf0, buf1,
    ):
        n_own = out_ref.shape[0]
        gpr = list_ref.shape[0] // regions
        me = me_ref[0]
        total = jnp.int32(0)
        for j in range(n_own):
            slab = own_slabs_ref[j]
            start = (slab - SLAB_REACH) * per_slab + regions

            def scan(r, count):
                a = lax.rem(start + r, regions)
                owner = a // reg_dev
                slot = lax.rem(me - owner + n_wide, n_wide) * reg_dev + lax.rem(a, reg_dev)
                listed = list_ref[slot * gpr] == slab
                for e in range(1, gpr):
                    listed = jnp.logical_or(listed, list_ref[slot * gpr + e] == slab)
                sel_ref[count] = slot
                return count + listed.astype(jnp.int32)

            first_group = total // GROUP
            total = lax.fori_loop(0, window, scan, total)
            for e in range(GROUP):
                sel_ref[total + e] = regions
            total = (total + GROUP - 1) // GROUP * GROUP

            def mark(g, carry):
                slab_ref[g] = j
                return carry

            lax.fori_loop(first_group, total // GROUP, mark, 0)
        n_groups = total // GROUP
        for e in range(GROUP):
            sel_ref[total + e] = regions
        slab_ref[n_groups] = 0
        n_pairs = (n_groups + 1) // 2
        last = 2 * n_pairs - 1
        out_ref[...] = jnp.zeros(out_ref.shape, jnp.float32)

        def fill(g, buf):
            g_t = gsites_ref[slab_ref[g]].T
            for e in range(GROUP):
                slot = sel_ref[g * GROUP + e]
                buf[:, e * cap : (e + 1) * cap] = corr_block(g_t, sites_ref[slot])

        def use(g, buf):
            j = slab_ref[g]
            weights = jnp.concatenate(
                [w_ref[sel_ref[g * GROUP + e]] for e in range(GROUP)], axis=1
            )
            out_ref[j] = out_ref[j] + contract_lanes(weights, buf[...])

        fill(0, buf0)

        def pair(i, carry):
            g = 2 * i
            use(g, buf0)
            fill(g + 1, buf1)
            use(g + 1, buf1)
            fill(jnp.minimum(g + 2, last), buf0)
            return carry

        lax.fori_loop(0, n_pairs, pair, 0)
        out_ref[...] = out_ref[...] / cap

    return grid_kernel, window


def grid_stage(me, own_slabs, list_slots, site_slots, w_slots, gsites, reg_dev, n_wide, regions, slab_count):
    solves, cap = w_slots.shape[1:]
    n_own, _, gpts = gsites.shape
    kernel, window = make_grid_kernel(regions // slab_count, reg_dev, n_wide, cap, regions)
    vmem = pl.BlockSpec(memory_space=pltpu.VMEM)
    smem = pl.BlockSpec(memory_space=pltpu.SMEM)
    sel_len = n_own * (window + GROUP) + 2 * GROUP
    return pl.pallas_call(
        kernel,
        out_shape=jax.ShapeDtypeStruct((n_own, solves, gpts), jnp.float32),
        in_specs=[smem, smem, smem, vmem, vmem, vmem],
        out_specs=vmem,
        compiler_params=KERNEL_PARAMS,
        scratch_shapes=[
            pltpu.SMEM((sel_len,), jnp.int32),
            pltpu.SMEM((sel_len // GROUP + 2,), jnp.int32),
            pltpu.VMEM((gpts, GROUP * cap), jnp.float32),
            pltpu.VMEM((gpts, GROUP * cap), jnp.float32),
        ],
    )(me, own_slabs, list_slots, site_slots, w_slots, gsites)


def body(
    obs_latitude,
    obs_offset,
    innovation,
    obs_error,
    region_sizes,
    tile_columns,
    slab_list,
    slab_order,
    grid_latitude,
    grid_offset,
    ridge_weight,
    huber_cut,
    step_size,
):
    reg_dev, capacity = innovation.shape
    n_wide = lax.axis_size("wide")
    regions = reg_dev * n_wide
    margin = reg_dev // 2
    me = lax.axis_index("wide")
    first_row = me * reg_dev
    row_ids = first_row + jnp.arange(reg_dev, dtype=jnp.int32)
    obs_lon = FULL_TURN * (row_ids[:, None].astype(jnp.float32) + obs_offset) / regions
    obs_sites = unit_rows(obs_latitude, obs_lon)
    gpr = slab_list.shape[1]
    packed = jnp.concatenate(
        [
            obs_sites[:, :4, :],
            jnp.pad(slab_list.astype(jnp.float32), ((0, 0), (0, capacity - gpr)))[:, None, :],
        ],
        axis=1,
    )
    slots = gather_slots(packed, "wide")
    spare = jnp.zeros((ROWS, ROWS, capacity), jnp.float32)
    site_slots = jnp.concatenate(
        [jnp.pad(slots[:, :3, :], ((0, 0), (0, ROWS - 3), (0, 0))), spare], axis=0
    )
    list_slots = slots[:, 4, :gpr].astype(jnp.int32).reshape(-1)
    live_mask = (jnp.arange(capacity, dtype=jnp.int32)[None, :] < region_sizes[:, None]).astype(
        jnp.float32
    )
    solves = ridge_weight.shape[0]
    diagonal = (obs_error * obs_error)[:, None, :] + ridge_weight[None, :, None]
    observed = (innovation * live_mask)[:, None, :]
    obs_weights = observed / diagonal
    tile_scale = 2.0 / (capacity * tile_columns.shape[1])
    n_slab = lax.axis_size("slab")
    assert n_slab == 2 and margin * n_slab == reg_dev
    sidx = lax.axis_index("slab")
    sub = reg_dev // n_slab
    blocks = n_wide * n_slab
    pairs = ("wide", "slab")
    other_pairs = [(b, b ^ 1) for b in range(blocks)]
    q1_pairs = [(b, (b - 2) % blocks) if b % 2 == 0 else (b, (b + 2) % blocks) for b in range(blocks)]
    q2_pairs = [(b, (b - 1) % blocks) if b % 2 == 0 else (b, (b + 1) % blocks) for b in range(blocks)]
    first = sidx == 0
    scal = jnp.stack([sidx * sub, first_row, first.astype(jnp.int32)]).astype(jnp.int32)
    count = lax.axis_size("wide")
    both = jnp.concatenate([obs_sites, obs_weights], axis=1)
    tail = lax.slice_in_dim(both, reg_dev - margin, reg_dev, axis=0)
    head = lax.slice_in_dim(both, 0, margin, axis=0)
    left_pack = lax.ppermute(tail, "wide", [(i, (i + 1) % count) for i in range(count)])
    right_pack = lax.ppermute(head, "wide", [((i + 1) % count, i) for i in range(count)])
    common = (obs_sites, left_pack, right_pack, innovation, obs_error)

    def own_rows(mine):
        other = lax.ppermute(mine, pairs, other_pairs)
        return other, jnp.where(first, jnp.concatenate([mine, other]), jnp.concatenate([other, mine]))

    vectors = common + (obs_weights,)
    for sweep_index in range(ITERS):
        mine = update(
            scal, sub, tile_columns, region_sizes, ridge_weight, huber_cut, step_size, vectors,
            margin, tile_scale, regions, sweep_index == 0,
        )
        if sweep_index + 1 < ITERS:
            other = lax.ppermute(mine, pairs, other_pairs)
            q1 = lax.ppermute(mine, pairs, q1_pairs)
            q2 = lax.ppermute(mine, pairs, q2_pairs)
            vectors = common + (q1, q2, mine, other)
    other, obs_weights = own_rows(mine)
    w_slots = jnp.concatenate(
        [gather_slots(obs_weights, "wide"), jnp.zeros((ROWS, solves, capacity), jnp.float32)], axis=0
    )

    slab_count = slab_order.shape[0]
    n_own = slab_count // (n_wide * n_slab)
    pos0 = (me * n_slab + lax.axis_index("slab")) * n_own
    own_slabs = lax.dynamic_slice_in_dim(slab_order, pos0, n_own, 0)
    g_lat = grid_latitude[own_slabs]
    g_lon = FULL_TURN * (own_slabs[:, None].astype(jnp.float32) + grid_offset[own_slabs]) / slab_count
    gsites = unit_rows(g_lat, g_lon)
    grid_increment = grid_stage(
        me.astype(jnp.int32).reshape(1),
        own_slabs,
        list_slots,
        site_slots,
        w_slots,
        gsites,
        reg_dev,
        n_wide,
        regions,
        slab_count,
    )
    return (obs_weights, grid_increment)


def solution(mesh):
    in_specs = (
        P(("groups", "wide"), None),
        P(("groups", "wide"), None),
        P(("groups", "wide"), None),
        P(("groups", "wide"), None),
        P(("groups", "wide")),
        P(("groups", "wide"), None),
        P(("groups", "wide"), None),
        P("groups"),
        P(),
        P(),
        P("narrow"),
        P("narrow"),
        P("narrow"),
    )
    out_specs = (
        P(("groups", "wide"), "narrow", None),
        P(("groups", "wide", "slab"), "narrow", None),
    )
    return jax.shard_map(body, mesh=mesh, in_specs=in_specs, out_specs=out_specs, check_vma=False)
```

```python
import jax
import jax.numpy as jnp
from jax import lax
from jax.experimental import pallas as pl
from jax.experimental.pallas import tpu as pltpu
from jax.sharding import PartitionSpec as P

ITERS = 2
SLAB_REACH = 4

DECAY_RATE = 1.0 / 0.15
FULL_TURN = 6.283185307179586
HIGHEST = lax.Precision.HIGHEST
MATMUL_PRECISION = lax.Precision.HIGH
ROWS = 8
GROUP = 2


def with_halo(cells, axis, width):
    count = lax.axis_size(axis)
    head = lax.slice_in_dim(cells, 0, width, axis=0)
    tail = lax.slice_in_dim(cells, cells.shape[0] - width, cells.shape[0], axis=0)
    return jnp.concatenate(
        [
            lax.ppermute(tail, axis, [(i, (i + 1) % count) for i in range(count)]),
            cells,
            lax.ppermute(head, axis, [((i + 1) % count, i) for i in range(count)]),
        ],
        axis=0,
    )


def gather_slots(x, axis):
    count = lax.axis_size(axis)
    parts = [x]
    for s in range(1, count):
        parts.append(lax.ppermute(x, axis, [(i, (i + s) % count) for i in range(count)]))
    return jnp.concatenate(parts, axis=0)


def unit_rows(latitude, longitude):
    c = jnp.cos(latitude)
    zero = jnp.zeros_like(latitude)
    return jnp.stack(
        [c * jnp.cos(longitude), c * jnp.sin(longitude), jnp.sin(latitude)] + [zero] * (ROWS - 3),
        axis=-2,
    )


def corr_block(col_t, row):
    dx = col_t[:, 0:1] - row[0:1, :]
    dy = col_t[:, 1:2] - row[1:2, :]
    dz = col_t[:, 2:3] - row[2:3, :]
    d2 = dx * dx + dy * dy + dz * dz
    return jnp.exp(jnp.sqrt(d2) * (-DECAY_RATE))


def contract_lanes(w, c):
    return lax.dot_general(
        w, c, (((1,), (1,)), ((), ())), precision=MATMUL_PRECISION, preferred_element_type=jnp.float32
    )


def make_update_kernel(margin, tile_scale, regions, first_sweep):
    def update_kernel(scal_ref, tc_ref, sizes_ref, ridge_ref, huber_ref, step_ref, *refs):
        if first_sweep:
            own_ref, sl_ref, sr_ref, innov_ref, err_ref, wo_ref = refs[:6]
        else:
            own_ref, sl_ref, sr_ref, innov_ref, err_ref, q1_ref, q2_ref, mine_ref, other_ref = refs[:9]
        out_ref, buf0, buf1, hs_ref, hw_ref = refs[-5:]
        reg_dev, _, cap = own_ref.shape
        count, solves, _ = out_ref.shape
        tiles = tc_ref.shape[1]
        base = scal_ref[0]
        first_row = scal_ref[1]

        hs_ref[0:margin] = sl_ref[:, 0:ROWS, :]
        hs_ref[margin : margin + reg_dev] = own_ref[...]
        hs_ref[margin + reg_dev :] = sr_ref[:, 0:ROWS, :]
        if first_sweep:
            hw_ref[0:margin] = sl_ref[:, ROWS:, :]
            hw_ref[margin : margin + reg_dev] = wo_ref[...]
            hw_ref[margin + reg_dev :] = sr_ref[:, ROWS:, :]
        else:
            sel = scal_ref[2] == 1
            q1 = q1_ref[...]
            q2 = q2_ref[...]
            mine = mine_ref[...]
            other = other_ref[...]
            hw_ref[0:margin] = jnp.where(sel, q2, q1)
            hw_ref[margin : margin + count] = jnp.where(sel, mine, other)
            hw_ref[margin + count : margin + 2 * count] = jnp.where(sel, other, mine)
            hw_ref[margin + reg_dev :] = jnp.where(sel, q1, q2)

        rows = lax.broadcasted_iota(jnp.int32, (solves, cap), 0)
        ridge_b = jnp.zeros((solves, cap), jnp.float32)
        huber_b = jnp.zeros((solves, cap), jnp.float32)
        step_b = jnp.zeros((solves, cap), jnp.float32)
        for k in range(solves):
            ridge_b = jnp.where(rows == k, ridge_ref[k], ridge_b)
            huber_b = jnp.where(rows == k, huber_ref[k], huber_b)
            step_b = jnp.where(rows == k, step_ref[k], step_b)
        lanes = lax.broadcasted_iota(jnp.int32, (1, cap), 1)

        def column(a, t):
            return lax.rem(tc_ref[a, t] - first_row + margin + regions, regions)

        def fill(i, buf):
            a = i + base
            own_t = own_ref[a].T
            for t in range(tiles):
                buf[:, t * cap : (t + 1) * cap] = corr_block(own_t, hs_ref[column(a, t)])

        def use(i, buf):
            a = i + base
            weights = jnp.concatenate([hw_ref[column(a, t)] for t in range(tiles)], axis=1)
            cov = contract_lanes(weights, buf[...])
            current = hw_ref[a + margin]
            err = err_ref[pl.ds(a, 1), :]
            live = (lanes < sizes_ref[a]).astype(jnp.float32)
            diag = err * err + ridge_b
            thr = huber_b * err
            applied = cov * tile_scale + diag * current
            residual = (innov_ref[pl.ds(a, 1), :] * live - applied) * live
            factor = thr / jnp.maximum(jnp.abs(residual), thr)
            out_ref[i] = current + step_b * factor * residual / diag

        fill(0, buf0)

        def pair(i, carry):
            a = 2 * i
            use(a, buf0)
            fill(a + 1, buf1)
            use(a + 1, buf1)
            fill(jnp.minimum(a + 2, count - 1), buf0)
            return carry

        lax.fori_loop(0, count // 2, pair, 0)

    return update_kernel


def update(scal, count, tc, sizes, ridge, huber, step, vectors, margin, tile_scale, regions, first_sweep):
    own_sites = vectors[0]
    reg_dev, _, cap = own_sites.shape
    solves = ridge.shape[0]
    assert count % 2 == 0
    tiles = tc.shape[1]
    vmem = pl.BlockSpec(memory_space=pltpu.VMEM)
    smem = pl.BlockSpec(memory_space=pltpu.SMEM)
    halo_n = reg_dev + 2 * margin
    return pl.pallas_call(
        make_update_kernel(margin, tile_scale, regions, first_sweep),
        out_shape=jax.ShapeDtypeStruct((count, solves, cap), jnp.float32),
        in_specs=[smem] * 6 + [vmem] * len(vectors),
        out_specs=vmem,
        scratch_shapes=[
            pltpu.VMEM((cap, tiles * cap), jnp.float32),
            pltpu.VMEM((cap, tiles * cap), jnp.float32),
            pltpu.VMEM((halo_n, ROWS, cap), jnp.float32),
            pltpu.VMEM((halo_n, solves, cap), jnp.float32),
        ],
    )(scal, tc, sizes, ridge, huber, step, *vectors)


def make_grid_kernel(per_slab, reg_dev, n_wide, cap, regions):
    window = (2 * SLAB_REACH + 1) * per_slab

    def grid_kernel(
        me_ref, own_slabs_ref, list_ref, sites_ref, w_ref, gsites_ref, out_ref,
        sel_ref, slab_ref, buf0, buf1,
    ):
        n_own = out_ref.shape[0]
        gpr = list_ref.shape[0] // regions
        me = me_ref[0]
        total = jnp.int32(0)
        for j in range(n_own):
            slab = own_slabs_ref[j]
            start = (slab - SLAB_REACH) * per_slab + regions

            def scan(r, count):
                a = lax.rem(start + r, regions)
                owner = a // reg_dev
                slot = lax.rem(me - owner + n_wide, n_wide) * reg_dev + lax.rem(a, reg_dev)
                listed = list_ref[slot * gpr] == slab
                for e in range(1, gpr):
                    listed = jnp.logical_or(listed, list_ref[slot * gpr + e] == slab)
                sel_ref[count] = slot
                return count + listed.astype(jnp.int32)

            first_group = total // GROUP
            total = lax.fori_loop(0, window, scan, total)
            for e in range(GROUP):
                sel_ref[total + e] = regions
            total = (total + GROUP - 1) // GROUP * GROUP

            def mark(g, carry):
                slab_ref[g] = j
                return carry

            lax.fori_loop(first_group, total // GROUP, mark, 0)
        n_groups = total // GROUP
        for e in range(GROUP):
            sel_ref[total + e] = regions
        slab_ref[n_groups] = 0
        n_pairs = (n_groups + 1) // 2
        last = 2 * n_pairs - 1
        out_ref[...] = jnp.zeros(out_ref.shape, jnp.float32)

        def fill(g, buf):
            g_t = gsites_ref[slab_ref[g]].T
            for e in range(GROUP):
                slot = sel_ref[g * GROUP + e]
                buf[:, e * cap : (e + 1) * cap] = corr_block(g_t, sites_ref[slot])

        def use(g, buf):
            j = slab_ref[g]
            weights = jnp.concatenate(
                [w_ref[sel_ref[g * GROUP + e]] for e in range(GROUP)], axis=1
            )
            out_ref[j] = out_ref[j] + contract_lanes(weights, buf[...])

        fill(0, buf0)

        def pair(i, carry):
            g = 2 * i
            use(g, buf0)
            fill(g + 1, buf1)
            use(g + 1, buf1)
            fill(jnp.minimum(g + 2, last), buf0)
            return carry

        lax.fori_loop(0, n_pairs, pair, 0)
        out_ref[...] = out_ref[...] / cap

    return grid_kernel, window


def grid_stage(me, own_slabs, list_slots, site_slots, w_slots, gsites, reg_dev, n_wide, regions, slab_count):
    solves, cap = w_slots.shape[1:]
    n_own, _, gpts = gsites.shape
    kernel, window = make_grid_kernel(regions // slab_count, reg_dev, n_wide, cap, regions)
    vmem = pl.BlockSpec(memory_space=pltpu.VMEM)
    smem = pl.BlockSpec(memory_space=pltpu.SMEM)
    sel_len = n_own * (window + GROUP) + 2 * GROUP
    return pl.pallas_call(
        kernel,
        out_shape=jax.ShapeDtypeStruct((n_own, solves, gpts), jnp.float32),
        in_specs=[smem, smem, smem, vmem, vmem, vmem],
        out_specs=vmem,
        scratch_shapes=[
            pltpu.SMEM((sel_len,), jnp.int32),
            pltpu.SMEM((sel_len // GROUP + 2,), jnp.int32),
            pltpu.VMEM((gpts, GROUP * cap), jnp.float32),
            pltpu.VMEM((gpts, GROUP * cap), jnp.float32),
        ],
    )(me, own_slabs, list_slots, site_slots, w_slots, gsites)


def body(
    obs_latitude,
    obs_offset,
    innovation,
    obs_error,
    region_sizes,
    tile_columns,
    slab_list,
    slab_order,
    grid_latitude,
    grid_offset,
    ridge_weight,
    huber_cut,
    step_size,
):
    reg_dev, capacity = innovation.shape
    n_wide = lax.axis_size("wide")
    regions = reg_dev * n_wide
    margin = reg_dev // 2
    me = lax.axis_index("wide")
    first_row = me * reg_dev
    row_ids = first_row + jnp.arange(reg_dev, dtype=jnp.int32)
    obs_lon = FULL_TURN * (row_ids[:, None].astype(jnp.float32) + obs_offset) / regions
    obs_sites = unit_rows(obs_latitude, obs_lon)
    gpr = slab_list.shape[1]
    packed = jnp.concatenate(
        [
            obs_sites[:, :4, :],
            jnp.pad(slab_list.astype(jnp.float32), ((0, 0), (0, capacity - gpr)))[:, None, :],
        ],
        axis=1,
    )
    slots = gather_slots(packed, "wide")
    spare = jnp.zeros((ROWS, ROWS, capacity), jnp.float32)
    site_slots = jnp.concatenate(
        [jnp.pad(slots[:, :3, :], ((0, 0), (0, ROWS - 3), (0, 0))), spare], axis=0
    )
    list_slots = slots[:, 4, :gpr].astype(jnp.int32).reshape(-1)
    live_mask = (jnp.arange(capacity, dtype=jnp.int32)[None, :] < region_sizes[:, None]).astype(
        jnp.float32
    )
    solves = ridge_weight.shape[0]
    diagonal = (obs_error * obs_error)[:, None, :] + ridge_weight[None, :, None]
    observed = (innovation * live_mask)[:, None, :]
    obs_weights = observed / diagonal
    tile_scale = 2.0 / (capacity * tile_columns.shape[1])
    n_slab = lax.axis_size("slab")
    assert n_slab == 2 and margin * n_slab == reg_dev
    sidx = lax.axis_index("slab")
    sub = reg_dev // n_slab
    blocks = n_wide * n_slab
    pairs = ("wide", "slab")
    other_pairs = [(b, b ^ 1) for b in range(blocks)]
    q1_pairs = [(b, (b - 2) % blocks) if b % 2 == 0 else (b, (b + 2) % blocks) for b in range(blocks)]
    q2_pairs = [(b, (b - 1) % blocks) if b % 2 == 0 else (b, (b + 1) % blocks) for b in range(blocks)]
    first = sidx == 0
    scal = jnp.stack([sidx * sub, first_row, first.astype(jnp.int32)]).astype(jnp.int32)
    count = lax.axis_size("wide")
    both = jnp.concatenate([obs_sites, obs_weights], axis=1)
    tail = lax.slice_in_dim(both, reg_dev - margin, reg_dev, axis=0)
    head = lax.slice_in_dim(both, 0, margin, axis=0)
    left_pack = lax.ppermute(tail, "wide", [(i, (i + 1) % count) for i in range(count)])
    right_pack = lax.ppermute(head, "wide", [((i + 1) % count, i) for i in range(count)])
    common = (obs_sites, left_pack, right_pack, innovation, obs_error)

    def own_rows(mine):
        other = lax.ppermute(mine, pairs, other_pairs)
        return other, jnp.where(first, jnp.concatenate([mine, other]), jnp.concatenate([other, mine]))

    vectors = common + (obs_weights,)
    for sweep_index in range(ITERS):
        mine = update(
            scal, sub, tile_columns, region_sizes, ridge_weight, huber_cut, step_size, vectors,
            margin, tile_scale, regions, sweep_index == 0,
        )
        if sweep_index + 1 < ITERS:
            other = lax.ppermute(mine, pairs, other_pairs)
            q1 = lax.ppermute(mine, pairs, q1_pairs)
            q2 = lax.ppermute(mine, pairs, q2_pairs)
            vectors = common + (q1, q2, mine, other)
    other, obs_weights = own_rows(mine)
    w_slots = jnp.concatenate(
        [gather_slots(obs_weights, "wide"), jnp.zeros((ROWS, solves, capacity), jnp.float32)], axis=0
    )

    slab_count = slab_order.shape[0]
    n_own = slab_count // (n_wide * n_slab)
    pos0 = (me * n_slab + lax.axis_index("slab")) * n_own
    own_slabs = lax.dynamic_slice_in_dim(slab_order, pos0, n_own, 0)
    g_lat = grid_latitude[own_slabs]
    g_lon = FULL_TURN * (own_slabs[:, None].astype(jnp.float32) + grid_offset[own_slabs]) / slab_count
    gsites = unit_rows(g_lat, g_lon)
    grid_increment = grid_stage(
        me.astype(jnp.int32).reshape(1),
        own_slabs,
        list_slots,
        site_slots,
        w_slots,
        gsites,
        reg_dev,
        n_wide,
        regions,
        slab_count,
    )
    return (obs_weights, grid_increment)


def solution(mesh):
    in_specs = (
        P(("groups", "wide"), None),
        P(("groups", "wide"), None),
        P(("groups", "wide"), None),
        P(("groups", "wide"), None),
        P(("groups", "wide")),
        P(("groups", "wide"), None),
        P(("groups", "wide"), None),
        P("groups"),
        P(),
        P(),
        P("narrow"),
        P("narrow"),
        P("narrow"),
    )
    out_specs = (
        P(("groups", "wide"), "narrow", None),
        P(("groups", "wide", "slab"), "narrow", None),
    )
    return jax.shard_map(body, mesh=mesh, in_specs=in_specs, out_specs=out_specs, check_vma=False)
```

```python
import jax
import jax.numpy as jnp
from jax import lax
from jax.experimental import pallas as pl
from jax.experimental.pallas import tpu as pltpu
from jax.sharding import PartitionSpec as P

ITERS = 2
SLAB_REACH = 4

DECAY_RATE = 1.0 / 0.15
FULL_TURN = 6.283185307179586
HIGHEST = lax.Precision.HIGHEST
MATMUL_PRECISION = lax.Precision.HIGH
ROWS = 8
GROUP = 1


def with_halo(cells, axis, width):
    count = lax.axis_size(axis)
    head = lax.slice_in_dim(cells, 0, width, axis=0)
    tail = lax.slice_in_dim(cells, cells.shape[0] - width, cells.shape[0], axis=0)
    return jnp.concatenate(
        [
            lax.ppermute(tail, axis, [(i, (i + 1) % count) for i in range(count)]),
            cells,
            lax.ppermute(head, axis, [((i + 1) % count, i) for i in range(count)]),
        ],
        axis=0,
    )


def gather_slots(x, axis):
    count = lax.axis_size(axis)
    parts = [x]
    for s in range(1, count):
        parts.append(lax.ppermute(x, axis, [(i, (i + s) % count) for i in range(count)]))
    return jnp.concatenate(parts, axis=0)


def unit_rows(latitude, longitude):
    c = jnp.cos(latitude)
    zero = jnp.zeros_like(latitude)
    return jnp.stack(
        [c * jnp.cos(longitude), c * jnp.sin(longitude), jnp.sin(latitude)] + [zero] * (ROWS - 3),
        axis=-2,
    )


def corr_block(col_t, row):
    dx = col_t[:, 0:1] - row[0:1, :]
    dy = col_t[:, 1:2] - row[1:2, :]
    dz = col_t[:, 2:3] - row[2:3, :]
    d2 = dx * dx + dy * dy + dz * dz
    return jnp.exp(jnp.sqrt(d2) * (-DECAY_RATE))


def contract_lanes(w, c):
    return lax.dot_general(
        w, c, (((1,), (1,)), ((), ())), precision=MATMUL_PRECISION, preferred_element_type=jnp.float32
    )


def make_update_kernel(margin, tile_scale, regions, first_sweep):
    def update_kernel(scal_ref, tc_ref, sizes_ref, ridge_ref, huber_ref, step_ref, *refs):
        if first_sweep:
            own_ref, sl_ref, sr_ref, innov_ref, err_ref, wo_ref = refs[:6]
        else:
            own_ref, sl_ref, sr_ref, innov_ref, err_ref, q1_ref, q2_ref, mine_ref, other_ref = refs[:9]
        out_ref, buf0, buf1, hs_ref, hw_ref = refs[-5:]
        reg_dev, _, cap = own_ref.shape
        count, solves, _ = out_ref.shape
        tiles = tc_ref.shape[1]
        base = scal_ref[0]
        first_row = scal_ref[1]

        hs_ref[0:margin] = sl_ref[:, 0:ROWS, :]
        hs_ref[margin : margin + reg_dev] = own_ref[...]
        hs_ref[margin + reg_dev :] = sr_ref[:, 0:ROWS, :]
        if first_sweep:
            hw_ref[0:margin] = sl_ref[:, ROWS:, :]
            hw_ref[margin : margin + reg_dev] = wo_ref[...]
            hw_ref[margin + reg_dev :] = sr_ref[:, ROWS:, :]
        else:
            sel = scal_ref[2] == 1
            q1 = q1_ref[...]
            q2 = q2_ref[...]
            mine = mine_ref[...]
            other = other_ref[...]
            hw_ref[0:margin] = jnp.where(sel, q2, q1)
            hw_ref[margin : margin + count] = jnp.where(sel, mine, other)
            hw_ref[margin + count : margin + 2 * count] = jnp.where(sel, other, mine)
            hw_ref[margin + reg_dev :] = jnp.where(sel, q1, q2)

        rows = lax.broadcasted_iota(jnp.int32, (solves, cap), 0)
        ridge_b = jnp.zeros((solves, cap), jnp.float32)
        huber_b = jnp.zeros((solves, cap), jnp.float32)
        step_b = jnp.zeros((solves, cap), jnp.float32)
        for k in range(solves):
            ridge_b = jnp.where(rows == k, ridge_ref[k], ridge_b)
            huber_b = jnp.where(rows == k, huber_ref[k], huber_b)
            step_b = jnp.where(rows == k, step_ref[k], step_b)
        lanes = lax.broadcasted_iota(jnp.int32, (1, cap), 1)

        def column(a, t):
            return lax.rem(tc_ref[a, t] - first_row + margin + regions, regions)

        def fill(i, buf):
            a = i + base
            own_t = own_ref[a].T
            for t in range(tiles):
                buf[:, t * cap : (t + 1) * cap] = corr_block(own_t, hs_ref[column(a, t)])

        def use(i, buf):
            a = i + base
            weights = jnp.concatenate([hw_ref[column(a, t)] for t in range(tiles)], axis=1)
            cov = contract_lanes(weights, buf[...])
            current = hw_ref[a + margin]
            err = err_ref[pl.ds(a, 1), :]
            live = (lanes < sizes_ref[a]).astype(jnp.float32)
            diag = err * err + ridge_b
            thr = huber_b * err
            applied = cov * tile_scale + diag * current
            residual = (innov_ref[pl.ds(a, 1), :] * live - applied) * live
            factor = thr / jnp.maximum(jnp.abs(residual), thr)
            out_ref[i] = current + step_b * factor * residual / diag

        fill(0, buf0)

        def pair(i, carry):
            a = 2 * i
            use(a, buf0)
            fill(a + 1, buf1)
            use(a + 1, buf1)
            fill(jnp.minimum(a + 2, count - 1), buf0)
            return carry

        lax.fori_loop(0, count // 2, pair, 0)

    return update_kernel


def update(scal, count, tc, sizes, ridge, huber, step, vectors, margin, tile_scale, regions, first_sweep):
    own_sites = vectors[0]
    reg_dev, _, cap = own_sites.shape
    solves = ridge.shape[0]
    assert count % 2 == 0
    tiles = tc.shape[1]
    vmem = pl.BlockSpec(memory_space=pltpu.VMEM)
    smem = pl.BlockSpec(memory_space=pltpu.SMEM)
    halo_n = reg_dev + 2 * margin
    return pl.pallas_call(
        make_update_kernel(margin, tile_scale, regions, first_sweep),
        out_shape=jax.ShapeDtypeStruct((count, solves, cap), jnp.float32),
        in_specs=[smem] * 6 + [vmem] * len(vectors),
        out_specs=vmem,
        scratch_shapes=[
            pltpu.VMEM((cap, tiles * cap), jnp.float32),
            pltpu.VMEM((cap, tiles * cap), jnp.float32),
            pltpu.VMEM((halo_n, ROWS, cap), jnp.float32),
            pltpu.VMEM((halo_n, solves, cap), jnp.float32),
        ],
    )(scal, tc, sizes, ridge, huber, step, *vectors)


def make_grid_kernel(per_slab, reg_dev, n_wide, cap, regions):
    window = (2 * SLAB_REACH + 1) * per_slab

    def grid_kernel(
        me_ref, own_slabs_ref, list_ref, sites_ref, w_ref, gsites_ref, out_ref,
        sel_ref, slab_ref, buf0, buf1,
    ):
        n_own = out_ref.shape[0]
        gpr = list_ref.shape[0] // regions
        me = me_ref[0]
        total = jnp.int32(0)
        for j in range(n_own):
            slab = own_slabs_ref[j]
            start = (slab - SLAB_REACH) * per_slab + regions

            def scan(r, count):
                a = lax.rem(start + r, regions)
                owner = a // reg_dev
                slot = lax.rem(me - owner + n_wide, n_wide) * reg_dev + lax.rem(a, reg_dev)
                listed = list_ref[slot * gpr] == slab
                for e in range(1, gpr):
                    listed = jnp.logical_or(listed, list_ref[slot * gpr + e] == slab)
                sel_ref[count] = slot
                return count + listed.astype(jnp.int32)

            first_group = total // GROUP
            total = lax.fori_loop(0, window, scan, total)
            for e in range(GROUP):
                sel_ref[total + e] = regions
            total = (total + GROUP - 1) // GROUP * GROUP

            def mark(g, carry):
                slab_ref[g] = j
                return carry

            lax.fori_loop(first_group, total // GROUP, mark, 0)
        n_groups = total // GROUP
        for e in range(GROUP):
            sel_ref[total + e] = regions
        slab_ref[n_groups] = 0
        n_pairs = (n_groups + 1) // 2
        last = 2 * n_pairs - 1
        out_ref[...] = jnp.zeros(out_ref.shape, jnp.float32)

        def fill(g, buf):
            g_t = gsites_ref[slab_ref[g]].T
            for e in range(GROUP):
                slot = sel_ref[g * GROUP + e]
                buf[:, e * cap : (e + 1) * cap] = corr_block(g_t, sites_ref[slot])

        def use(g, buf):
            j = slab_ref[g]
            weights = jnp.concatenate(
                [w_ref[sel_ref[g * GROUP + e]] for e in range(GROUP)], axis=1
            )
            out_ref[j] = out_ref[j] + contract_lanes(weights, buf[...])

        fill(0, buf0)

        def pair(i, carry):
            g = 2 * i
            use(g, buf0)
            fill(g + 1, buf1)
            use(g + 1, buf1)
            fill(jnp.minimum(g + 2, last), buf0)
            return carry

        lax.fori_loop(0, n_pairs, pair, 0)
        out_ref[...] = out_ref[...] / cap

    return grid_kernel, window


def grid_stage(me, own_slabs, list_slots, site_slots, w_slots, gsites, reg_dev, n_wide, regions, slab_count):
    solves, cap = w_slots.shape[1:]
    n_own, _, gpts = gsites.shape
    kernel, window = make_grid_kernel(regions // slab_count, reg_dev, n_wide, cap, regions)
    vmem = pl.BlockSpec(memory_space=pltpu.VMEM)
    smem = pl.BlockSpec(memory_space=pltpu.SMEM)
    sel_len = n_own * (window + GROUP) + 2 * GROUP
    return pl.pallas_call(
        kernel,
        out_shape=jax.ShapeDtypeStruct((n_own, solves, gpts), jnp.float32),
        in_specs=[smem, smem, smem, vmem, vmem, vmem],
        out_specs=vmem,
        scratch_shapes=[
            pltpu.SMEM((sel_len,), jnp.int32),
            pltpu.SMEM((sel_len // GROUP + 2,), jnp.int32),
            pltpu.VMEM((gpts, GROUP * cap), jnp.float32),
            pltpu.VMEM((gpts, GROUP * cap), jnp.float32),
        ],
    )(me, own_slabs, list_slots, site_slots, w_slots, gsites)


def body(
    obs_latitude,
    obs_offset,
    innovation,
    obs_error,
    region_sizes,
    tile_columns,
    slab_list,
    slab_order,
    grid_latitude,
    grid_offset,
    ridge_weight,
    huber_cut,
    step_size,
):
    reg_dev, capacity = innovation.shape
    n_wide = lax.axis_size("wide")
    regions = reg_dev * n_wide
    margin = reg_dev // 2
    me = lax.axis_index("wide")
    first_row = me * reg_dev
    row_ids = first_row + jnp.arange(reg_dev, dtype=jnp.int32)
    obs_lon = FULL_TURN * (row_ids[:, None].astype(jnp.float32) + obs_offset) / regions
    obs_sites = unit_rows(obs_latitude, obs_lon)
    gpr = slab_list.shape[1]
    packed = jnp.concatenate(
        [
            obs_sites[:, :4, :],
            jnp.pad(slab_list.astype(jnp.float32), ((0, 0), (0, capacity - gpr)))[:, None, :],
        ],
        axis=1,
    )
    slots = gather_slots(packed, "wide")
    spare = jnp.zeros((ROWS, ROWS, capacity), jnp.float32)
    site_slots = jnp.concatenate(
        [jnp.pad(slots[:, :3, :], ((0, 0), (0, ROWS - 3), (0, 0))), spare], axis=0
    )
    list_slots = slots[:, 4, :gpr].astype(jnp.int32).reshape(-1)
    live_mask = (jnp.arange(capacity, dtype=jnp.int32)[None, :] < region_sizes[:, None]).astype(
        jnp.float32
    )
    solves = ridge_weight.shape[0]
    diagonal = (obs_error * obs_error)[:, None, :] + ridge_weight[None, :, None]
    observed = (innovation * live_mask)[:, None, :]
    obs_weights = observed / diagonal
    tile_scale = 2.0 / (capacity * tile_columns.shape[1])
    n_slab = lax.axis_size("slab")
    assert n_slab == 2 and margin * n_slab == reg_dev
    sidx = lax.axis_index("slab")
    sub = reg_dev // n_slab
    blocks = n_wide * n_slab
    pairs = ("wide", "slab")
    other_pairs = [(b, b ^ 1) for b in range(blocks)]
    q1_pairs = [(b, (b - 2) % blocks) if b % 2 == 0 else (b, (b + 2) % blocks) for b in range(blocks)]
    q2_pairs = [(b, (b - 1) % blocks) if b % 2 == 0 else (b, (b + 1) % blocks) for b in range(blocks)]
    first = sidx == 0
    scal = jnp.stack([sidx * sub, first_row, first.astype(jnp.int32)]).astype(jnp.int32)
    count = lax.axis_size("wide")
    both = jnp.concatenate([obs_sites, obs_weights], axis=1)
    tail = lax.slice_in_dim(both, reg_dev - margin, reg_dev, axis=0)
    head = lax.slice_in_dim(both, 0, margin, axis=0)
    left_pack = lax.ppermute(tail, "wide", [(i, (i + 1) % count) for i in range(count)])
    right_pack = lax.ppermute(head, "wide", [((i + 1) % count, i) for i in range(count)])
    common = (obs_sites, left_pack, right_pack, innovation, obs_error)

    def own_rows(mine):
        other = lax.ppermute(mine, pairs, other_pairs)
        return other, jnp.where(first, jnp.concatenate([mine, other]), jnp.concatenate([other, mine]))

    vectors = common + (obs_weights,)
    for sweep_index in range(ITERS):
        mine = update(
            scal, sub, tile_columns, region_sizes, ridge_weight, huber_cut, step_size, vectors,
            margin, tile_scale, regions, sweep_index == 0,
        )
        if sweep_index + 1 < ITERS:
            other = lax.ppermute(mine, pairs, other_pairs)
            q1 = lax.ppermute(mine, pairs, q1_pairs)
            q2 = lax.ppermute(mine, pairs, q2_pairs)
            vectors = common + (q1, q2, mine, other)
    other, obs_weights = own_rows(mine)
    w_slots = jnp.concatenate(
        [gather_slots(obs_weights, "wide"), jnp.zeros((ROWS, solves, capacity), jnp.float32)], axis=0
    )

    slab_count = slab_order.shape[0]
    n_own = slab_count // (n_wide * n_slab)
    pos0 = (me * n_slab + lax.axis_index("slab")) * n_own
    own_slabs = lax.dynamic_slice_in_dim(slab_order, pos0, n_own, 0)
    g_lat = grid_latitude[own_slabs]
    g_lon = FULL_TURN * (own_slabs[:, None].astype(jnp.float32) + grid_offset[own_slabs]) / slab_count
    gsites = unit_rows(g_lat, g_lon)
    grid_increment = grid_stage(
        me.astype(jnp.int32).reshape(1),
        own_slabs,
        list_slots,
        site_slots,
        w_slots,
        gsites,
        reg_dev,
        n_wide,
        regions,
        slab_count,
    )
    return (obs_weights, grid_increment)


def solution(mesh):
    in_specs = (
        P(("groups", "wide"), None),
        P(("groups", "wide"), None),
        P(("groups", "wide"), None),
        P(("groups", "wide"), None),
        P(("groups", "wide")),
        P(("groups", "wide"), None),
        P(("groups", "wide"), None),
        P("groups"),
        P(),
        P(),
        P("narrow"),
        P("narrow"),
        P("narrow"),
    )
    out_specs = (
        P(("groups", "wide"), "narrow", None),
        P(("groups", "wide", "slab"), "narrow", None),
    )
    return jax.shard_map(body, mesh=mesh, in_specs=in_specs, out_specs=out_specs, check_vma=False)
```
